32 devices in a mesh: dp: 8 (over z, core), mask: 4 (over y, x).
Axes of the slice: x: 2, y: 2, z: 4, core: 2. Of those that a mesh axis runs over, the one named last changes fastest.
Arguments:
- patches: bfloat16 [2048, 768], P(('dp', 'mask')), parts along dimension 0
- visible_index: int32 [32, 51], P('dp'), parts along dimension 0, may hold values from 0 to 255, as said below
- embed_w: bfloat16 [768, 1024], replicated
- w_qkv: bfloat16 [1024, 3072], replicated, may hold values from -0.1875 to 0.1875
- w_out: bfloat16 [1024, 1024], replicated, may hold values from -0.1875 to 0.1875
- mask_embed: bfloat16 [1024], replicated, may hold values from -4 to 4
- dec_in: bfloat16 [1024, 768], replicated, may hold values from -0.1875 to 0.1875
- conv_w: bfloat16 [3, 16, 48, 48], replicated, may hold values from -0.5 to 0.5
- dec_out: bfloat16 [768, 1024], replicated, may hold values from -0.21875 to 0.21875
Outputs:
- embed_grad: float32 [6144, 1024], P(('dp', 'mask')), parts along dimension 0
- copy_loss: float32 [32], P(('dp', 'mask')), parts along dimension 0
The draws below stay inside these ranges and needn't reach their ends.
There are 8 independent parts, one for each index of `dp`. The reference program is written for one: setup_inputs(seed, part) draws one part's arguments, and reference() takes and returns one part's arrays. A program takes and returns all parts, laid end to end along the dimension named above; an argument that names none is the same for every part. Nothing has to cross between parts.
Inputs may be any that keep to these rules, and one draw needn't show every extreme that they name: `visible_index`: each row lists 51 different patches; among the 64 patches of one index of mask (patches k * 64 to (k + 1) * 64 - 1) a row lists at most 26, and in every row some index's patches reach 26.
All inputs are finite; a program needn't handle non-finite values.
Results may differ from the reference program's by a relative error of at most 0.02.
Values may be sent and summed in bfloat16 or wider, within the bound.
No kernel may reach another device: no remote copies, remote signals or barrier semaphores. Data moves between devices by JAX's collectives and lax.ppermute only.
A program may use at most 128 MiB of HBM per device.

```python
import math
import jax
import jax.numpy as jnp
from jax import lax

D = 1024
HEADS = 16
C = 768
DD = 768
GROUPS = 16
TOK_DEV = 64
HD = 64
P_SIZE = 256
VIS = 51
COPIES = 4
CAP = 26


def draw_visible_index(key, part):
    first, second, third = jax.random.split(key, 3)
    owners = P_SIZE // TOK_DEV
    shuffled = jax.vmap(lambda sub_key: jax.random.permutation(sub_key, P_SIZE))(jax.random.split(first, COPIES))
    blocked = shuffled.astype(jnp.int32).reshape(COPIES, owners, TOK_DEV)
    ranks = jnp.argsort(jnp.argsort(blocked, axis=-1), axis=-1).astype(jnp.int32)
    eligible = (ranks < CAP).astype(jnp.int32).reshape(COPIES, P_SIZE)
    forced = jax.random.randint(second, (COPIES, 1), 0, owners)
    block_of = jnp.arange(P_SIZE, dtype=jnp.int32) // TOK_DEV
    in_forced = (block_of[None, :] == forced).astype(jnp.int32)
    scores = jax.vmap(lambda sub_key: jax.random.permutation(sub_key, P_SIZE))(jax.random.split(third, COPIES)).astype(jnp.int32)
    scores = scores + eligible * P_SIZE + eligible * in_forced * (2 * P_SIZE)
    ranked, picked = lax.top_k(scores, VIS)
    return picked.astype(jnp.int32)


def draw_patches(key, part):
    first, second = jax.random.split(key, 2)
    row_scale = jnp.exp(jax.random.uniform(first, (P_SIZE, 1), minval=math.log(0.4), maxval=math.log(4.0)))
    values = jax.random.truncated_normal(second, -3.0, 3.0, (P_SIZE, C)) * row_scale
    return values.astype(jnp.float32).astype(jnp.bfloat16)


def draw_embed_w(key, part):
    first, second = jax.random.split(key)
    column_scale = jnp.exp(jax.random.uniform(first, (1, D), minval=math.log(0.4), maxval=math.log(4.0)))
    base = jax.random.truncated_normal(second, -3.0, 3.0, (C, D))
    values = base * column_scale / math.sqrt(C)
    return values.astype(jnp.float32).astype(jnp.bfloat16)


def normal_values(own_key, dims, width, reach, held_as=jnp.bfloat16):
    result = width * jax.random.normal(own_key, dims, jnp.float32)
    return jnp.clip(result, min=-reach, max=reach).astype(held_as)


def setup_inputs(seed: int = 0, part: int = 0) -> dict:
    splits = jax.random.split(jax.random.key(seed), 10)
    part_splits = jax.random.split(jax.random.fold_in(splits[9], part), 10)
    return {
        "patches": draw_patches(jax.random.fold_in(jax.random.fold_in(splits[9], part), 71), part),
        "visible_index": draw_visible_index(jax.random.fold_in(jax.random.fold_in(splits[9], part), 71), part),
        "embed_w": draw_embed_w(jax.random.fold_in(splits[9], 71), part),
        "w_qkv": normal_values(splits[3], (D, 3 * D), D ** -0.5, 0.1875),
        "w_out": normal_values(splits[4], (D, D), D ** -0.5, 0.1875),
        "mask_embed": normal_values(splits[5], (D,), 1.0, 4.0),
        "dec_in": normal_values(splits[6], (D, DD), D ** -0.5, 0.1875),
        "conv_w": normal_values(splits[7], (3, GROUPS, DD // GROUPS, DD // GROUPS), (3 * DD // GROUPS) ** -0.5, 0.5),
        "dec_out": normal_values(splits[8], (DD, D), DD ** -0.5, 0.21875),
    }


EPSILON = 1e-06

def row_norm(values):
    average = lax.optimization_barrier(jnp.mean(values, axis=-1, keepdims=True))
    centred = values - average
    spread = lax.optimization_barrier(jnp.mean(centred * centred, axis=-1, keepdims=True))
    return centred * lax.rsqrt(spread + EPSILON)

def head_norm(values):
    return values * lax.rsqrt(lax.optimization_barrier(jnp.mean(values * values, axis=-1, keepdims=True)) + EPSILON)

def mix_heads(queries, key_rows, values):
    score_scale = 1.0 / math.sqrt(queries.shape[-1])
    scores = jnp.einsum('qhd,khd->hqk', queries.astype(jnp.float32), key_rows.astype(jnp.float32)) * score_scale
    exponent = jnp.exp(scores)
    weights = (exponent / lax.optimization_barrier(jnp.sum(exponent, axis=-1, keepdims=True))).astype(jnp.bfloat16)
    mixed = jnp.einsum('hqk,khd->qhd', weights.astype(jnp.float32), values.astype(jnp.float32))
    return mixed.astype(jnp.bfloat16)

def attention_branch(inputs, w_qkv, w_out):
    row_count = inputs.shape[0]
    normed = row_norm(inputs.astype(jnp.float32)).astype(jnp.bfloat16)
    projected = jnp.dot(normed, w_qkv, preferred_element_type=jnp.float32).astype(jnp.bfloat16)
    projected = projected.reshape(row_count, 3, HEADS, HD)
    queries = head_norm(projected[:, 0].astype(jnp.float32)).astype(jnp.bfloat16)
    key_rows = head_norm(projected[:, 1].astype(jnp.float32)).astype(jnp.bfloat16)
    context = mix_heads(queries, key_rows, projected[:, 2])
    return jnp.dot(context.reshape(row_count, D), w_out, preferred_element_type=jnp.float32)

def decode(visible_out, positions, mask_embed, dec_in, conv_w, dec_out):
    canvas = jnp.broadcast_to(mask_embed, (P_SIZE, D)).at[positions].set(visible_out)
    lowered = jnp.dot(canvas, dec_in, preferred_element_type=jnp.float32).astype(jnp.bfloat16)
    grouped = lowered.reshape(P_SIZE, GROUPS, DD // GROUPS)
    padded = jnp.pad(grouped, ((1, 1), (0, 0), (0, 0)))
    convolved = jnp.zeros((P_SIZE, GROUPS, DD // GROUPS), jnp.float32)
    for offset in range(3):
        convolved = convolved + jnp.einsum('pgi,gio->pgo', padded[offset:offset + P_SIZE].astype(jnp.float32), conv_w[offset].astype(jnp.float32))
    activated = jax.nn.gelu(row_norm(convolved.reshape(P_SIZE, DD)), approximate=False)
    hidden = (lowered.astype(jnp.float32) + activated).astype(jnp.bfloat16)
    return jnp.dot(hidden, dec_out, preferred_element_type=jnp.float32)

def copy_terms(visible_in, positions, targets, w_qkv, w_out, mask_embed, dec_in, conv_w, dec_out):
    visible_out = (visible_in.astype(jnp.float32) + attention_branch(visible_in, w_qkv, w_out)).astype(jnp.bfloat16)
    predicted = decode(visible_out, positions, mask_embed, dec_in, conv_w, dec_out)
    slot_ids = jnp.arange(P_SIZE, dtype=jnp.int32)
    seen = lax.optimization_barrier(jnp.max((slot_ids[:, None] == positions[None, :]).astype(jnp.float32), axis=1))
    mismatch = (predicted - targets.astype(jnp.float32)) * (1.0 - seen)[:, None]
    return jnp.sum(mismatch * mismatch)

def reference(patches, visible_index, embed_w, w_qkv, w_out, mask_embed, dec_in, conv_w, dec_out):
    embedded = jnp.dot(patches, embed_w, preferred_element_type=jnp.float32).astype(jnp.bfloat16)
    targets = row_norm(attention_branch(embedded, w_qkv, w_out)).astype(jnp.bfloat16)
    factor = 0.5 / math.sqrt(COPIES * VIS)

    def one_copy(running, positions):
        positions = positions.astype(jnp.int32)
        visible_in = embedded[positions]

        def objective(rows_in):
            return copy_terms(rows_in, positions, targets, w_qkv, w_out, mask_embed, dec_in, conv_w, dec_out)
        squares, pullback = jax.vjp(objective, visible_in)
        grad_in, = pullback(jnp.ones_like(squares) * factor)
        chosen = patches[positions]
        grad_term = jnp.dot(chosen.T, grad_in, preferred_element_type=jnp.float32)
        return (running + grad_term, squares / ((P_SIZE - VIS) * D))
    start = jnp.zeros((C, D), jnp.float32)
    embed_grad, copy_loss = lax.scan(one_copy, start, visible_index)
    return (embed_grad, copy_loss)
```

```python
import math

import jax
import jax.numpy as jnp
from jax import lax
from jax.sharding import PartitionSpec as P

D = 1024
HEADS = 16
DD = 768
GROUPS = 16


EPSILON = 1e-06


def row_norm(values):
    average = jnp.mean(values, axis=-1, keepdims=True)
    centred = values - average
    spread = jnp.mean(centred * centred, axis=-1, keepdims=True)
    return centred * lax.rsqrt(spread + EPSILON)


def head_norm(values):
    return values * lax.rsqrt(jnp.mean(values * values, axis=-1, keepdims=True) + EPSILON)


def mix_heads(queries, key_rows, values):
    score_scale = 1.0 / math.sqrt(queries.shape[-1])
    scores = (
        jnp.einsum("qhd,khd->hqk", queries, key_rows, preferred_element_type=jnp.float32)
        * score_scale
    )
    exponent = jnp.exp(scores)
    weights = (exponent / jnp.sum(exponent, axis=-1, keepdims=True)).astype(jnp.bfloat16)
    mixed = jnp.einsum("hqk,khd->qhd", weights, values, preferred_element_type=jnp.float32)
    return mixed.astype(jnp.bfloat16)


def split_project(projected):
    queries = head_norm(projected[:, 0].astype(jnp.float32)).astype(jnp.bfloat16)
    key_rows = head_norm(projected[:, 1].astype(jnp.float32)).astype(jnp.bfloat16)
    return mix_heads(queries, key_rows, projected[:, 2])


def attention_branch(inputs, w_qkv, w_out):
    row_count = inputs.shape[0]
    normed = row_norm(inputs.astype(jnp.float32)).astype(jnp.bfloat16)
    projected = jnp.dot(normed, w_qkv, preferred_element_type=jnp.float32).astype(jnp.bfloat16)
    context = split_project(projected.reshape(row_count, 3, HEADS, D // HEADS))
    return jnp.dot(context.reshape(row_count, D), w_out, preferred_element_type=jnp.float32)


def decoder_output(visible_out, positions, total_rows, mask_embed, dec_in, conv_w, dec_out):
    canvas = jnp.broadcast_to(mask_embed, (total_rows, D)).at[positions].set(visible_out)
    lowered = jnp.dot(canvas, dec_in, preferred_element_type=jnp.float32).astype(jnp.bfloat16)
    grouped = lowered.reshape(total_rows, GROUPS, DD // GROUPS)
    padded = jnp.pad(grouped, ((1, 1), (0, 0), (0, 0)))
    convolved = jnp.zeros((total_rows, GROUPS, DD // GROUPS), jnp.float32)
    for offset in range(3):
        convolved = convolved + jnp.einsum(
            "pgi,gio->pgo",
            padded[offset : offset + total_rows],
            conv_w[offset],
            preferred_element_type=jnp.float32,
        )
    activated = jax.nn.gelu(row_norm(convolved.reshape(total_rows, DD)), approximate=False)
    hidden = (lowered.astype(jnp.float32) + activated).astype(jnp.bfloat16)
    return jnp.dot(hidden, dec_out, preferred_element_type=jnp.float32)


def copy_terms(visible_in, positions, targets, w_qkv, w_out, mask_embed, dec_in, conv_w, dec_out):
    total_rows = targets.shape[0]
    visible_out = (
        visible_in.astype(jnp.float32) + attention_branch(visible_in, w_qkv, w_out)
    ).astype(jnp.bfloat16)
    predicted = decoder_output(
        visible_out, positions, total_rows, mask_embed, dec_in, conv_w, dec_out
    )
    slot_ids = jnp.arange(total_rows, dtype=jnp.int32)
    seen = jnp.max((slot_ids[:, None] == positions[None, :]).astype(jnp.float32), axis=1)
    mismatch = (predicted - targets.astype(jnp.float32)) * (1.0 - seen)[:, None]
    return jnp.sum(mismatch * mismatch)


def ring_gather(values, group_size):
    parts = [values]
    for shift in range(1, group_size):
        pairs = [(source, (source - shift) % group_size) for source in range(group_size)]
        parts.append(lax.ppermute(values, "mask", pairs))
    return jnp.concatenate(parts, axis=0)


def unroll_blocks(rotated, own_index, block_rows):
    total_rows = rotated.shape[0]
    doubled = jnp.concatenate([rotated, rotated], axis=0)
    start = total_rows - own_index * block_rows
    return lax.dynamic_slice_in_dim(doubled, start, total_rows, 0)


def split_teacher(embedded, w_qkv, w_out, own_index, group_size):
    total_rows = embedded.shape[0]
    head_dim = D // HEADS
    heads_here = HEADS // group_size
    head_width = heads_here * head_dim
    normed = row_norm(embedded.astype(jnp.float32)).astype(jnp.bfloat16)
    own_cols = lax.dynamic_slice_in_dim(
        w_qkv.reshape(D, 3, D), own_index * head_width, head_width, 2
    )
    projected = jnp.einsum(
        "sd,dtw->stw", normed, own_cols, preferred_element_type=jnp.float32
    ).astype(jnp.bfloat16)
    context = split_project(projected.reshape(total_rows, 3, heads_here, head_dim))
    out_rows = lax.dynamic_slice_in_dim(w_out, own_index * head_width, head_width, 0)
    partial_value = jnp.dot(
        context.reshape(total_rows, head_width), out_rows, preferred_element_type=jnp.float32
    )
    return lax.psum(partial_value.astype(jnp.bfloat16), "mask").astype(jnp.float32)


def on_device(patches, visible_index, embed_w, w_qkv, w_out, mask_embed, dec_in, conv_w, dec_out):
    tok_rows = patches.shape[0]
    group_size = lax.axis_size("mask")
    own_index = lax.axis_index("mask")
    copies = visible_index.shape[0]
    visible_count = visible_index.shape[1]
    total_rows = tok_rows * group_size
    col_width = patches.shape[1] // group_size
    positions = lax.dynamic_index_in_dim(visible_index, own_index, 0, keepdims=False)
    clip_pixels = unroll_blocks(ring_gather(patches, group_size), own_index, tok_rows)
    embedded = jnp.dot(clip_pixels, embed_w, preferred_element_type=jnp.float32).astype(
        jnp.bfloat16
    )
    visible_in = embedded[positions]
    if HEADS * total_rows * total_rows * 4 <= (1 << 24):
        branch = attention_branch(embedded, w_qkv, w_out)
    else:
        branch = split_teacher(embedded, w_qkv, w_out, own_index, group_size)
    all_targets = row_norm(branch).astype(jnp.bfloat16)

    def objective(rows_in):
        return copy_terms(
            rows_in, positions, all_targets, w_qkv, w_out, mask_embed, dec_in, conv_w, dec_out
        )

    squares, pullback = jax.vjp(objective, visible_in)
    factor = 0.5 / math.sqrt(copies * visible_count)
    (grad_in,) = pullback(jnp.ones_like(squares) * factor)
    copy_loss = jnp.reshape(squares / ((total_rows - visible_count) * D), (1,))
    slot_copy = (own_index + jnp.arange(group_size, dtype=jnp.int32)) % group_size
    flat_index = visible_index[slot_copy].reshape(copies * visible_count)
    own_cols = lax.dynamic_slice_in_dim(clip_pixels, own_index * col_width, col_width, 1)
    gathered = own_cols[flat_index]
    embed_grad = jnp.einsum(
        "vc,vd->cd",
        gathered,
        ring_gather(grad_in, group_size),
        preferred_element_type=jnp.float32,
    )
    return (embed_grad, copy_loss)


def solution(mesh):
    placed = (P(("dp", "mask"), None), P("dp", None), P(), P(), P(), P(), P(), P(), P())
    return jax.shard_map(
        on_device,
        mesh=mesh,
        in_specs=placed,
        out_specs=(P(("dp", "mask"), None), P(("dp", "mask"))),
        check_vma=False,
    )
```

```python
import math

import jax
import jax.numpy as jnp
from jax import lax
from jax.sharding import PartitionSpec as P

D = 1024
HEADS = 16
DD = 768
GROUPS = 16


EPSILON = 1e-06


def row_norm(values):
    average = jnp.mean(values, axis=-1, keepdims=True)
    centred = values - average
    spread = jnp.mean(centred * centred, axis=-1, keepdims=True)
    return centred * lax.rsqrt(spread + EPSILON)


def head_norm(values):
    return values * lax.rsqrt(jnp.mean(values * values, axis=-1, keepdims=True) + EPSILON)


def mix_heads(queries, key_rows, values):
    score_scale = 1.0 / math.sqrt(queries.shape[-1])
    scores = (
        jnp.einsum("qhd,khd->hqk", queries, key_rows, preferred_element_type=jnp.float32)
        * score_scale
    )
    exponent = jnp.exp(scores)
    weights = (exponent / jnp.sum(exponent, axis=-1, keepdims=True)).astype(jnp.bfloat16)
    mixed = jnp.einsum("hqk,khd->qhd", weights, values, preferred_element_type=jnp.float32)
    return mixed.astype(jnp.bfloat16)


def split_project(projected):
    queries = head_norm(projected[:, 0].astype(jnp.float32)).astype(jnp.bfloat16)
    key_rows = head_norm(projected[:, 1].astype(jnp.float32)).astype(jnp.bfloat16)
    return mix_heads(queries, key_rows, projected[:, 2])


def attention_branch(inputs, w_qkv, w_out):
    row_count = inputs.shape[0]
    head_dim = D // HEADS
    normed = row_norm(inputs.astype(jnp.float32)).astype(jnp.bfloat16)
    projected = jnp.einsum(
        "sd,dk->ks", normed, w_qkv, preferred_element_type=jnp.float32
    ).astype(jnp.bfloat16)
    projected = projected.reshape(3, HEADS, head_dim, row_count)
    queries = head_norm_cols(projected[0].astype(jnp.float32)).astype(jnp.bfloat16)
    key_rows = head_norm_cols(projected[1].astype(jnp.float32)).astype(jnp.bfloat16)
    score_scale = 1.0 / math.sqrt(head_dim)
    scores = (
        jnp.einsum("hdq,hdk->hqk", queries, key_rows, preferred_element_type=jnp.float32)
        * score_scale
    )
    exponent = jnp.exp(scores)
    weights = (exponent / jnp.sum(exponent, axis=-1, keepdims=True)).astype(jnp.bfloat16)
    context = jnp.einsum(
        "hqk,hdk->qhd", weights, projected[2], preferred_element_type=jnp.float32
    ).astype(jnp.bfloat16)
    return jnp.dot(context.reshape(row_count, D), w_out, preferred_element_type=jnp.float32)


def head_norm_cols(values):
    return values * lax.rsqrt(jnp.mean(values * values, axis=-2, keepdims=True) + EPSILON)


def decoder_output(visible_out, positions, true_rows, mask_embed, dec_in, conv_w, dec_out):
    total_rows = true_rows.shape[0]
    canvas = jnp.broadcast_to(mask_embed, (total_rows, D)).at[positions].set(visible_out)
    lowered = jnp.dot(canvas, dec_in, preferred_element_type=jnp.float32).astype(jnp.bfloat16)
    grouped = lowered.reshape(total_rows, GROUPS, DD // GROUPS)
    has_prev = (true_rows > 0)[:, None, None]
    has_next = (true_rows < total_rows - 1)[:, None, None]
    zero = jnp.zeros_like(grouped)
    shifted = (
        jnp.where(has_prev, jnp.roll(grouped, 1, axis=0), zero),
        grouped,
        jnp.where(has_next, jnp.roll(grouped, -1, axis=0), zero),
    )
    convolved = jnp.zeros((total_rows, GROUPS, DD // GROUPS), jnp.float32)
    for offset in range(3):
        convolved = convolved + jnp.einsum(
            "pgi,gio->pgo",
            shifted[offset],
            conv_w[offset],
            preferred_element_type=jnp.float32,
        )
    activated = jax.nn.gelu(row_norm(convolved.reshape(total_rows, DD)), approximate=False)
    hidden = (lowered.astype(jnp.float32) + activated).astype(jnp.bfloat16)
    return jnp.dot(hidden, dec_out, preferred_element_type=jnp.float32)


def copy_terms(
    visible_in, positions, true_rows, targets, w_qkv, w_out, mask_embed, dec_in, conv_w, dec_out
):
    total_rows = targets.shape[0]
    visible_out = (
        visible_in.astype(jnp.float32) + attention_branch(visible_in, w_qkv, w_out)
    ).astype(jnp.bfloat16)
    predicted = decoder_output(
        visible_out, positions, true_rows, mask_embed, dec_in, conv_w, dec_out
    )
    slot_ids = jnp.arange(total_rows, dtype=jnp.int32)
    seen = jnp.max((slot_ids[:, None] == positions[None, :]).astype(jnp.float32), axis=1)
    mismatch = (predicted - targets.astype(jnp.float32)) * (1.0 - seen)[:, None]
    return jnp.sum(mismatch * mismatch)


def ring_gather(values, group_size):
    parts = [values]
    for shift in range(1, group_size):
        pairs = [(source, (source - shift) % group_size) for source in range(group_size)]
        parts.append(lax.ppermute(values, "mask", pairs))
    return jnp.concatenate(parts, axis=0)


def split_teacher(embedded, w_qkv, w_out, own_index, group_size):
    total_rows = embedded.shape[0]
    head_dim = D // HEADS
    heads_here = HEADS // group_size
    head_width = heads_here * head_dim
    normed = row_norm(embedded.astype(jnp.float32)).astype(jnp.bfloat16)
    own_cols = lax.dynamic_slice_in_dim(
        w_qkv.reshape(D, 3, D), own_index * head_width, head_width, 2
    )
    projected = jnp.einsum(
        "sd,dtw->stw", normed, own_cols, preferred_element_type=jnp.float32
    ).astype(jnp.bfloat16)
    context = split_project(projected.reshape(total_rows, 3, heads_here, head_dim))
    out_rows = lax.dynamic_slice_in_dim(w_out, own_index * head_width, head_width, 0)
    partial_value = jnp.dot(
        context.reshape(total_rows, head_width), out_rows, preferred_element_type=jnp.float32
    )
    return lax.psum(partial_value.astype(jnp.bfloat16), "mask").astype(jnp.float32)


def on_device(patches, visible_index, embed_w, w_qkv, w_out, mask_embed, dec_in, conv_w, dec_out):
    tok_rows = patches.shape[0]
    group_size = lax.axis_size("mask")
    own_index = lax.axis_index("mask")
    copies = visible_index.shape[0]
    visible_count = visible_index.shape[1]
    total_rows = tok_rows * group_size
    col_width = patches.shape[1] // group_size
    offset = own_index * tok_rows
    true_rows = (jnp.arange(total_rows, dtype=jnp.int32) + offset) % total_rows
    rotated_index = (visible_index - offset) % total_rows
    positions = lax.dynamic_index_in_dim(rotated_index, own_index, 0, keepdims=False)
    clip_pixels = ring_gather(patches, group_size)
    embedded = jnp.dot(clip_pixels, embed_w, preferred_element_type=jnp.float32).astype(
        jnp.bfloat16
    )
    visible_in = embedded[positions]
    if HEADS * total_rows * total_rows * 4 <= (1 << 24):
        branch = attention_branch(embedded, w_qkv, w_out)
    else:
        branch = split_teacher(embedded, w_qkv, w_out, own_index, group_size)
    all_targets = row_norm(branch).astype(jnp.bfloat16)

    def objective(rows_in):
        return copy_terms(
            rows_in, positions, true_rows, all_targets, w_qkv, w_out, mask_embed, dec_in, conv_w, dec_out
        )

    squares, pullback = jax.vjp(objective, visible_in)
    factor = 0.5 / math.sqrt(copies * visible_count)
    (grad_in,) = pullback(jnp.ones_like(squares) * factor)
    copy_loss = jnp.reshape(squares / ((total_rows - visible_count) * D), (1,))
    slot_copy = (own_index + jnp.arange(group_size, dtype=jnp.int32)) % group_size
    flat_index = rotated_index[slot_copy].reshape(copies * visible_count)
    own_cols = lax.dynamic_slice_in_dim(clip_pixels, own_index * col_width, col_width, 1)
    gathered = own_cols[flat_index]
    embed_grad = jnp.einsum(
        "vc,vd->cd",
        gathered,
        ring_gather(grad_in, group_size),
        preferred_element_type=jnp.float32,
    )
    return (embed_grad, copy_loss)


def solution(mesh):
    placed = (P(("dp", "mask"), None), P("dp", None), P(), P(), P(), P(), P(), P(), P())
    return jax.shard_map(
        on_device,
        mesh=mesh,
        in_specs=placed,
        out_specs=(P(("dp", "mask"), None), P(("dp", "mask"))),
        check_vma=False,
    )
```

```python
import math

import jax
import jax.numpy as jnp
from jax import lax
from jax.sharding import PartitionSpec as P

D = 1024
HEADS = 16
DD = 768
GROUPS = 16


EPSILON = 1e-06


def row_norm(values):
    average = jnp.mean(values, axis=-1, keepdims=True)
    centred = values - average
    spread = jnp.mean(centred * centred, axis=-1, keepdims=True)
    return centred * lax.rsqrt(spread + EPSILON)


def head_norm(values):
    return values * lax.rsqrt(jnp.mean(values * values, axis=-1, keepdims=True) + EPSILON)


def mix_heads(queries, key_rows, values):
    score_scale = 1.0 / math.sqrt(queries.shape[-1])
    scores = (
        jnp.einsum("qhd,khd->hqk", queries, key_rows, preferred_element_type=jnp.float32)
        * score_scale
    )
    exponent = jnp.exp(scores)
    weights = (exponent / jnp.sum(exponent, axis=-1, keepdims=True)).astype(jnp.bfloat16)
    mixed = jnp.einsum("hqk,khd->qhd", weights, values, preferred_element_type=jnp.float32)
    return mixed.astype(jnp.bfloat16)


def split_project(projected):
    queries = head_norm(projected[:, 0].astype(jnp.float32)).astype(jnp.bfloat16)
    key_rows = head_norm(projected[:, 1].astype(jnp.float32)).astype(jnp.bfloat16)
    return mix_heads(queries, key_rows, projected[:, 2])


def attention_branch(inputs, w_qkv, w_out):
    row_count = inputs.shape[0]
    normed = row_norm(inputs.astype(jnp.float32)).astype(jnp.bfloat16)
    projected = jnp.dot(normed, w_qkv, preferred_element_type=jnp.float32).astype(jnp.bfloat16)
    context = split_project(projected.reshape(row_count, 3, HEADS, D // HEADS))
    return jnp.dot(context.reshape(row_count, D), w_out, preferred_element_type=jnp.float32)


def decoder_output(visible_out, positions, true_rows, mask_embed, dec_in, conv_w, dec_out):
    total_rows = true_rows.shape[0]
    canvas = jnp.broadcast_to(mask_embed, (total_rows, D)).at[positions].set(visible_out)
    lowered = jnp.dot(canvas, dec_in, preferred_element_type=jnp.float32).astype(jnp.bfloat16)
    grouped = lowered.reshape(total_rows, GROUPS, DD // GROUPS)
    has_prev = (true_rows > 0)[:, None, None]
    has_next = (true_rows < total_rows - 1)[:, None, None]
    zero = jnp.zeros_like(grouped)
    shifted = (
        jnp.where(has_prev, jnp.roll(grouped, 1, axis=0), zero),
        grouped,
        jnp.where(has_next, jnp.roll(grouped, -1, axis=0), zero),
    )
    convolved = jnp.zeros((total_rows, GROUPS, DD // GROUPS), jnp.float32)
    for offset in range(3):
        convolved = convolved + jnp.einsum(
            "pgi,gio->pgo",
            shifted[offset],
            conv_w[offset],
            preferred_element_type=jnp.float32,
        )
    activated = jax.nn.gelu(row_norm(convolved.reshape(total_rows, DD)), approximate=False)
    hidden = (lowered.astype(jnp.float32) + activated).astype(jnp.bfloat16)
    return jnp.dot(hidden, dec_out, preferred_element_type=jnp.float32)


def copy_terms(
    visible_in, positions, true_rows, targets, w_qkv, w_out, mask_embed, dec_in, conv_w, dec_out
):
    total_rows = targets.shape[0]
    visible_out = (
        visible_in.astype(jnp.float32) + attention_branch(visible_in, w_qkv, w_out)
    ).astype(jnp.bfloat16)
    predicted = decoder_output(
        visible_out, positions, true_rows, mask_embed, dec_in, conv_w, dec_out
    )
    slot_ids = jnp.arange(total_rows, dtype=jnp.int32)
    seen = jnp.max((slot_ids[:, None] == positions[None, :]).astype(jnp.float32), axis=1)
    mismatch = (predicted - targets.astype(jnp.float32)) * (1.0 - seen)[:, None]
    return jnp.sum(mismatch * mismatch)


def ring_gather(values, group_size):
    parts = [values]
    for shift in range(1, group_size):
        pairs = [(source, (source - shift) % group_size) for source in range(group_size)]
        parts.append(lax.ppermute(values, "mask", pairs))
    return jnp.concatenate(parts, axis=0)


def split_teacher(embedded, w_qkv, w_out, own_index, group_size):
    total_rows = embedded.shape[0]
    head_dim = D // HEADS
    heads_here = HEADS // group_size
    head_width = heads_here * head_dim
    normed = row_norm(embedded.astype(jnp.float32)).astype(jnp.bfloat16)
    own_cols = lax.dynamic_slice_in_dim(
        w_qkv.reshape(D, 3, D), own_index * head_width, head_width, 2
    )
    projected = jnp.einsum(
        "sd,dtw->stw", normed, own_cols, preferred_element_type=jnp.float32
    ).astype(jnp.bfloat16)
    context = split_project(projected.reshape(total_rows, 3, heads_here, head_dim))
    out_rows = lax.dynamic_slice_in_dim(w_out, own_index * head_width, head_width, 0)
    partial_value = jnp.dot(
        context.reshape(total_rows, head_width), out_rows, preferred_element_type=jnp.float32
    )
    return lax.psum(partial_value.astype(jnp.bfloat16), "mask").astype(jnp.float32)


def on_device(patches, visible_index, embed_w, w_qkv, w_out, mask_embed, dec_in, conv_w, dec_out):
    tok_rows = patches.shape[0]
    group_size = lax.axis_size("mask")
    own_index = lax.axis_index("mask")
    copies = visible_index.shape[0]
    visible_count = visible_index.shape[1]
    total_rows = tok_rows * group_size
    col_width = patches.shape[1] // group_size
    offset = own_index * tok_rows
    true_rows = (jnp.arange(total_rows, dtype=jnp.int32) + offset) % total_rows
    rotated_index = (visible_index - offset) % total_rows
    positions = lax.dynamic_index_in_dim(rotated_index, own_index, 0, keepdims=False)
    clip_pixels = ring_gather(patches, group_size)
    embedded = jnp.dot(clip_pixels, embed_w, preferred_element_type=jnp.float32).astype(
        jnp.bfloat16
    )
    visible_in = embedded[positions]
    if HEADS * total_rows * total_rows * 4 <= (1 << 24):
        branch = attention_branch(embedded, w_qkv, w_out)
    else:
        branch = split_teacher(embedded, w_qkv, w_out, own_index, group_size)
    all_targets = row_norm(branch).astype(jnp.bfloat16)

    def objective(rows_in):
        return copy_terms(
            rows_in, positions, true_rows, all_targets, w_qkv, w_out, mask_embed, dec_in, conv_w, dec_out
        )

    squares, pullback = jax.vjp(objective, visible_in)
    factor = 0.5 / math.sqrt(copies * visible_count)
    (grad_in,) = pullback(jnp.ones_like(squares) * factor)
    copy_loss = jnp.reshape(squares / ((total_rows - visible_count) * D), (1,))
    slot_copy = (own_index + jnp.arange(group_size, dtype=jnp.int32)) % group_size
    flat_index = rotated_index[slot_copy].reshape(copies * visible_count)
    own_cols = lax.dynamic_slice_in_dim(clip_pixels, own_index * col_width, col_width, 1)
    gathered = own_cols[flat_index]
    embed_grad = jnp.einsum(
        "vc,vd->cd",
        gathered,
        ring_gather(grad_in, group_size),
        preferred_element_type=jnp.float32,
    )
    return (embed_grad, copy_loss)


def solution(mesh):
    placed = (P(("dp", "mask"), None), P("dp", None), P(), P(), P(), P(), P(), P(), P())
    return jax.shard_map(
        on_device,
        mesh=mesh,
        in_specs=placed,
        out_specs=(P(("dp", "mask"), None), P(("dp", "mask"))),
        check_vma=False,
    )
```

```python
import math

import jax
import jax.numpy as jnp
from jax import lax
from jax.sharding import PartitionSpec as P

D = 1024
HEADS = 16
DD = 768
GROUPS = 16


EPSILON = 1e-06


def row_norm(values):
    average = jnp.mean(values, axis=-1, keepdims=True)
    centred = values - average
    spread = jnp.mean(centred * centred, axis=-1, keepdims=True)
    return centred * lax.rsqrt(spread + EPSILON)


def head_norm(values):
    return values * lax.rsqrt(jnp.mean(values * values, axis=-1, keepdims=True) + EPSILON)


def mix_heads(queries, key_rows, values):
    score_scale = 1.0 / math.sqrt(queries.shape[-1])
    scores = (
        jnp.einsum("qhd,khd->hqk", queries, key_rows, preferred_element_type=jnp.float32)
        * score_scale
    )
    exponent = jnp.exp(scores)
    weights = (exponent / jnp.sum(exponent, axis=-1, keepdims=True)).astype(jnp.bfloat16)
    mixed = jnp.einsum("hqk,khd->qhd", weights, values, preferred_element_type=jnp.float32)
    return mixed.astype(jnp.bfloat16)


def split_project(projected):
    queries = head_norm(projected[:, 0].astype(jnp.float32)).astype(jnp.bfloat16)
    key_rows = head_norm(projected[:, 1].astype(jnp.float32)).astype(jnp.bfloat16)
    return mix_heads(queries, key_rows, projected[:, 2])


def attention_branch(inputs, w_qkv, w_out):
    row_count = inputs.shape[0]
    normed = row_norm(inputs.astype(jnp.float32)).astype(jnp.bfloat16)
    projected = jnp.dot(normed, w_qkv, preferred_element_type=jnp.float32).astype(jnp.bfloat16)
    context = split_project(projected.reshape(row_count, 3, HEADS, D // HEADS))
    return jnp.dot(context.reshape(row_count, D), w_out, preferred_element_type=jnp.float32)


def decoder_output(visible_out, positions, total_rows, mask_embed, dec_in, conv_w, dec_out):
    slot_ids = jnp.arange(total_rows, dtype=jnp.int32)
    picks = (slot_ids[:, None] == positions[None, :]).astype(jnp.bfloat16)
    seen = jnp.max(picks, axis=1, keepdims=True)
    lowered_visible = jnp.dot(visible_out, dec_in, preferred_element_type=jnp.float32).astype(
        jnp.bfloat16
    )
    lowered_mask = jnp.dot(
        mask_embed[None, :], dec_in, preferred_element_type=jnp.float32
    ).astype(jnp.bfloat16)
    placed = jnp.dot(picks, lowered_visible, preferred_element_type=jnp.float32)
    lowered = jnp.where(seen > 0, placed, lowered_mask.astype(jnp.float32)).astype(jnp.bfloat16)
    grouped = lowered.reshape(total_rows, GROUPS, DD // GROUPS)
    padded = jnp.pad(grouped, ((1, 1), (0, 0), (0, 0)))
    convolved = jnp.zeros((total_rows, GROUPS, DD // GROUPS), jnp.float32)
    for offset in range(3):
        convolved = convolved + jnp.einsum(
            "pgi,gio->pgo",
            padded[offset : offset + total_rows],
            conv_w[offset],
            preferred_element_type=jnp.float32,
        )
    activated = jax.nn.gelu(row_norm(convolved.reshape(total_rows, DD)), approximate=False)
    hidden = (lowered.astype(jnp.float32) + activated).astype(jnp.bfloat16)
    return jnp.dot(hidden, dec_out, preferred_element_type=jnp.float32)


def copy_terms(visible_in, positions, targets, w_qkv, w_out, mask_embed, dec_in, conv_w, dec_out):
    total_rows = targets.shape[0]
    visible_out = (
        visible_in.astype(jnp.float32) + attention_branch(visible_in, w_qkv, w_out)
    ).astype(jnp.bfloat16)
    predicted = decoder_output(
        visible_out, positions, total_rows, mask_embed, dec_in, conv_w, dec_out
    )
    slot_ids = jnp.arange(total_rows, dtype=jnp.int32)
    seen = jnp.max((slot_ids[:, None] == positions[None, :]).astype(jnp.float32), axis=1)
    mismatch = (predicted - targets.astype(jnp.float32)) * (1.0 - seen)[:, None]
    return jnp.sum(mismatch * mismatch)


def ring_gather(values, group_size):
    parts = [values]
    for shift in range(1, group_size):
        pairs = [(source, (source - shift) % group_size) for source in range(group_size)]
        parts.append(lax.ppermute(values, "mask", pairs))
    return parts


def in_mask_order(parts, own_index):
    group_size = len(parts)
    blocks = []
    for block in range(group_size):
        slot = (block - own_index) % group_size
        chosen = parts[0]
        for other in range(1, group_size):
            chosen = jnp.where(slot == other, parts[other], chosen)
        blocks.append(chosen)
    return jnp.concatenate(blocks, axis=0)


def split_teacher(embedded, w_qkv, w_out, own_index, group_size):
    total_rows = embedded.shape[0]
    head_dim = D // HEADS
    heads_here = HEADS // group_size
    head_width = heads_here * head_dim
    normed = row_norm(embedded.astype(jnp.float32)).astype(jnp.bfloat16)
    own_cols = lax.dynamic_slice_in_dim(
        w_qkv.reshape(D, 3, D), own_index * head_width, head_width, 2
    )
    projected = jnp.einsum(
        "sd,dtw->stw", normed, own_cols, preferred_element_type=jnp.float32
    ).astype(jnp.bfloat16)
    context = split_project(projected.reshape(total_rows, 3, heads_here, head_dim))
    out_rows = lax.dynamic_slice_in_dim(w_out, own_index * head_width, head_width, 0)
    partial_value = jnp.dot(
        context.reshape(total_rows, head_width), out_rows, preferred_element_type=jnp.float32
    )
    return lax.psum(partial_value.astype(jnp.bfloat16), "mask").astype(jnp.float32)


def on_device(patches, visible_index, embed_w, w_qkv, w_out, mask_embed, dec_in, conv_w, dec_out):
    tok_rows = patches.shape[0]
    group_size = lax.axis_size("mask")
    own_index = lax.axis_index("mask")
    copies = visible_index.shape[0]
    visible_count = visible_index.shape[1]
    total_rows = tok_rows * group_size
    col_width = patches.shape[1] // group_size
    positions = lax.dynamic_index_in_dim(visible_index, own_index, 0, keepdims=False)
    clip_pixels = in_mask_order(ring_gather(patches, group_size), own_index)
    embedded = jnp.dot(clip_pixels, embed_w, preferred_element_type=jnp.float32).astype(
        jnp.bfloat16
    )
    visible_in = embedded[positions]
    if HEADS * total_rows * total_rows * 4 <= (1 << 24):
        branch = attention_branch(embedded, w_qkv, w_out)
    else:
        branch = split_teacher(embedded, w_qkv, w_out, own_index, group_size)
    all_targets = row_norm(branch).astype(jnp.bfloat16)

    def objective(rows_in):
        return copy_terms(
            rows_in, positions, all_targets, w_qkv, w_out, mask_embed, dec_in, conv_w, dec_out
        )

    squares, pullback = jax.vjp(objective, visible_in)
    factor = 0.5 / math.sqrt(copies * visible_count)
    (grad_in,) = pullback(jnp.ones_like(squares) * factor)
    copy_loss = jnp.reshape(squares / ((total_rows - visible_count) * D), (1,))
    slot_copy = (own_index + jnp.arange(group_size, dtype=jnp.int32)) % group_size
    flat_index = visible_index[slot_copy].reshape(copies * visible_count)
    own_cols = lax.dynamic_slice_in_dim(clip_pixels, own_index * col_width, col_width, 1)
    gathered = own_cols[flat_index]
    embed_grad = jnp.einsum(
        "vc,vd->cd",
        gathered,
        jnp.concatenate(ring_gather(grad_in, group_size), axis=0),
        preferred_element_type=jnp.float32,
    )
    return (embed_grad, copy_loss)


def solution(mesh):
    placed = (P(("dp", "mask"), None), P("dp", None), P(), P(), P(), P(), P(), P(), P())
    return jax.shard_map(
        on_device,
        mesh=mesh,
        in_specs=placed,
        out_specs=(P(("dp", "mask"), None), P(("dp", "mask"))),
        check_vma=False,
    )
```

```python
import math

import jax
import jax.numpy as jnp
from jax import lax
from jax.sharding import PartitionSpec as P

D = 1024
HEADS = 16
DD = 768
GROUPS = 16


EPSILON = 1e-06


def row_norm(values):
    average = jnp.mean(values, axis=-1, keepdims=True)
    centred = values - average
    spread = jnp.mean(centred * centred, axis=-1, keepdims=True)
    return centred * lax.rsqrt(spread + EPSILON)


def head_norm(values):
    return values * lax.rsqrt(jnp.mean(values * values, axis=-1, keepdims=True) + EPSILON)


def mix_heads(queries, key_rows, values):
    score_scale = 1.0 / math.sqrt(queries.shape[-1])
    scores = (
        jnp.einsum("qhd,khd->hqk", queries, key_rows, preferred_element_type=jnp.float32)
        * score_scale
    )
    exponent = jnp.exp(scores)
    weights = (exponent / jnp.sum(exponent, axis=-1, keepdims=True)).astype(jnp.bfloat16)
    mixed = jnp.einsum("hqk,khd->qhd", weights, values, preferred_element_type=jnp.float32)
    return mixed.astype(jnp.bfloat16)


def split_project(projected):
    queries = head_norm(projected[:, 0].astype(jnp.float32)).astype(jnp.bfloat16)
    key_rows = head_norm(projected[:, 1].astype(jnp.float32)).astype(jnp.bfloat16)
    return mix_heads(queries, key_rows, projected[:, 2])


def project_heads(inputs, w_qkv):
    row_count = inputs.shape[0]
    normed = row_norm(inputs.astype(jnp.float32)).astype(jnp.bfloat16)
    projected = jnp.dot(normed, w_qkv, preferred_element_type=jnp.float32).astype(jnp.bfloat16)
    projected = projected.reshape(row_count, 3, HEADS, D // HEADS)
    queries = head_norm(projected[:, 0].astype(jnp.float32)).astype(jnp.bfloat16)
    key_rows = head_norm(projected[:, 1].astype(jnp.float32)).astype(jnp.bfloat16)
    return queries, key_rows, projected[:, 2]


def attention_from(heads, w_out):
    context = mix_heads(*heads)
    row_count = context.shape[0]
    return jnp.dot(context.reshape(row_count, D), w_out, preferred_element_type=jnp.float32)


def attention_branch(inputs, w_qkv, w_out):
    return attention_from(project_heads(inputs, w_qkv), w_out)


@jax.custom_vjp
def reuse_heads(inputs, w_qkv, heads):
    return heads


def reuse_heads_fwd(inputs, w_qkv, heads):
    return heads, (inputs, w_qkv)


def reuse_heads_bwd(saved, cotangents):
    inputs, w_qkv = saved
    _, pullback = jax.vjp(lambda rows: project_heads(rows, w_qkv), inputs)
    (d_inputs,) = pullback(cotangents)
    zeros = tuple(jnp.zeros_like(part) for part in cotangents)
    return d_inputs, jnp.zeros_like(w_qkv), zeros


reuse_heads.defvjp(reuse_heads_fwd, reuse_heads_bwd)


def decoder_output(visible_out, positions, total_rows, mask_embed, dec_in, conv_w, dec_out):
    slot_ids = jnp.arange(total_rows, dtype=jnp.int32)
    picks = (slot_ids[:, None] == positions[None, :]).astype(jnp.bfloat16)
    seen = jnp.max(picks, axis=1, keepdims=True)
    lowered_visible = jnp.dot(visible_out, dec_in, preferred_element_type=jnp.float32).astype(
        jnp.bfloat16
    )
    lowered_mask = jnp.dot(
        mask_embed[None, :], dec_in, preferred_element_type=jnp.float32
    ).astype(jnp.bfloat16)
    placed = jnp.dot(picks, lowered_visible, preferred_element_type=jnp.float32)
    lowered = jnp.where(seen > 0, placed, lowered_mask.astype(jnp.float32)).astype(jnp.bfloat16)
    grouped = lowered.reshape(total_rows, GROUPS, DD // GROUPS)
    padded = jnp.pad(grouped, ((1, 1), (0, 0), (0, 0)))
    convolved = jnp.zeros((total_rows, GROUPS, DD // GROUPS), jnp.float32)
    for offset in range(3):
        convolved = convolved + jnp.einsum(
            "pgi,gio->pgo",
            padded[offset : offset + total_rows],
            conv_w[offset],
            preferred_element_type=jnp.float32,
        )
    activated = jax.nn.gelu(row_norm(convolved.reshape(total_rows, DD)), approximate=False)
    hidden = (lowered.astype(jnp.float32) + activated).astype(jnp.bfloat16)
    return jnp.dot(hidden, dec_out, preferred_element_type=jnp.float32)


def copy_terms(
    visible_in, positions, targets, w_qkv, w_out, mask_embed, dec_in, conv_w, dec_out, heads
):
    total_rows = targets.shape[0]
    if heads is None:
        branch = attention_branch(visible_in, w_qkv, w_out)
    else:
        branch = attention_from(reuse_heads(visible_in, w_qkv, heads), w_out)
    visible_out = (visible_in.astype(jnp.float32) + branch).astype(jnp.bfloat16)
    predicted = decoder_output(
        visible_out, positions, total_rows, mask_embed, dec_in, conv_w, dec_out
    )
    slot_ids = jnp.arange(total_rows, dtype=jnp.int32)
    seen = jnp.max((slot_ids[:, None] == positions[None, :]).astype(jnp.float32), axis=1)
    mismatch = (predicted - targets.astype(jnp.float32)) * (1.0 - seen)[:, None]
    return jnp.sum(mismatch * mismatch)


def ring_gather(values, group_size):
    parts = [values]
    for shift in range(1, group_size):
        pairs = [(source, (source - shift) % group_size) for source in range(group_size)]
        parts.append(lax.ppermute(values, "mask", pairs))
    return parts


def in_mask_order(parts, own_index):
    group_size = len(parts)
    blocks = []
    for block in range(group_size):
        slot = (block - own_index) % group_size
        chosen = parts[0]
        for other in range(1, group_size):
            chosen = jnp.where(slot == other, parts[other], chosen)
        blocks.append(chosen)
    return jnp.concatenate(blocks, axis=0)


def split_teacher(embedded, w_qkv, w_out, own_index, group_size):
    total_rows = embedded.shape[0]
    head_dim = D // HEADS
    heads_here = HEADS // group_size
    head_width = heads_here * head_dim
    normed = row_norm(embedded.astype(jnp.float32)).astype(jnp.bfloat16)
    own_cols = lax.dynamic_slice_in_dim(
        w_qkv.reshape(D, 3, D), own_index * head_width, head_width, 2
    )
    projected = jnp.einsum(
        "sd,dtw->stw", normed, own_cols, preferred_element_type=jnp.float32
    ).astype(jnp.bfloat16)
    context = split_project(projected.reshape(total_rows, 3, heads_here, head_dim))
    out_rows = lax.dynamic_slice_in_dim(w_out, own_index * head_width, head_width, 0)
    partial_value = jnp.dot(
        context.reshape(total_rows, head_width), out_rows, preferred_element_type=jnp.float32
    )
    return lax.psum(partial_value.astype(jnp.bfloat16), "mask").astype(jnp.float32)


def on_device(patches, visible_index, embed_w, w_qkv, w_out, mask_embed, dec_in, conv_w, dec_out):
    tok_rows = patches.shape[0]
    group_size = lax.axis_size("mask")
    own_index = lax.axis_index("mask")
    copies = visible_index.shape[0]
    visible_count = visible_index.shape[1]
    total_rows = tok_rows * group_size
    col_width = patches.shape[1] // group_size
    positions = lax.dynamic_index_in_dim(visible_index, own_index, 0, keepdims=False)
    clip_pixels = in_mask_order(ring_gather(patches, group_size), own_index)
    embedded = jnp.dot(clip_pixels, embed_w, preferred_element_type=jnp.float32).astype(
        jnp.bfloat16
    )
    visible_in = embedded[positions]
    if HEADS * total_rows * total_rows * 4 <= (1 << 24):
        clip_heads = project_heads(embedded, w_qkv)
        branch = attention_from(clip_heads, w_out)
        visible_heads = tuple(part[positions] for part in clip_heads)
    else:
        branch = split_teacher(embedded, w_qkv, w_out, own_index, group_size)
        visible_heads = None
    all_targets = row_norm(branch).astype(jnp.bfloat16)

    def objective(rows_in):
        return copy_terms(
            rows_in,
            positions,
            all_targets,
            w_qkv,
            w_out,
            mask_embed,
            dec_in,
            conv_w,
            dec_out,
            visible_heads,
        )

    squares, pullback = jax.vjp(objective, visible_in)
    factor = 0.5 / math.sqrt(copies * visible_count)
    (grad_in,) = pullback(jnp.ones_like(squares) * factor)
    copy_loss = jnp.reshape(squares / ((total_rows - visible_count) * D), (1,))
    slot_copy = (own_index + jnp.arange(group_size, dtype=jnp.int32)) % group_size
    flat_index = visible_index[slot_copy].reshape(copies * visible_count)
    own_cols = lax.dynamic_slice_in_dim(clip_pixels, own_index * col_width, col_width, 1)
    gathered = own_cols[flat_index]
    embed_grad = jnp.einsum(
        "vc,vd->cd",
        gathered,
        jnp.concatenate(ring_gather(grad_in, group_size), axis=0),
        preferred_element_type=jnp.float32,
    )
    return (embed_grad, copy_loss)


def solution(mesh):
    placed = (P(("dp", "mask"), None), P("dp", None), P(), P(), P(), P(), P(), P(), P())
    return jax.shard_map(
        on_device,
        mesh=mesh,
        in_specs=placed,
        out_specs=(P(("dp", "mask"), None), P(("dp", "mask"))),
        check_vma=False,
    )
```

```python
import math

import jax
import jax.numpy as jnp
from jax import lax
from jax.sharding import PartitionSpec as P

D = 1024
HEADS = 16
DD = 768
GROUPS = 16


EPSILON = 1e-06


def row_norm(values):
    average = jnp.mean(values, axis=-1, keepdims=True)
    centred = values - average
    spread = jnp.mean(centred * centred, axis=-1, keepdims=True)
    return centred * lax.rsqrt(spread + EPSILON)


def head_norm(values):
    return values * lax.rsqrt(jnp.mean(values * values, axis=-1, keepdims=True) + EPSILON)


def mix_heads(queries, key_rows, values):
    score_scale = 1.0 / math.sqrt(queries.shape[-1])
    scores = (
        jnp.einsum("qhd,khd->hqk", queries, key_rows, preferred_element_type=jnp.float32)
        * score_scale
    )
    exponent = jnp.exp(scores)
    weights = (exponent / jnp.sum(exponent, axis=-1, keepdims=True)).astype(jnp.bfloat16)
    mixed = jnp.einsum("hqk,khd->qhd", weights, values, preferred_element_type=jnp.float32)
    return mixed.astype(jnp.bfloat16)


def split_project(projected):
    queries = head_norm(projected[:, 0].astype(jnp.float32)).astype(jnp.bfloat16)
    key_rows = head_norm(projected[:, 1].astype(jnp.float32)).astype(jnp.bfloat16)
    return mix_heads(queries, key_rows, projected[:, 2])


def project_rows(inputs, w_qkv):
    normed = row_norm(inputs.astype(jnp.float32)).astype(jnp.bfloat16)
    return jnp.dot(normed, w_qkv, preferred_element_type=jnp.float32).astype(jnp.bfloat16)


def attention_from(projected, w_out):
    row_count = projected.shape[0]
    context = split_project(projected.reshape(row_count, 3, HEADS, D // HEADS))
    return jnp.dot(context.reshape(row_count, D), w_out, preferred_element_type=jnp.float32)


def attention_branch(inputs, w_qkv, w_out):
    return attention_from(project_rows(inputs, w_qkv), w_out)


@jax.custom_vjp
def reuse_rows(inputs, w_qkv, projected):
    return projected


def reuse_rows_fwd(inputs, w_qkv, projected):
    return projected, (inputs, w_qkv)


def reuse_rows_bwd(saved, cotangent):
    inputs, w_qkv = saved
    _, pullback = jax.vjp(lambda rows: project_rows(rows, w_qkv), inputs)
    (d_inputs,) = pullback(cotangent)
    return d_inputs, jnp.zeros_like(w_qkv), jnp.zeros_like(cotangent)


reuse_rows.defvjp(reuse_rows_fwd, reuse_rows_bwd)


def decoder_output(visible_out, positions, total_rows, mask_embed, dec_in, conv_w, dec_out):
    slot_ids = jnp.arange(total_rows, dtype=jnp.int32)
    picks = (slot_ids[:, None] == positions[None, :]).astype(jnp.bfloat16)
    seen = jnp.max(picks, axis=1, keepdims=True)
    lowered_visible = jnp.dot(visible_out, dec_in, preferred_element_type=jnp.float32).astype(
        jnp.bfloat16
    )
    lowered_mask = jnp.dot(
        mask_embed[None, :], dec_in, preferred_element_type=jnp.float32
    ).astype(jnp.bfloat16)
    placed = jnp.dot(picks, lowered_visible, preferred_element_type=jnp.float32)
    lowered = jnp.where(seen > 0, placed, lowered_mask.astype(jnp.float32)).astype(jnp.bfloat16)
    grouped = lowered.reshape(total_rows, GROUPS, DD // GROUPS)
    padded = jnp.pad(grouped, ((1, 1), (0, 0), (0, 0)))
    convolved = jnp.zeros((total_rows, GROUPS, DD // GROUPS), jnp.float32)
    for offset in range(3):
        convolved = convolved + jnp.einsum(
            "pgi,gio->pgo",
            padded[offset : offset + total_rows],
            conv_w[offset],
            preferred_element_type=jnp.float32,
        )
    activated = jax.nn.gelu(row_norm(convolved.reshape(total_rows, DD)), approximate=False)
    hidden = (lowered.astype(jnp.float32) + activated).astype(jnp.bfloat16)
    return jnp.dot(hidden, dec_out, preferred_element_type=jnp.float32)


def copy_terms(
    visible_in, positions, targets, w_qkv, w_out, mask_embed, dec_in, conv_w, dec_out, projected
):
    total_rows = targets.shape[0]
    if projected is None:
        branch = attention_branch(visible_in, w_qkv, w_out)
    else:
        branch = attention_from(reuse_rows(visible_in, w_qkv, projected), w_out)
    visible_out = (visible_in.astype(jnp.float32) + branch).astype(jnp.bfloat16)
    predicted = decoder_output(
        visible_out, positions, total_rows, mask_embed, dec_in, conv_w, dec_out
    )
    slot_ids = jnp.arange(total_rows, dtype=jnp.int32)
    seen = jnp.max((slot_ids[:, None] == positions[None, :]).astype(jnp.float32), axis=1)
    mismatch = (predicted - targets.astype(jnp.float32)) * (1.0 - seen)[:, None]
    return jnp.sum(mismatch * mismatch)


def ring_gather(values, group_size):
    parts = [values]
    for shift in range(1, group_size):
        pairs = [(source, (source - shift) % group_size) for source in range(group_size)]
        parts.append(lax.ppermute(values, "mask", pairs))
    return parts


def in_mask_order(parts, own_index):
    group_size = len(parts)
    blocks = []
    for block in range(group_size):
        slot = (block - own_index) % group_size
        chosen = parts[0]
        for other in range(1, group_size):
            chosen = jnp.where(slot == other, parts[other], chosen)
        blocks.append(chosen)
    return jnp.concatenate(blocks, axis=0)


def split_teacher(embedded, w_qkv, w_out, own_index, group_size):
    total_rows = embedded.shape[0]
    head_dim = D // HEADS
    heads_here = HEADS // group_size
    head_width = heads_here * head_dim
    normed = row_norm(embedded.astype(jnp.float32)).astype(jnp.bfloat16)
    own_cols = lax.dynamic_slice_in_dim(
        w_qkv.reshape(D, 3, D), own_index * head_width, head_width, 2
    )
    projected = jnp.einsum(
        "sd,dtw->stw", normed, own_cols, preferred_element_type=jnp.float32
    ).astype(jnp.bfloat16)
    context = split_project(projected.reshape(total_rows, 3, heads_here, head_dim))
    out_rows = lax.dynamic_slice_in_dim(w_out, own_index * head_width, head_width, 0)
    partial_value = jnp.dot(
        context.reshape(total_rows, head_width), out_rows, preferred_element_type=jnp.float32
    )
    return lax.psum(partial_value.astype(jnp.bfloat16), "mask").astype(jnp.float32)


def on_device(patches, visible_index, embed_w, w_qkv, w_out, mask_embed, dec_in, conv_w, dec_out):
    tok_rows = patches.shape[0]
    group_size = lax.axis_size("mask")
    own_index = lax.axis_index("mask")
    copies = visible_index.shape[0]
    visible_count = visible_index.shape[1]
    total_rows = tok_rows * group_size
    col_width = patches.shape[1] // group_size
    positions = lax.dynamic_index_in_dim(visible_index, own_index, 0, keepdims=False)
    clip_pixels = in_mask_order(ring_gather(patches, group_size), own_index)
    embedded = jnp.dot(clip_pixels, embed_w, preferred_element_type=jnp.float32).astype(
        jnp.bfloat16
    )
    visible_in = embedded[positions]
    if HEADS * total_rows * total_rows * 4 <= (1 << 24):
        clip_projected = project_rows(embedded, w_qkv)
        branch = attention_from(clip_projected, w_out)
        visible_projected = clip_projected[positions]
    else:
        branch = split_teacher(embedded, w_qkv, w_out, own_index, group_size)
        visible_projected = None
    all_targets = row_norm(branch).astype(jnp.bfloat16)

    def objective(rows_in):
        return copy_terms(
            rows_in,
            positions,
            all_targets,
            w_qkv,
            w_out,
            mask_embed,
            dec_in,
            conv_w,
            dec_out,
            visible_projected,
        )

    squares, pullback = jax.vjp(objective, visible_in)
    factor = 0.5 / math.sqrt(copies * visible_count)
    (grad_in,) = pullback(jnp.ones_like(squares) * factor)
    copy_loss = jnp.reshape(squares / ((total_rows - visible_count) * D), (1,))
    slot_copy = (own_index + jnp.arange(group_size, dtype=jnp.int32)) % group_size
    flat_index = visible_index[slot_copy].reshape(copies * visible_count)
    own_cols = lax.dynamic_slice_in_dim(clip_pixels, own_index * col_width, col_width, 1)
    gathered = own_cols[flat_index]
    embed_grad = jnp.einsum(
        "vc,vd->cd",
        gathered,
        jnp.concatenate(ring_gather(grad_in, group_size), axis=0),
        preferred_element_type=jnp.float32,
    )
    return (embed_grad, copy_loss)


def solution(mesh):
    placed = (P(("dp", "mask"), None), P("dp", None), P(), P(), P(), P(), P(), P(), P())
    return jax.shard_map(
        on_device,
        mesh=mesh,
        in_specs=placed,
        out_specs=(P(("dp", "mask"), None), P(("dp", "mask"))),
        check_vma=False,
    )
```

```python
import math

import jax
import jax.numpy as jnp
from jax import lax
from jax.sharding import PartitionSpec as P

D = 1024
HEADS = 16
DD = 768
GROUPS = 16


EPSILON = 1e-06


def row_norm(values):
    average = jnp.mean(values, axis=-1, keepdims=True)
    centred = values - average
    spread = jnp.mean(centred * centred, axis=-1, keepdims=True)
    return centred * lax.rsqrt(spread + EPSILON)


def head_norm(values):
    return values * lax.rsqrt(jnp.mean(values * values, axis=-1, keepdims=True) + EPSILON)


def mix_heads(queries, key_rows, values):
    score_scale = 1.0 / math.sqrt(queries.shape[-1])
    scores = (
        jnp.einsum("qhd,khd->hqk", queries, key_rows, preferred_element_type=jnp.float32)
        * score_scale
    )
    exponent = jnp.exp(scores)
    weights = (exponent / jnp.sum(exponent, axis=-1, keepdims=True)).astype(jnp.bfloat16)
    mixed = jnp.einsum("hqk,khd->qhd", weights, values, preferred_element_type=jnp.float32)
    return mixed.astype(jnp.bfloat16)


def split_project(projected):
    queries = head_norm(projected[:, 0].astype(jnp.float32)).astype(jnp.bfloat16)
    key_rows = head_norm(projected[:, 1].astype(jnp.float32)).astype(jnp.bfloat16)
    return mix_heads(queries, key_rows, projected[:, 2])


def project_rows(inputs, w_qkv):
    normed = row_norm(inputs.astype(jnp.float32)).astype(jnp.bfloat16)
    return jnp.dot(normed, w_qkv, preferred_element_type=jnp.float32).astype(jnp.bfloat16)


def attention_from(projected, w_out):
    row_count = projected.shape[0]
    context = split_project(projected.reshape(row_count, 3, HEADS, D // HEADS))
    return jnp.dot(context.reshape(row_count, D), w_out, preferred_element_type=jnp.float32)


def attention_branch(inputs, w_qkv, w_out):
    return attention_from(project_rows(inputs, w_qkv), w_out)


@jax.custom_vjp
def reuse_rows(inputs, w_qkv, projected):
    return projected


def reuse_rows_fwd(inputs, w_qkv, projected):
    return projected, (inputs, w_qkv)


def reuse_rows_bwd(saved, cotangent):
    inputs, w_qkv = saved
    _, pullback = jax.vjp(
        lambda rows: row_norm(rows.astype(jnp.float32)).astype(jnp.bfloat16), inputs
    )
    d_normed = jnp.dot(w_qkv, cotangent.T, preferred_element_type=jnp.float32).T
    (d_inputs,) = pullback(d_normed.astype(jnp.bfloat16))
    return d_inputs, jnp.zeros_like(w_qkv), jnp.zeros_like(cotangent)


reuse_rows.defvjp(reuse_rows_fwd, reuse_rows_bwd)


def decoder_output(visible_out, positions, total_rows, mask_embed, dec_in, conv_w, dec_out):
    slot_ids = jnp.arange(total_rows, dtype=jnp.int32)
    picks = (slot_ids[:, None] == positions[None, :]).astype(jnp.bfloat16)
    seen = jnp.max(picks, axis=1, keepdims=True)
    lowered_visible = jnp.dot(visible_out, dec_in, preferred_element_type=jnp.float32).astype(
        jnp.bfloat16
    )
    lowered_mask = jnp.dot(
        mask_embed[None, :], dec_in, preferred_element_type=jnp.float32
    ).astype(jnp.bfloat16)
    placed = jnp.dot(picks, lowered_visible, preferred_element_type=jnp.float32)
    lowered = jnp.where(seen > 0, placed, lowered_mask.astype(jnp.float32)).astype(jnp.bfloat16)
    grouped = lowered.reshape(total_rows, GROUPS, DD // GROUPS)
    padded = jnp.pad(grouped, ((1, 1), (0, 0), (0, 0)))
    convolved = jnp.zeros((total_rows, GROUPS, DD // GROUPS), jnp.float32)
    for offset in range(3):
        convolved = convolved + jnp.einsum(
            "pgi,gio->pgo",
            padded[offset : offset + total_rows],
            conv_w[offset],
            preferred_element_type=jnp.float32,
        )
    activated = jax.nn.gelu(row_norm(convolved.reshape(total_rows, DD)), approximate=False)
    hidden = (lowered.astype(jnp.float32) + activated).astype(jnp.bfloat16)
    return lax.optimization_barrier(
        jnp.dot(hidden, dec_out, preferred_element_type=jnp.float32)
    )


def copy_terms(
    visible_in, positions, targets, w_qkv, w_out, mask_embed, dec_in, conv_w, dec_out, projected
):
    total_rows = targets.shape[0]
    if projected is None:
        branch = attention_branch(visible_in, w_qkv, w_out)
    else:
        branch = attention_from(reuse_rows(visible_in, w_qkv, projected), w_out)
    visible_out = (visible_in.astype(jnp.float32) + branch).astype(jnp.bfloat16)
    predicted = decoder_output(
        visible_out, positions, total_rows, mask_embed, dec_in, conv_w, dec_out
    )
    slot_ids = jnp.arange(total_rows, dtype=jnp.int32)
    seen = jnp.max((slot_ids[:, None] == positions[None, :]).astype(jnp.float32), axis=1)
    mismatch = (predicted - targets.astype(jnp.float32)) * (1.0 - seen)[:, None]
    return jnp.sum(mismatch * mismatch)


def ring_gather(values, group_size):
    parts = [values]
    for shift in range(1, group_size):
        pairs = [(source, (source - shift) % group_size) for source in range(group_size)]
        parts.append(lax.ppermute(values, "mask", pairs))
    return parts


def in_mask_order(parts, own_index):
    group_size = len(parts)
    blocks = []
    for block in range(group_size):
        slot = (block - own_index) % group_size
        chosen = parts[0]
        for other in range(1, group_size):
            chosen = jnp.where(slot == other, parts[other], chosen)
        blocks.append(chosen)
    return jnp.concatenate(blocks, axis=0)


def split_teacher(embedded, w_qkv, w_out, own_index, group_size):
    total_rows = embedded.shape[0]
    head_dim = D // HEADS
    heads_here = HEADS // group_size
    head_width = heads_here * head_dim
    normed = row_norm(embedded.astype(jnp.float32)).astype(jnp.bfloat16)
    own_cols = lax.dynamic_slice_in_dim(
        w_qkv.reshape(D, 3, D), own_index * head_width, head_width, 2
    )
    projected = jnp.einsum(
        "sd,dtw->stw", normed, own_cols, preferred_element_type=jnp.float32
    ).astype(jnp.bfloat16)
    context = split_project(projected.reshape(total_rows, 3, heads_here, head_dim))
    out_rows = lax.dynamic_slice_in_dim(w_out, own_index * head_width, head_width, 0)
    partial_value = jnp.dot(
        context.reshape(total_rows, head_width), out_rows, preferred_element_type=jnp.float32
    )
    return lax.psum(partial_value.astype(jnp.bfloat16), "mask").astype(jnp.float32)


def on_device(patches, visible_index, embed_w, w_qkv, w_out, mask_embed, dec_in, conv_w, dec_out):
    tok_rows = patches.shape[0]
    group_size = lax.axis_size("mask")
    own_index = lax.axis_index("mask")
    copies = visible_index.shape[0]
    visible_count = visible_index.shape[1]
    total_rows = tok_rows * group_size
    col_width = patches.shape[1] // group_size
    positions = lax.dynamic_index_in_dim(visible_index, own_index, 0, keepdims=False)
    clip_pixels = in_mask_order(ring_gather(patches, group_size), own_index)
    embedded = jnp.dot(clip_pixels, embed_w, preferred_element_type=jnp.float32).astype(
        jnp.bfloat16
    )
    clip_ids = jnp.arange(total_rows, dtype=jnp.int32)
    own_picks = (positions[:, None] == clip_ids[None, :]).astype(jnp.bfloat16)
    visible_in = jnp.dot(own_picks, embedded, preferred_element_type=jnp.float32).astype(
        jnp.bfloat16
    )
    if HEADS * total_rows * total_rows * 4 <= (1 << 24):
        clip_projected = project_rows(embedded, w_qkv)
        branch = attention_from(clip_projected, w_out)
        visible_projected = jnp.dot(
            own_picks, clip_projected, preferred_element_type=jnp.float32
        ).astype(jnp.bfloat16)
    else:
        branch = split_teacher(embedded, w_qkv, w_out, own_index, group_size)
        visible_projected = None
    all_targets = row_norm(branch).astype(jnp.bfloat16)

    def objective(rows_in):
        return copy_terms(
            rows_in,
            positions,
            all_targets,
            w_qkv,
            w_out,
            mask_embed,
            dec_in,
            conv_w,
            dec_out,
            visible_projected,
        )

    squares, pullback = jax.vjp(objective, visible_in)
    factor = 0.5 / math.sqrt(copies * visible_count)
    (grad_in,) = pullback(jnp.ones_like(squares) * factor)
    copy_loss = jnp.reshape(squares / ((total_rows - visible_count) * D), (1,))
    slot_copy = (own_index + jnp.arange(group_size, dtype=jnp.int32)) % group_size
    flat_index = visible_index[slot_copy].reshape(copies * visible_count)
    own_cols = lax.dynamic_slice_in_dim(clip_pixels, own_index * col_width, col_width, 1)
    all_picks = (flat_index[:, None] == clip_ids[None, :]).astype(jnp.bfloat16)
    gathered = jnp.dot(all_picks, own_cols, preferred_element_type=jnp.float32).astype(
        jnp.bfloat16
    )
    embed_grad = jnp.einsum(
        "vc,vd->cd",
        gathered,
        jnp.concatenate(ring_gather(grad_in, group_size), axis=0),
        preferred_element_type=jnp.float32,
    )
    return (embed_grad, copy_loss)


def solution(mesh):
    placed = (P(("dp", "mask"), None), P("dp", None), P(), P(), P(), P(), P(), P(), P())
    return jax.shard_map(
        on_device,
        mesh=mesh,
        in_specs=placed,
        out_specs=(P(("dp", "mask"), None), P(("dp", "mask"))),
        check_vma=False,
    )
```

```python
import math

import jax
import jax.numpy as jnp
from jax import lax
from jax.experimental import pallas as pl
from jax.experimental.pallas import tpu as pltpu
from jax.sharding import PartitionSpec as P

D = 1024
HEADS = 16
DD = 768
GROUPS = 16


EPSILON = 1e-06


def row_norm(values):
    average = jnp.mean(values, axis=-1, keepdims=True)
    centred = values - average
    spread = jnp.mean(centred * centred, axis=-1, keepdims=True)
    return centred * lax.rsqrt(spread + EPSILON)


def head_norm(values):
    return values * lax.rsqrt(jnp.mean(values * values, axis=-1, keepdims=True) + EPSILON)


def mix_heads(queries, key_rows, values):
    score_scale = 1.0 / math.sqrt(queries.shape[-1])
    scores = (
        jnp.einsum("qhd,khd->hqk", queries, key_rows, preferred_element_type=jnp.float32)
        * score_scale
    )
    exponent = jnp.exp(scores)
    weights = (exponent / jnp.sum(exponent, axis=-1, keepdims=True)).astype(jnp.bfloat16)
    mixed = jnp.einsum("hqk,khd->qhd", weights, values, preferred_element_type=jnp.float32)
    return mixed.astype(jnp.bfloat16)


def split_project(projected):
    queries = head_norm(projected[:, 0].astype(jnp.float32)).astype(jnp.bfloat16)
    key_rows = head_norm(projected[:, 1].astype(jnp.float32)).astype(jnp.bfloat16)
    return mix_heads(queries, key_rows, projected[:, 2])


def attention_branch(inputs, w_qkv, w_out):
    row_count = inputs.shape[0]
    normed = row_norm(inputs.astype(jnp.float32)).astype(jnp.bfloat16)
    projected = jnp.dot(normed, w_qkv, preferred_element_type=jnp.float32).astype(jnp.bfloat16)
    context = split_project(projected.reshape(row_count, 3, HEADS, D // HEADS))
    return jnp.dot(context.reshape(row_count, D), w_out, preferred_element_type=jnp.float32)


def decoder_output(visible_out, positions, total_rows, mask_embed, dec_in, conv_w, dec_out):
    slot_ids = jnp.arange(total_rows, dtype=jnp.int32)
    picks = (slot_ids[:, None] == positions[None, :]).astype(jnp.bfloat16)
    seen = jnp.max(picks, axis=1, keepdims=True)
    lowered_visible = jnp.dot(visible_out, dec_in, preferred_element_type=jnp.float32).astype(
        jnp.bfloat16
    )
    lowered_mask = jnp.dot(
        mask_embed[None, :], dec_in, preferred_element_type=jnp.float32
    ).astype(jnp.bfloat16)
    placed = jnp.dot(picks, lowered_visible, preferred_element_type=jnp.float32)
    lowered = jnp.where(seen > 0, placed, lowered_mask.astype(jnp.float32)).astype(jnp.bfloat16)
    grouped = lowered.reshape(total_rows, GROUPS, DD // GROUPS)
    padded = jnp.pad(grouped, ((1, 1), (0, 0), (0, 0)))
    convolved = jnp.zeros((total_rows, GROUPS, DD // GROUPS), jnp.float32)
    for offset in range(3):
        convolved = convolved + jnp.einsum(
            "pgi,gio->pgo",
            padded[offset : offset + total_rows],
            conv_w[offset],
            preferred_element_type=jnp.float32,
        )
    activated = jax.nn.gelu(row_norm(convolved.reshape(total_rows, DD)), approximate=False)
    hidden = (lowered.astype(jnp.float32) + activated).astype(jnp.bfloat16)
    return jnp.dot(hidden, dec_out, preferred_element_type=jnp.float32)


def copy_terms(visible_in, positions, targets, w_qkv, w_out, mask_embed, dec_in, conv_w, dec_out):
    total_rows = targets.shape[0]
    visible_out = (
        visible_in.astype(jnp.float32) + attention_branch(visible_in, w_qkv, w_out)
    ).astype(jnp.bfloat16)
    predicted = decoder_output(
        visible_out, positions, total_rows, mask_embed, dec_in, conv_w, dec_out
    )
    slot_ids = jnp.arange(total_rows, dtype=jnp.int32)
    seen = jnp.max((slot_ids[:, None] == positions[None, :]).astype(jnp.float32), axis=1)
    mismatch = (predicted - targets.astype(jnp.float32)) * (1.0 - seen)[:, None]
    return jnp.sum(mismatch * mismatch)


def teacher_kernel(pixels_ref, embed_w_ref, w_qkv_ref, w_out_ref, embedded_ref, targets_ref,
                   context_ref):
    rows = pixels_ref.shape[0]
    head_dim = D // HEADS
    embedded = jnp.dot(pixels_ref[...], embed_w_ref[...], preferred_element_type=jnp.float32)
    embedded = embedded.astype(jnp.bfloat16)
    embedded_ref[...] = embedded
    values = embedded.astype(jnp.float32)
    average = jnp.mean(values, axis=-1, keepdims=True)
    centred = values - average
    spread = jnp.mean(centred * centred, axis=-1, keepdims=True)
    normed = (centred * lax.rsqrt(spread + EPSILON)).astype(jnp.bfloat16)
    lane = lax.broadcasted_iota(jnp.int32, (rows, 2 * head_dim), 1)
    first = lane < head_dim
    score_scale = 1.0 / math.sqrt(head_dim)

    def pair_norm(block):
        squares = block * block
        low = jnp.sum(jnp.where(first, squares, 0.0), axis=-1, keepdims=True) / head_dim
        high = jnp.sum(jnp.where(first, 0.0, squares), axis=-1, keepdims=True) / head_dim
        scale = jnp.where(first, lax.rsqrt(low + EPSILON), lax.rsqrt(high + EPSILON))
        return (block * scale).astype(jnp.bfloat16)

    for pair in range(HEADS // 2):
        width = 2 * head_dim
        cols = slice(pair * width, (pair + 1) * width)
        q_block = jnp.dot(normed, w_qkv_ref[:, pair * width:(pair + 1) * width],
                          preferred_element_type=jnp.float32).astype(jnp.bfloat16)
        k_block = jnp.dot(normed, w_qkv_ref[:, D + pair * width:D + (pair + 1) * width],
                          preferred_element_type=jnp.float32).astype(jnp.bfloat16)
        v_block = jnp.dot(normed, w_qkv_ref[:, 2 * D + pair * width:2 * D + (pair + 1) * width],
                          preferred_element_type=jnp.float32).astype(jnp.bfloat16)
        queries = pair_norm(q_block.astype(jnp.float32))
        key_rows = pair_norm(k_block.astype(jnp.float32))
        zero = jnp.zeros_like(queries)
        mixed = []
        for half in range(2):
            chosen = first if half == 0 else jnp.logical_not(first)
            scores = lax.dot_general(
                jnp.where(chosen, queries, zero), key_rows,
                (((1,), (1,)), ((), ())), preferred_element_type=jnp.float32) * score_scale
            exponent = jnp.exp(scores)
            weights = (exponent / jnp.sum(exponent, axis=-1, keepdims=True)).astype(jnp.bfloat16)
            mixed.append(jnp.dot(weights, v_block, preferred_element_type=jnp.float32))
        context = jnp.where(first, mixed[0], mixed[1]).astype(jnp.bfloat16)
        context_ref[:, cols] = context
    branch = jnp.dot(context_ref[...], w_out_ref[...], preferred_element_type=jnp.float32)
    average = jnp.mean(branch, axis=-1, keepdims=True)
    centred = branch - average
    spread = jnp.mean(centred * centred, axis=-1, keepdims=True)
    targets_ref[...] = (centred * lax.rsqrt(spread + EPSILON)).astype(jnp.bfloat16)


def teacher(pixels, embed_w, w_qkv, w_out):
    rows = pixels.shape[0]
    return pl.pallas_call(
        teacher_kernel,
        out_shape=(jax.ShapeDtypeStruct((rows, D), jnp.bfloat16),
                   jax.ShapeDtypeStruct((rows, D), jnp.bfloat16)),
        scratch_shapes=[pltpu.VMEM((rows, D), jnp.bfloat16)],
    )(pixels, embed_w, w_qkv, w_out)


def ring_gather(values, group_size):
    parts = [values]
    for shift in range(1, group_size):
        pairs = [(source, (source - shift) % group_size) for source in range(group_size)]
        parts.append(lax.ppermute(values, "mask", pairs))
    return parts


def in_mask_order(parts, own_index):
    group_size = len(parts)
    blocks = []
    for block in range(group_size):
        slot = (block - own_index) % group_size
        chosen = parts[0]
        for other in range(1, group_size):
            chosen = jnp.where(slot == other, parts[other], chosen)
        blocks.append(chosen)
    return jnp.concatenate(blocks, axis=0)


def split_teacher(embedded, w_qkv, w_out, own_index, group_size):
    total_rows = embedded.shape[0]
    head_dim = D // HEADS
    heads_here = HEADS // group_size
    head_width = heads_here * head_dim
    normed = row_norm(embedded.astype(jnp.float32)).astype(jnp.bfloat16)
    own_cols = lax.dynamic_slice_in_dim(
        w_qkv.reshape(D, 3, D), own_index * head_width, head_width, 2
    )
    projected = jnp.einsum(
        "sd,dtw->stw", normed, own_cols, preferred_element_type=jnp.float32
    ).astype(jnp.bfloat16)
    context = split_project(projected.reshape(total_rows, 3, heads_here, head_dim))
    out_rows = lax.dynamic_slice_in_dim(w_out, own_index * head_width, head_width, 0)
    partial_value = jnp.dot(
        context.reshape(total_rows, head_width), out_rows, preferred_element_type=jnp.float32
    )
    return lax.psum(partial_value.astype(jnp.bfloat16), "mask").astype(jnp.float32)


def on_device(patches, visible_index, embed_w, w_qkv, w_out, mask_embed, dec_in, conv_w, dec_out):
    tok_rows = patches.shape[0]
    group_size = lax.axis_size("mask")
    own_index = lax.axis_index("mask")
    copies = visible_index.shape[0]
    visible_count = visible_index.shape[1]
    total_rows = tok_rows * group_size
    col_width = patches.shape[1] // group_size
    positions = lax.dynamic_index_in_dim(visible_index, own_index, 0, keepdims=False)
    clip_pixels = in_mask_order(ring_gather(patches, group_size), own_index)
    if total_rows <= 256:
        embedded, all_targets = teacher(clip_pixels, embed_w, w_qkv, w_out)
    else:
        embedded = jnp.dot(clip_pixels, embed_w, preferred_element_type=jnp.float32).astype(
            jnp.bfloat16
        )
        branch = split_teacher(embedded, w_qkv, w_out, own_index, group_size)
        all_targets = row_norm(branch).astype(jnp.bfloat16)
    visible_in = embedded[positions]

    def objective(rows_in):
        return copy_terms(
            rows_in, positions, all_targets, w_qkv, w_out, mask_embed, dec_in, conv_w, dec_out
        )

    squares, pullback = jax.vjp(objective, visible_in)
    factor = 0.5 / math.sqrt(copies * visible_count)
    (grad_in,) = pullback(jnp.ones_like(squares) * factor)
    copy_loss = jnp.reshape(squares / ((total_rows - visible_count) * D), (1,))
    slot_copy = (own_index + jnp.arange(group_size, dtype=jnp.int32)) % group_size
    flat_index = visible_index[slot_copy].reshape(copies * visible_count)
    own_cols = lax.dynamic_slice_in_dim(clip_pixels, own_index * col_width, col_width, 1)
    gathered = own_cols[flat_index]
    embed_grad = jnp.einsum(
        "vc,vd->cd",
        gathered,
        jnp.concatenate(ring_gather(grad_in, group_size), axis=0),
        preferred_element_type=jnp.float32,
    )
    return (embed_grad, copy_loss)


def solution(mesh):
    placed = (P(("dp", "mask"), None), P("dp", None), P(), P(), P(), P(), P(), P(), P())
    return jax.shard_map(
        on_device,
        mesh=mesh,
        in_specs=placed,
        out_specs=(P(("dp", "mask"), None), P(("dp", "mask"))),
        check_vma=False,
    )
```

```python
import math

import jax
import jax.numpy as jnp
from jax import lax
from jax.experimental import pallas as pl
from jax.experimental.pallas import tpu as pltpu
from jax.sharding import PartitionSpec as P

D = 1024
HEADS = 16
DD = 768
GROUPS = 16


EPSILON = 1e-06


def row_norm(values):
    average = jnp.mean(values, axis=-1, keepdims=True)
    centred = values - average
    spread = jnp.mean(centred * centred, axis=-1, keepdims=True)
    return centred * lax.rsqrt(spread + EPSILON)


def head_norm(values):
    return values * lax.rsqrt(jnp.mean(values * values, axis=-1, keepdims=True) + EPSILON)


def mix_heads(queries, key_rows, values):
    score_scale = 1.0 / math.sqrt(queries.shape[-1])
    scores = (
        jnp.einsum("qhd,khd->hqk", queries, key_rows, preferred_element_type=jnp.float32)
        * score_scale
    )
    exponent = jnp.exp(scores)
    weights = (exponent / jnp.sum(exponent, axis=-1, keepdims=True)).astype(jnp.bfloat16)
    mixed = jnp.einsum("hqk,khd->qhd", weights, values, preferred_element_type=jnp.float32)
    return mixed.astype(jnp.bfloat16)


def split_project(projected):
    queries = head_norm(projected[:, 0].astype(jnp.float32)).astype(jnp.bfloat16)
    key_rows = head_norm(projected[:, 1].astype(jnp.float32)).astype(jnp.bfloat16)
    return mix_heads(queries, key_rows, projected[:, 2])


def attention_branch(inputs, w_qkv, w_out):
    row_count = inputs.shape[0]
    normed = row_norm(inputs.astype(jnp.float32)).astype(jnp.bfloat16)
    projected = jnp.dot(normed, w_qkv, preferred_element_type=jnp.float32).astype(jnp.bfloat16)
    context = split_project(projected.reshape(row_count, 3, HEADS, D // HEADS))
    return jnp.dot(context.reshape(row_count, D), w_out, preferred_element_type=jnp.float32)


def decoder_output(visible_out, positions, total_rows, mask_embed, dec_in, conv_w, dec_out):
    slot_ids = jnp.arange(total_rows, dtype=jnp.int32)
    picks = (slot_ids[:, None] == positions[None, :]).astype(jnp.bfloat16)
    seen = jnp.max(picks, axis=1, keepdims=True)
    lowered_visible = jnp.dot(visible_out, dec_in, preferred_element_type=jnp.float32).astype(
        jnp.bfloat16
    )
    lowered_mask = jnp.dot(
        mask_embed[None, :], dec_in, preferred_element_type=jnp.float32
    ).astype(jnp.bfloat16)
    placed = jnp.dot(picks, lowered_visible, preferred_element_type=jnp.float32)
    lowered = jnp.where(seen > 0, placed, lowered_mask.astype(jnp.float32)).astype(jnp.bfloat16)
    grouped = lowered.reshape(total_rows, GROUPS, DD // GROUPS)
    padded = jnp.pad(grouped, ((1, 1), (0, 0), (0, 0)))
    convolved = jnp.zeros((total_rows, GROUPS, DD // GROUPS), jnp.float32)
    for offset in range(3):
        convolved = convolved + jnp.einsum(
            "pgi,gio->pgo",
            padded[offset : offset + total_rows],
            conv_w[offset],
            preferred_element_type=jnp.float32,
        )
    activated = jax.nn.gelu(row_norm(convolved.reshape(total_rows, DD)), approximate=False)
    hidden = (lowered.astype(jnp.float32) + activated).astype(jnp.bfloat16)
    return jnp.dot(hidden, dec_out, preferred_element_type=jnp.float32)


def copy_terms(visible_in, positions, targets, w_qkv, w_out, mask_embed, dec_in, conv_w, dec_out):
    total_rows = targets.shape[0]
    visible_out = (
        visible_in.astype(jnp.float32) + attention_branch(visible_in, w_qkv, w_out)
    ).astype(jnp.bfloat16)
    predicted = decoder_output(
        visible_out, positions, total_rows, mask_embed, dec_in, conv_w, dec_out
    )
    slot_ids = jnp.arange(total_rows, dtype=jnp.int32)
    seen = jnp.max((slot_ids[:, None] == positions[None, :]).astype(jnp.float32), axis=1)
    mismatch = (predicted - targets.astype(jnp.float32)) * (1.0 - seen)[:, None]
    return jnp.sum(mismatch * mismatch)


def teacher_kernel(embedded_ref, q_ref, k_ref, v_ref, w_out_ref, targets_ref, normed_ref, acc_ref):
    pair = pl.program_id(0)
    rows = embedded_ref.shape[0]
    head_dim = D // HEADS

    @pl.when(pair == 0)
    def _():
        values = embedded_ref[...].astype(jnp.float32)
        average = jnp.mean(values, axis=-1, keepdims=True)
        centred = values - average
        spread = jnp.mean(centred * centred, axis=-1, keepdims=True)
        normed_ref[...] = (centred * lax.rsqrt(spread + EPSILON)).astype(jnp.bfloat16)

    normed = normed_ref[...]
    lane = lax.broadcasted_iota(jnp.int32, (rows, 2 * head_dim), 1)
    first = lane < head_dim
    score_scale = 1.0 / math.sqrt(head_dim)

    def pair_norm(block):
        squares = block * block
        low = jnp.sum(jnp.where(first, squares, 0.0), axis=-1, keepdims=True) / head_dim
        high = jnp.sum(jnp.where(first, 0.0, squares), axis=-1, keepdims=True) / head_dim
        scale = jnp.where(first, lax.rsqrt(low + EPSILON), lax.rsqrt(high + EPSILON))
        return (block * scale).astype(jnp.bfloat16)

    def project(w_ref):
        return jnp.dot(normed, w_ref[...], preferred_element_type=jnp.float32).astype(jnp.bfloat16)

    queries = pair_norm(project(q_ref).astype(jnp.float32))
    key_rows = pair_norm(project(k_ref).astype(jnp.float32))
    v_block = project(v_ref)
    zero = jnp.zeros_like(queries)
    mixed = []
    for half in range(2):
        chosen = first if half == 0 else jnp.logical_not(first)
        scores = lax.dot_general(
            jnp.where(chosen, queries, zero), key_rows,
            (((1,), (1,)), ((), ())), preferred_element_type=jnp.float32) * score_scale
        exponent = jnp.exp(scores)
        weights = (exponent / jnp.sum(exponent, axis=-1, keepdims=True)).astype(jnp.bfloat16)
        mixed.append(jnp.dot(weights, v_block, preferred_element_type=jnp.float32))
    context = jnp.where(first, mixed[0], mixed[1]).astype(jnp.bfloat16)
    part = jnp.dot(context, w_out_ref[...], preferred_element_type=jnp.float32)

    @pl.when(pair == 0)
    def _():
        acc_ref[...] = part

    @pl.when(pair > 0)
    def _():
        acc_ref[...] += part

    @pl.when(pair == pl.num_programs(0) - 1)
    def _():
        branch = acc_ref[...]
        average = jnp.mean(branch, axis=-1, keepdims=True)
        centred = branch - average
        spread = jnp.mean(centred * centred, axis=-1, keepdims=True)
        targets_ref[...] = (centred * lax.rsqrt(spread + EPSILON)).astype(jnp.bfloat16)


def teacher(embedded, w_qkv, w_out):
    rows = embedded.shape[0]
    width = 2 * (D // HEADS)
    pairs = HEADS // 2
    return pl.pallas_call(
        teacher_kernel,
        grid=(pairs,),
        in_specs=[
            pl.BlockSpec((rows, D), lambda p: (0, 0)),
            pl.BlockSpec((D, width), lambda p: (0, p)),
            pl.BlockSpec((D, width), lambda p: (0, pairs + p)),
            pl.BlockSpec((D, width), lambda p: (0, 2 * pairs + p)),
            pl.BlockSpec((width, D), lambda p: (p, 0)),
        ],
        out_specs=pl.BlockSpec((rows, D), lambda p: (0, 0)),
        out_shape=jax.ShapeDtypeStruct((rows, D), jnp.bfloat16),
        scratch_shapes=[pltpu.VMEM((rows, D), jnp.bfloat16), pltpu.VMEM((rows, D), jnp.float32)],
    )(embedded, w_qkv, w_qkv, w_qkv, w_out)


def ring_gather(values, group_size):
    parts = [values]
    for shift in range(1, group_size):
        pairs = [(source, (source - shift) % group_size) for source in range(group_size)]
        parts.append(lax.ppermute(values, "mask", pairs))
    return parts


def in_mask_order(parts, own_index):
    group_size = len(parts)
    blocks = []
    for block in range(group_size):
        slot = (block - own_index) % group_size
        chosen = parts[0]
        for other in range(1, group_size):
            chosen = jnp.where(slot == other, parts[other], chosen)
        blocks.append(chosen)
    return jnp.concatenate(blocks, axis=0)


def split_teacher(embedded, w_qkv, w_out, own_index, group_size):
    total_rows = embedded.shape[0]
    head_dim = D // HEADS
    heads_here = HEADS // group_size
    head_width = heads_here * head_dim
    normed = row_norm(embedded.astype(jnp.float32)).astype(jnp.bfloat16)
    own_cols = lax.dynamic_slice_in_dim(
        w_qkv.reshape(D, 3, D), own_index * head_width, head_width, 2
    )
    projected = jnp.einsum(
        "sd,dtw->stw", normed, own_cols, preferred_element_type=jnp.float32
    ).astype(jnp.bfloat16)
    context = split_project(projected.reshape(total_rows, 3, heads_here, head_dim))
    out_rows = lax.dynamic_slice_in_dim(w_out, own_index * head_width, head_width, 0)
    partial_value = jnp.dot(
        context.reshape(total_rows, head_width), out_rows, preferred_element_type=jnp.float32
    )
    return lax.psum(partial_value.astype(jnp.bfloat16), "mask").astype(jnp.float32)


def on_device(patches, visible_index, embed_w, w_qkv, w_out, mask_embed, dec_in, conv_w, dec_out):
    tok_rows = patches.shape[0]
    group_size = lax.axis_size("mask")
    own_index = lax.axis_index("mask")
    copies = visible_index.shape[0]
    visible_count = visible_index.shape[1]
    total_rows = tok_rows * group_size
    col_width = patches.shape[1] // group_size
    positions = lax.dynamic_index_in_dim(visible_index, own_index, 0, keepdims=False)
    clip_pixels = in_mask_order(ring_gather(patches, group_size), own_index)
    embedded = jnp.dot(clip_pixels, embed_w, preferred_element_type=jnp.float32).astype(
        jnp.bfloat16
    )
    visible_in = embedded[positions]
    if total_rows <= 256:
        all_targets = teacher(embedded, w_qkv, w_out)
    else:
        branch = split_teacher(embedded, w_qkv, w_out, own_index, group_size)
        all_targets = row_norm(branch).astype(jnp.bfloat16)

    def objective(rows_in):
        return copy_terms(
            rows_in, positions, all_targets, w_qkv, w_out, mask_embed, dec_in, conv_w, dec_out
        )

    squares, pullback = jax.vjp(objective, visible_in)
    factor = 0.5 / math.sqrt(copies * visible_count)
    (grad_in,) = pullback(jnp.ones_like(squares) * factor)
    copy_loss = jnp.reshape(squares / ((total_rows - visible_count) * D), (1,))
    slot_copy = (own_index + jnp.arange(group_size, dtype=jnp.int32)) % group_size
    flat_index = visible_index[slot_copy].reshape(copies * visible_count)
    own_cols = lax.dynamic_slice_in_dim(clip_pixels, own_index * col_width, col_width, 1)
    gathered = own_cols[flat_index]
    embed_grad = jnp.einsum(
        "vc,vd->cd",
        gathered,
        jnp.concatenate(ring_gather(grad_in, group_size), axis=0),
        preferred_element_type=jnp.float32,
    )
    return (embed_grad, copy_loss)


def solution(mesh):
    placed = (P(("dp", "mask"), None), P("dp", None), P(), P(), P(), P(), P(), P(), P())
    return jax.shard_map(
        on_device,
        mesh=mesh,
        in_specs=placed,
        out_specs=(P(("dp", "mask"), None), P(("dp", "mask"))),
        check_vma=False,
    )
```

```python
import math

import jax
import jax.numpy as jnp
from jax import lax
from jax.sharding import PartitionSpec as P

D = 1024
HEADS = 16
DD = 768
GROUPS = 16


EPSILON = 1e-06


def row_norm(values):
    average = jnp.mean(values, axis=-1, keepdims=True)
    centred = values - average
    spread = jnp.mean(centred * centred, axis=-1, keepdims=True)
    return centred * lax.rsqrt(spread + EPSILON)


def head_norm(values):
    return values * lax.rsqrt(jnp.mean(values * values, axis=-1, keepdims=True) + EPSILON)


def mix_heads(queries, key_rows, values):
    score_scale = 1.0 / math.sqrt(queries.shape[-1])
    scores = (
        jnp.einsum("qhd,khd->hqk", queries, key_rows, preferred_element_type=jnp.float32)
        * score_scale
    )
    exponent = jnp.exp(scores)
    weights = (exponent / jnp.sum(exponent, axis=-1, keepdims=True)).astype(jnp.bfloat16)
    mixed = jnp.einsum("hqk,khd->qhd", weights, values, preferred_element_type=jnp.float32)
    return mixed.astype(jnp.bfloat16)


def split_project(projected):
    queries = head_norm(projected[:, 0].astype(jnp.float32)).astype(jnp.bfloat16)
    key_rows = head_norm(projected[:, 1].astype(jnp.float32)).astype(jnp.bfloat16)
    return mix_heads(queries, key_rows, projected[:, 2])


def project_rows(inputs, w_qkv):
    normed = row_norm(inputs.astype(jnp.float32)).astype(jnp.bfloat16)
    return jnp.dot(normed, w_qkv, preferred_element_type=jnp.float32).astype(jnp.bfloat16)


def attention_from(projected, w_out):
    row_count = projected.shape[0]
    context = split_project(projected.reshape(row_count, 3, HEADS, D // HEADS))
    return jnp.dot(context.reshape(row_count, D), w_out, preferred_element_type=jnp.float32)


def attention_branch(inputs, w_qkv, w_out):
    return attention_from(project_rows(inputs, w_qkv), w_out)


@jax.custom_vjp
def reuse_rows(inputs, w_qkv, projected):
    return projected


def reuse_rows_fwd(inputs, w_qkv, projected):
    return projected, (inputs, w_qkv)


def reuse_rows_bwd(saved, cotangent):
    inputs, w_qkv = saved
    _, pullback = jax.vjp(lambda rows: project_rows(rows, w_qkv), inputs)
    (d_inputs,) = pullback(cotangent)
    return d_inputs, jnp.zeros_like(w_qkv), jnp.zeros_like(cotangent)


reuse_rows.defvjp(reuse_rows_fwd, reuse_rows_bwd)


def decoder_output(visible_out, positions, total_rows, mask_embed, dec_in, conv_w, dec_out):
    slot_ids = jnp.arange(total_rows, dtype=jnp.int32)
    picks = (slot_ids[:, None] == positions[None, :]).astype(jnp.bfloat16)
    seen = jnp.max(picks, axis=1, keepdims=True)
    lowered_visible = jnp.dot(visible_out, dec_in, preferred_element_type=jnp.float32).astype(
        jnp.bfloat16
    )
    lowered_mask = jnp.dot(
        mask_embed[None, :], dec_in, preferred_element_type=jnp.float32
    ).astype(jnp.bfloat16)
    placed = jnp.dot(picks, lowered_visible, preferred_element_type=jnp.float32)
    lowered = jnp.where(seen > 0, placed, lowered_mask.astype(jnp.float32)).astype(jnp.bfloat16)
    padded = jnp.pad(lowered, ((1, 1), (0, 0)))
    group_width = DD // GROUPS
    same_group = (
        jnp.arange(GROUPS)[:, None, None, None] == jnp.arange(GROUPS)[None, None, :, None]
    )
    convolved = jnp.zeros((total_rows, DD), jnp.float32)
    for offset in range(3):
        spread_w = jnp.where(
            same_group, conv_w[offset][:, :, None, :], jnp.zeros((), conv_w.dtype)
        ).reshape(DD, DD)
        convolved = convolved + jnp.dot(
            padded[offset : offset + total_rows],
            spread_w,
            preferred_element_type=jnp.float32,
        )
    activated = jax.nn.gelu(row_norm(convolved), approximate=False)
    hidden = (lowered.astype(jnp.float32) + activated).astype(jnp.bfloat16)
    return jnp.dot(hidden, dec_out, preferred_element_type=jnp.float32)


def copy_terms(
    visible_in, positions, targets, w_qkv, w_out, mask_embed, dec_in, conv_w, dec_out, projected
):
    total_rows = targets.shape[0]
    if projected is None:
        branch = attention_branch(visible_in, w_qkv, w_out)
    else:
        branch = attention_from(reuse_rows(visible_in, w_qkv, projected), w_out)
    visible_out = (visible_in.astype(jnp.float32) + branch).astype(jnp.bfloat16)
    predicted = decoder_output(
        visible_out, positions, total_rows, mask_embed, dec_in, conv_w, dec_out
    )
    slot_ids = jnp.arange(total_rows, dtype=jnp.int32)
    seen = jnp.max((slot_ids[:, None] == positions[None, :]).astype(jnp.float32), axis=1)
    mismatch = (predicted - targets.astype(jnp.float32)) * (1.0 - seen)[:, None]
    return jnp.sum(mismatch * mismatch)


def ring_gather(values, group_size):
    parts = [values]
    for shift in range(1, group_size):
        pairs = [(source, (source - shift) % group_size) for source in range(group_size)]
        parts.append(lax.ppermute(values, "mask", pairs))
    return parts


def in_mask_order(parts, own_index):
    group_size = len(parts)
    blocks = []
    for block in range(group_size):
        slot = (block - own_index) % group_size
        chosen = parts[0]
        for other in range(1, group_size):
            chosen = jnp.where(slot == other, parts[other], chosen)
        blocks.append(chosen)
    return jnp.concatenate(blocks, axis=0)


def split_teacher(embedded, w_qkv, w_out, own_index, group_size):
    total_rows = embedded.shape[0]
    head_dim = D // HEADS
    heads_here = HEADS // group_size
    head_width = heads_here * head_dim
    normed = row_norm(embedded.astype(jnp.float32)).astype(jnp.bfloat16)
    own_cols = lax.dynamic_slice_in_dim(
        w_qkv.reshape(D, 3, D), own_index * head_width, head_width, 2
    )
    projected = jnp.einsum(
        "sd,dtw->stw", normed, own_cols, preferred_element_type=jnp.float32
    ).astype(jnp.bfloat16)
    context = split_project(projected.reshape(total_rows, 3, heads_here, head_dim))
    out_rows = lax.dynamic_slice_in_dim(w_out, own_index * head_width, head_width, 0)
    partial_value = jnp.dot(
        context.reshape(total_rows, head_width), out_rows, preferred_element_type=jnp.float32
    )
    return lax.psum(partial_value.astype(jnp.bfloat16), "mask").astype(jnp.float32)


def on_device(patches, visible_index, embed_w, w_qkv, w_out, mask_embed, dec_in, conv_w, dec_out):
    tok_rows = patches.shape[0]
    group_size = lax.axis_size("mask")
    own_index = lax.axis_index("mask")
    copies = visible_index.shape[0]
    visible_count = visible_index.shape[1]
    total_rows = tok_rows * group_size
    col_width = patches.shape[1] // group_size
    positions = lax.dynamic_index_in_dim(visible_index, own_index, 0, keepdims=False)
    clip_pixels = in_mask_order(ring_gather(patches, group_size), own_index)
    embedded = jnp.dot(clip_pixels, embed_w, preferred_element_type=jnp.float32).astype(
        jnp.bfloat16
    )
    visible_in = embedded[positions]
    if HEADS * total_rows * total_rows * 4 <= (1 << 24):
        clip_projected = project_rows(embedded, w_qkv)
        branch = attention_from(clip_projected, w_out)
        visible_projected = clip_projected[positions]
    else:
        branch = split_teacher(embedded, w_qkv, w_out, own_index, group_size)
        visible_projected = None
    all_targets = row_norm(branch).astype(jnp.bfloat16)

    def objective(rows_in):
        return copy_terms(
            rows_in,
            positions,
            all_targets,
            w_qkv,
            w_out,
            mask_embed,
            dec_in,
            conv_w,
            dec_out,
            visible_projected,
        )

    squares, pullback = jax.vjp(objective, visible_in)
    factor = 0.5 / math.sqrt(copies * visible_count)
    (grad_in,) = pullback(jnp.ones_like(squares) * factor)
    copy_loss = jnp.reshape(squares / ((total_rows - visible_count) * D), (1,))
    slot_copy = (own_index + jnp.arange(group_size, dtype=jnp.int32)) % group_size
    flat_index = visible_index[slot_copy].reshape(copies * visible_count)
    own_cols = lax.dynamic_slice_in_dim(clip_pixels, own_index * col_width, col_width, 1)
    gathered = own_cols[flat_index]
    embed_grad = jnp.einsum(
        "vc,vd->cd",
        gathered,
        jnp.concatenate(ring_gather(grad_in, group_size), axis=0),
        preferred_element_type=jnp.float32,
    )
    return (embed_grad, copy_loss)


def solution(mesh):
    placed = (P(("dp", "mask"), None), P("dp", None), P(), P(), P(), P(), P(), P(), P())
    return jax.shard_map(
        on_device,
        mesh=mesh,
        in_specs=placed,
        out_specs=(P(("dp", "mask"), None), P(("dp", "mask"))),
        check_vma=False,
    )
```

```python
import math

import jax
import jax.numpy as jnp
from jax import lax
from jax.sharding import PartitionSpec as P

D = 1024
HEADS = 16
DD = 768
GROUPS = 16


EPSILON = 1e-06


def row_norm(values):
    average = jnp.mean(values, axis=-1, keepdims=True)
    centred = values - average
    spread = jnp.mean(centred * centred, axis=-1, keepdims=True)
    return centred * lax.rsqrt(spread + EPSILON)


def head_norm(values):
    return values * lax.rsqrt(jnp.mean(values * values, axis=-1, keepdims=True) + EPSILON)


def mix_heads(queries, key_rows, values):
    score_scale = 1.0 / math.sqrt(queries.shape[-1])
    scores = (
        jnp.einsum("qhd,khd->hqk", queries, key_rows, preferred_element_type=jnp.float32)
        * score_scale
    )
    exponent = jnp.exp(scores)
    weights = (exponent / jnp.sum(exponent, axis=-1, keepdims=True)).astype(jnp.bfloat16)
    mixed = jnp.einsum("hqk,khd->qhd", weights, values, preferred_element_type=jnp.float32)
    return mixed.astype(jnp.bfloat16)


def split_project(projected):
    queries = head_norm(projected[:, 0].astype(jnp.float32)).astype(jnp.bfloat16)
    key_rows = head_norm(projected[:, 1].astype(jnp.float32)).astype(jnp.bfloat16)
    return mix_heads(queries, key_rows, projected[:, 2])


def project_rows(inputs, w_qkv):
    normed = row_norm(inputs.astype(jnp.float32)).astype(jnp.bfloat16)
    return jnp.dot(normed, w_qkv, preferred_element_type=jnp.float32).astype(jnp.bfloat16)


def attention_from(projected, w_out):
    row_count = projected.shape[0]
    context = split_project(projected.reshape(row_count, 3, HEADS, D // HEADS))
    return jnp.dot(context.reshape(row_count, D), w_out, preferred_element_type=jnp.float32)


def attention_branch(inputs, w_qkv, w_out):
    return attention_from(project_rows(inputs, w_qkv), w_out)


@jax.custom_vjp
def reuse_rows(inputs, w_qkv, projected):
    return projected


def reuse_rows_fwd(inputs, w_qkv, projected):
    return projected, (inputs, w_qkv)


def reuse_rows_bwd(saved, cotangent):
    inputs, w_qkv = saved
    _, pullback = jax.vjp(lambda rows: project_rows(rows, w_qkv), inputs)
    (d_inputs,) = pullback(cotangent)
    return d_inputs, jnp.zeros_like(w_qkv), jnp.zeros_like(cotangent)


reuse_rows.defvjp(reuse_rows_fwd, reuse_rows_bwd)


def decoder_output(visible_out, positions, total_rows, mask_embed, dec_in, conv_w, dec_out):
    slot_ids = jnp.arange(total_rows, dtype=jnp.int32)
    picks = (slot_ids[:, None] == positions[None, :]).astype(jnp.bfloat16)
    seen = jnp.max(picks, axis=1, keepdims=True)
    lowered_visible = jnp.dot(visible_out, dec_in, preferred_element_type=jnp.float32).astype(
        jnp.bfloat16
    )
    lowered_mask = jnp.dot(
        mask_embed[None, :], dec_in, preferred_element_type=jnp.float32
    ).astype(jnp.bfloat16)
    placed = jnp.dot(picks, lowered_visible, preferred_element_type=jnp.float32)
    lowered = jnp.where(seen > 0, placed, lowered_mask.astype(jnp.float32)).astype(jnp.bfloat16)
    grouped = lowered.reshape(total_rows, GROUPS, DD // GROUPS)
    padded = jnp.pad(grouped, ((1, 1), (0, 0), (0, 0)))
    convolved = jnp.zeros((total_rows, GROUPS, DD // GROUPS), jnp.float32)
    for offset in range(3):
        convolved = convolved + jnp.einsum(
            "pgi,gio->pgo",
            padded[offset : offset + total_rows],
            conv_w[offset],
            preferred_element_type=jnp.float32,
        )
    activated = jax.nn.gelu(row_norm(convolved.reshape(total_rows, DD)), approximate=False)
    hidden = (lowered.astype(jnp.float32) + activated).astype(jnp.bfloat16)
    return jnp.dot(hidden, dec_out, preferred_element_type=jnp.float32)


def copy_terms(
    visible_in, positions, targets, w_qkv, w_out, mask_embed, dec_in, conv_w, dec_out, projected
):
    total_rows = targets.shape[0]
    if projected is None:
        branch = attention_branch(visible_in, w_qkv, w_out)
    else:
        branch = attention_from(reuse_rows(visible_in, w_qkv, projected), w_out)
    visible_out = (visible_in.astype(jnp.float32) + branch).astype(jnp.bfloat16)
    predicted = decoder_output(
        visible_out, positions, total_rows, mask_embed, dec_in, conv_w, dec_out
    )
    slot_ids = jnp.arange(total_rows, dtype=jnp.int32)
    seen = jnp.max((slot_ids[:, None] == positions[None, :]).astype(jnp.float32), axis=1)
    mismatch = (predicted - targets.astype(jnp.float32)) * (1.0 - seen)[:, None]
    return jnp.sum(mismatch * mismatch)


def ring_gather(values, group_size):
    parts = [values]
    for shift in range(1, group_size):
        pairs = [(source, (source - shift) % group_size) for source in range(group_size)]
        parts.append(lax.ppermute(values, "mask", pairs))
    return parts


def in_mask_order(parts, own_index):
    group_size = len(parts)
    blocks = []
    for block in range(group_size):
        slot = (block - own_index) % group_size
        chosen = parts[0]
        for other in range(1, group_size):
            chosen = jnp.where(slot == other, parts[other], chosen)
        blocks.append(chosen)
    return jnp.concatenate(blocks, axis=0)


def split_teacher(embedded, w_qkv, w_out, own_index, group_size):
    total_rows = embedded.shape[0]
    head_dim = D // HEADS
    heads_here = HEADS // group_size
    head_width = heads_here * head_dim
    normed = row_norm(embedded.astype(jnp.float32)).astype(jnp.bfloat16)
    own_cols = lax.dynamic_slice_in_dim(
        w_qkv.reshape(D, 3, D), own_index * head_width, head_width, 2
    )
    projected = jnp.einsum(
        "sd,dtw->stw", normed, own_cols, preferred_element_type=jnp.float32
    ).astype(jnp.bfloat16)
    context = split_project(projected.reshape(total_rows, 3, heads_here, head_dim))
    out_rows = lax.dynamic_slice_in_dim(w_out, own_index * head_width, head_width, 0)
    partial_value = jnp.dot(
        context.reshape(total_rows, head_width), out_rows, preferred_element_type=jnp.float32
    )
    return lax.psum(partial_value.astype(jnp.bfloat16), "mask").astype(jnp.float32)


def on_device(patches, visible_index, embed_w, w_qkv, w_out, mask_embed, dec_in, conv_w, dec_out):
    tok_rows = patches.shape[0]
    group_size = lax.axis_size("mask")
    own_index = lax.axis_index("mask")
    copies = visible_index.shape[0]
    visible_count = visible_index.shape[1]
    total_rows = tok_rows * group_size
    col_width = patches.shape[1] // group_size
    positions = lax.dynamic_index_in_dim(visible_index, own_index, 0, keepdims=False)
    clip_pixels = in_mask_order(ring_gather(patches, group_size), own_index)
    embedded = jnp.dot(clip_pixels, embed_w, preferred_element_type=jnp.float32).astype(
        jnp.bfloat16
    )
    clip_ids = jnp.arange(total_rows, dtype=jnp.int32)
    own_picks = (positions[:, None] == clip_ids[None, :]).astype(jnp.bfloat16)
    visible_in = jnp.dot(own_picks, embedded, preferred_element_type=jnp.float32).astype(
        jnp.bfloat16
    )
    if HEADS * total_rows * total_rows * 4 <= (1 << 24):
        clip_projected = project_rows(embedded, w_qkv)
        branch = attention_from(clip_projected, w_out)
        visible_projected = jnp.dot(
            own_picks, clip_projected, preferred_element_type=jnp.float32
        ).astype(jnp.bfloat16)
    else:
        branch = split_teacher(embedded, w_qkv, w_out, own_index, group_size)
        visible_projected = None
    all_targets = row_norm(branch).astype(jnp.bfloat16)

    def objective(rows_in):
        return copy_terms(
            rows_in,
            positions,
            all_targets,
            w_qkv,
            w_out,
            mask_embed,
            dec_in,
            conv_w,
            dec_out,
            visible_projected,
        )

    squares, pullback = jax.vjp(objective, visible_in)
    factor = 0.5 / math.sqrt(copies * visible_count)
    (grad_in,) = pullback(jnp.ones_like(squares) * factor)
    copy_loss = jnp.reshape(squares / ((total_rows - visible_count) * D), (1,))
    slot_copy = (own_index + jnp.arange(group_size, dtype=jnp.int32)) % group_size
    flat_index = visible_index[slot_copy].reshape(copies * visible_count)
    own_cols = lax.dynamic_slice_in_dim(clip_pixels, own_index * col_width, col_width, 1)
    all_picks = (flat_index[:, None] == clip_ids[None, :]).astype(jnp.bfloat16)
    gathered = jnp.dot(all_picks, own_cols, preferred_element_type=jnp.float32).astype(
        jnp.bfloat16
    )
    embed_grad = jnp.einsum(
        "vc,vd->cd",
        gathered,
        jnp.concatenate(ring_gather(grad_in, group_size), axis=0),
        preferred_element_type=jnp.float32,
    )
    return (embed_grad, copy_loss)


def solution(mesh):
    placed = (P(("dp", "mask"), None), P("dp", None), P(), P(), P(), P(), P(), P(), P())
    return jax.shard_map(
        on_device,
        mesh=mesh,
        in_specs=placed,
        out_specs=(P(("dp", "mask"), None), P(("dp", "mask"))),
        check_vma=False,
    )
```

```python
import math

import jax
import jax.numpy as jnp
from jax import lax
from jax.sharding import PartitionSpec as P

D = 1024
HEADS = 16
DD = 768
GROUPS = 16


EPSILON = 1e-06


def row_norm(values):
    average = jnp.mean(values, axis=-1, keepdims=True)
    centred = values - average
    spread = jnp.mean(centred * centred, axis=-1, keepdims=True)
    return centred * lax.rsqrt(spread + EPSILON)


def head_norm(values):
    return values * lax.rsqrt(jnp.mean(values * values, axis=-1, keepdims=True) + EPSILON)


def mix_heads(queries, key_rows, values):
    score_scale = 1.0 / math.sqrt(queries.shape[-1])
    scores = (
        jnp.einsum("qhd,khd->hqk", queries, key_rows, preferred_element_type=jnp.float32)
        * score_scale
    )
    exponent = jnp.exp(scores)
    weights = (exponent / jnp.sum(exponent, axis=-1, keepdims=True)).astype(jnp.bfloat16)
    mixed = jnp.einsum("hqk,khd->qhd", weights, values, preferred_element_type=jnp.float32)
    return mixed.astype(jnp.bfloat16)


def split_project(projected):
    queries = head_norm(projected[:, 0].astype(jnp.float32)).astype(jnp.bfloat16)
    key_rows = head_norm(projected[:, 1].astype(jnp.float32)).astype(jnp.bfloat16)
    return mix_heads(queries, key_rows, projected[:, 2])


def project_rows(inputs, w_qkv):
    normed = row_norm(inputs.astype(jnp.float32)).astype(jnp.bfloat16)
    return jnp.dot(normed, w_qkv, preferred_element_type=jnp.float32).astype(jnp.bfloat16)


def attention_from(projected, w_out):
    row_count = projected.shape[0]
    context = split_project(projected.reshape(row_count, 3, HEADS, D // HEADS))
    return jnp.dot(context.reshape(row_count, D), w_out, preferred_element_type=jnp.float32)


def attention_branch(inputs, w_qkv, w_out):
    return attention_from(project_rows(inputs, w_qkv), w_out)


@jax.custom_vjp
def reuse_rows(inputs, w_qkv, projected):
    return projected


def reuse_rows_fwd(inputs, w_qkv, projected):
    return projected, (inputs, w_qkv)


def reuse_rows_bwd(saved, cotangent):
    inputs, w_qkv = saved
    _, pullback = jax.vjp(lambda rows: project_rows(rows, w_qkv), inputs)
    (d_inputs,) = pullback(cotangent)
    return d_inputs, jnp.zeros_like(w_qkv), jnp.zeros_like(cotangent)


reuse_rows.defvjp(reuse_rows_fwd, reuse_rows_bwd)


def decoder_output(visible_out, positions, total_rows, mask_embed, dec_in, conv_w, dec_out):
    slot_ids = jnp.arange(total_rows, dtype=jnp.int32)
    picks = (slot_ids[:, None] == positions[None, :]).astype(jnp.bfloat16)
    unseen = 1.0 - jnp.max(picks, axis=1, keepdims=True)
    picks = jnp.concatenate([picks, unseen], axis=1)
    distinct_rows = jnp.concatenate([visible_out, mask_embed[None, :]], axis=0)
    lowered_rows = jnp.dot(distinct_rows, dec_in, preferred_element_type=jnp.float32).astype(
        jnp.bfloat16
    )
    lowered = jnp.dot(picks, lowered_rows, preferred_element_type=jnp.float32).astype(
        jnp.bfloat16
    )
    grouped = lowered.reshape(total_rows, GROUPS, DD // GROUPS)
    padded = jnp.pad(grouped, ((1, 1), (0, 0), (0, 0)))
    convolved = jnp.zeros((total_rows, GROUPS, DD // GROUPS), jnp.float32)
    for offset in range(3):
        convolved = convolved + jnp.einsum(
            "pgi,gio->pgo",
            padded[offset : offset + total_rows],
            conv_w[offset],
            preferred_element_type=jnp.float32,
        )
    activated = jax.nn.gelu(row_norm(convolved.reshape(total_rows, DD)), approximate=False)
    hidden = (lowered.astype(jnp.float32) + activated).astype(jnp.bfloat16)
    return jnp.dot(hidden, dec_out, preferred_element_type=jnp.float32)


def copy_terms(
    visible_in, positions, targets, w_qkv, w_out, mask_embed, dec_in, conv_w, dec_out, projected
):
    total_rows = targets.shape[0]
    if projected is None:
        branch = attention_branch(visible_in, w_qkv, w_out)
    else:
        branch = attention_from(reuse_rows(visible_in, w_qkv, projected), w_out)
    visible_out = (visible_in.astype(jnp.float32) + branch).astype(jnp.bfloat16)
    predicted = decoder_output(
        visible_out, positions, total_rows, mask_embed, dec_in, conv_w, dec_out
    )
    slot_ids = jnp.arange(total_rows, dtype=jnp.int32)
    seen = jnp.max((slot_ids[:, None] == positions[None, :]).astype(jnp.float32), axis=1)
    mismatch = (predicted - targets.astype(jnp.float32)) * (1.0 - seen)[:, None]
    return jnp.sum(mismatch * mismatch)


def ring_gather(values, group_size):
    parts = [values]
    for shift in range(1, group_size):
        pairs = [(source, (source - shift) % group_size) for source in range(group_size)]
        parts.append(lax.ppermute(values, "mask", pairs))
    return parts


def in_mask_order(parts, own_index):
    group_size = len(parts)
    blocks = []
    for block in range(group_size):
        slot = (block - own_index) % group_size
        chosen = parts[0]
        for other in range(1, group_size):
            chosen = jnp.where(slot == other, parts[other], chosen)
        blocks.append(chosen)
    return jnp.concatenate(blocks, axis=0)


def split_teacher(embedded, w_qkv, w_out, own_index, group_size):
    total_rows = embedded.shape[0]
    head_dim = D // HEADS
    heads_here = HEADS // group_size
    head_width = heads_here * head_dim
    normed = row_norm(embedded.astype(jnp.float32)).astype(jnp.bfloat16)
    own_cols = lax.dynamic_slice_in_dim(
        w_qkv.reshape(D, 3, D), own_index * head_width, head_width, 2
    )
    projected = jnp.einsum(
        "sd,dtw->stw", normed, own_cols, preferred_element_type=jnp.float32
    ).astype(jnp.bfloat16)
    context = split_project(projected.reshape(total_rows, 3, heads_here, head_dim))
    out_rows = lax.dynamic_slice_in_dim(w_out, own_index * head_width, head_width, 0)
    partial_value = jnp.dot(
        context.reshape(total_rows, head_width), out_rows, preferred_element_type=jnp.float32
    )
    return lax.psum(partial_value.astype(jnp.bfloat16), "mask").astype(jnp.float32)


def on_device(patches, visible_index, embed_w, w_qkv, w_out, mask_embed, dec_in, conv_w, dec_out):
    tok_rows = patches.shape[0]
    group_size = lax.axis_size("mask")
    own_index = lax.axis_index("mask")
    copies = visible_index.shape[0]
    visible_count = visible_index.shape[1]
    total_rows = tok_rows * group_size
    col_width = patches.shape[1] // group_size
    positions = lax.dynamic_index_in_dim(visible_index, own_index, 0, keepdims=False)
    clip_pixels = in_mask_order(ring_gather(patches, group_size), own_index)
    embedded = jnp.dot(clip_pixels, embed_w, preferred_element_type=jnp.float32).astype(
        jnp.bfloat16
    )
    clip_ids = jnp.arange(total_rows, dtype=jnp.int32)
    own_picks = (positions[:, None] == clip_ids[None, :]).astype(jnp.bfloat16)
    visible_in = jnp.dot(own_picks, embedded, preferred_element_type=jnp.float32).astype(
        jnp.bfloat16
    )
    if HEADS * total_rows * total_rows * 4 <= (1 << 24):
        clip_projected = project_rows(embedded, w_qkv)
        branch = attention_from(clip_projected, w_out)
        visible_projected = jnp.dot(
            own_picks, clip_projected, preferred_element_type=jnp.float32
        ).astype(jnp.bfloat16)
    else:
        branch = split_teacher(embedded, w_qkv, w_out, own_index, group_size)
        visible_projected = None
    all_targets = row_norm(branch).astype(jnp.bfloat16)

    def objective(rows_in):
        return copy_terms(
            rows_in,
            positions,
            all_targets,
            w_qkv,
            w_out,
            mask_embed,
            dec_in,
            conv_w,
            dec_out,
            visible_projected,
        )

    squares, pullback = jax.vjp(objective, visible_in)
    factor = 0.5 / math.sqrt(copies * visible_count)
    (grad_in,) = pullback(jnp.ones_like(squares) * factor)
    copy_loss = jnp.reshape(squares / ((total_rows - visible_count) * D), (1,))
    slot_copy = (own_index + jnp.arange(group_size, dtype=jnp.int32)) % group_size
    slot_rows = []
    for slot in range(group_size):
        chosen = visible_index[0]
        for copy_id in range(1, copies):
            chosen = jnp.where(slot_copy[slot] == copy_id, visible_index[copy_id], chosen)
        slot_rows.append(chosen)
    flat_index = jnp.concatenate(slot_rows, axis=0)
    own_cols = lax.dynamic_slice_in_dim(clip_pixels, own_index * col_width, col_width, 1)
    all_picks = (flat_index[:, None] == clip_ids[None, :]).astype(jnp.bfloat16)
    gathered = jnp.dot(all_picks, own_cols, preferred_element_type=jnp.float32).astype(
        jnp.bfloat16
    )
    embed_grad = jnp.einsum(
        "vc,vd->cd",
        gathered,
        jnp.concatenate(ring_gather(grad_in, group_size), axis=0),
        preferred_element_type=jnp.float32,
    )
    return (embed_grad, copy_loss)


def solution(mesh):
    placed = (P(("dp", "mask"), None), P("dp", None), P(), P(), P(), P(), P(), P(), P())
    return jax.shard_map(
        on_device,
        mesh=mesh,
        in_specs=placed,
        out_specs=(P(("dp", "mask"), None), P(("dp", "mask"))),
        check_vma=False,
    )
```

```python
import math

import jax
import jax.numpy as jnp
from jax import lax
from jax.sharding import PartitionSpec as P

D = 1024
HEADS = 16
DD = 768
GROUPS = 16


EPSILON = 1e-06


def row_norm(values):
    average = jnp.mean(values, axis=-1, keepdims=True)
    centred = values - average
    spread = jnp.mean(centred * centred, axis=-1, keepdims=True)
    return centred * lax.rsqrt(spread + EPSILON)


def head_norm(values):
    return values * lax.rsqrt(jnp.mean(values * values, axis=-1, keepdims=True) + EPSILON)


def mix_heads(queries, key_rows, values):
    score_scale = 1.0 / math.sqrt(queries.shape[-1])
    scores = (
        jnp.einsum("qhd,khd->hqk", queries, key_rows, preferred_element_type=jnp.float32)
        * score_scale
    )
    exponent = jnp.exp(scores)
    weights = (exponent / jnp.sum(exponent, axis=-1, keepdims=True)).astype(jnp.bfloat16)
    mixed = jnp.einsum("hqk,khd->qhd", weights, values, preferred_element_type=jnp.float32)
    return mixed.astype(jnp.bfloat16)


def split_project(projected):
    queries = head_norm(projected[:, 0].astype(jnp.float32)).astype(jnp.bfloat16)
    key_rows = head_norm(projected[:, 1].astype(jnp.float32)).astype(jnp.bfloat16)
    return mix_heads(queries, key_rows, projected[:, 2])


def project_rows(inputs, w_qkv):
    normed = row_norm(inputs.astype(jnp.float32)).astype(jnp.bfloat16)
    return jnp.dot(normed, w_qkv, preferred_element_type=jnp.float32).astype(jnp.bfloat16)


def attention_from(projected, w_out):
    row_count = projected.shape[0]
    context = split_project(projected.reshape(row_count, 3, HEADS, D // HEADS))
    return jnp.dot(context.reshape(row_count, D), w_out, preferred_element_type=jnp.float32)


def attention_branch(inputs, w_qkv, w_out):
    return attention_from(project_rows(inputs, w_qkv), w_out)


@jax.custom_vjp
def reuse_rows(inputs, w_qkv, projected):
    return projected


def reuse_rows_fwd(inputs, w_qkv, projected):
    return projected, (inputs, w_qkv)


def reuse_rows_bwd(saved, cotangent):
    inputs, w_qkv = saved
    _, pullback = jax.vjp(lambda rows: project_rows(rows, w_qkv), inputs)
    (d_inputs,) = pullback(cotangent)
    return d_inputs, jnp.zeros_like(w_qkv), jnp.zeros_like(cotangent)


reuse_rows.defvjp(reuse_rows_fwd, reuse_rows_bwd)


def decoder_output(visible_out, positions, total_rows, mask_embed, dec_in, conv_w, dec_out):
    slot_ids = jnp.arange(total_rows, dtype=jnp.int32)
    picks = (slot_ids[:, None] == positions[None, :]).astype(jnp.bfloat16)
    seen = jnp.max(picks, axis=1, keepdims=True)
    lowered_visible = jnp.dot(visible_out, dec_in, preferred_element_type=jnp.float32).astype(
        jnp.bfloat16
    )
    lowered_mask = jnp.dot(
        mask_embed[None, :], dec_in, preferred_element_type=jnp.float32
    ).astype(jnp.bfloat16)
    placed = jnp.dot(picks, lowered_visible, preferred_element_type=jnp.float32)
    lowered = jnp.where(seen > 0, placed, lowered_mask.astype(jnp.float32)).astype(jnp.bfloat16)
    grouped = lowered.reshape(total_rows, GROUPS, DD // GROUPS)
    padded = jnp.pad(grouped, ((1, 1), (0, 0), (0, 0)))
    convolved = jnp.zeros((total_rows, GROUPS, DD // GROUPS), jnp.float32)
    for offset in range(3):
        convolved = convolved + jnp.einsum(
            "pgi,gio->pgo",
            padded[offset : offset + total_rows],
            conv_w[offset],
            preferred_element_type=jnp.float32,
        )
    activated = jax.nn.gelu(row_norm(convolved.reshape(total_rows, DD)), approximate=False)
    hidden = (lowered.astype(jnp.float32) + activated).astype(jnp.bfloat16)
    return jnp.dot(hidden, dec_out, preferred_element_type=jnp.float32)


def copy_terms(
    visible_in, positions, targets, w_qkv, w_out, mask_embed, dec_in, conv_w, dec_out, projected
):
    total_rows = targets.shape[0]
    if projected is None:
        branch = attention_branch(visible_in, w_qkv, w_out)
    else:
        branch = attention_from(reuse_rows(visible_in, w_qkv, projected), w_out)
    visible_out = (visible_in.astype(jnp.float32) + branch).astype(jnp.bfloat16)
    predicted = decoder_output(
        visible_out, positions, total_rows, mask_embed, dec_in, conv_w, dec_out
    )
    slot_ids = jnp.arange(total_rows, dtype=jnp.int32)
    seen = jnp.max((slot_ids[:, None] == positions[None, :]).astype(jnp.float32), axis=1)
    mismatch = (predicted - targets.astype(jnp.float32)) * (1.0 - seen)[:, None]
    return jnp.sum(mismatch * mismatch)


def ring_gather(values, group_size):
    parts = [values]
    for shift in range(1, group_size):
        pairs = [(source, (source - shift) % group_size) for source in range(group_size)]
        parts.append(lax.ppermute(values, "mask", pairs))
    return parts


def in_mask_order(parts, own_index):
    group_size = len(parts)
    blocks = []
    for block in range(group_size):
        slot = (block - own_index) % group_size
        chosen = parts[0]
        for other in range(1, group_size):
            chosen = jnp.where(slot == other, parts[other], chosen)
        blocks.append(chosen)
    return jnp.concatenate(blocks, axis=0)


def split_teacher(embedded, w_qkv, w_out, own_index, group_size):
    total_rows = embedded.shape[0]
    head_dim = D // HEADS
    heads_here = HEADS // group_size
    head_width = heads_here * head_dim
    normed = row_norm(embedded.astype(jnp.float32)).astype(jnp.bfloat16)
    own_cols = lax.dynamic_slice_in_dim(
        w_qkv.reshape(D, 3, D), own_index * head_width, head_width, 2
    )
    projected = jnp.einsum(
        "sd,dtw->stw", normed, own_cols, preferred_element_type=jnp.float32
    ).astype(jnp.bfloat16)
    context = split_project(projected.reshape(total_rows, 3, heads_here, head_dim))
    out_rows = lax.dynamic_slice_in_dim(w_out, own_index * head_width, head_width, 0)
    partial_value = jnp.dot(
        context.reshape(total_rows, head_width), out_rows, preferred_element_type=jnp.float32
    )
    return lax.psum(partial_value.astype(jnp.bfloat16), "mask").astype(jnp.float32)


def on_device(patches, visible_index, embed_w, w_qkv, w_out, mask_embed, dec_in, conv_w, dec_out):
    tok_rows = patches.shape[0]
    group_size = lax.axis_size("mask")
    own_index = lax.axis_index("mask")
    copies = visible_index.shape[0]
    visible_count = visible_index.shape[1]
    total_rows = tok_rows * group_size
    col_width = patches.shape[1] // group_size
    positions = lax.dynamic_index_in_dim(visible_index, own_index, 0, keepdims=False)
    clip_pixels = in_mask_order(ring_gather(patches, group_size), own_index)
    embedded = jnp.dot(clip_pixels, embed_w, preferred_element_type=jnp.float32).astype(
        jnp.bfloat16
    )
    clip_ids = jnp.arange(total_rows, dtype=jnp.int32)
    own_picks = (positions[:, None] == clip_ids[None, :]).astype(jnp.bfloat16)
    visible_in = jnp.dot(own_picks, embedded, preferred_element_type=jnp.float32).astype(
        jnp.bfloat16
    )
    if HEADS * total_rows * total_rows * 4 <= (1 << 24):
        clip_projected = project_rows(embedded, w_qkv)
        branch = attention_from(clip_projected, w_out)
        visible_projected = jnp.dot(
            own_picks, clip_projected, preferred_element_type=jnp.float32
        ).astype(jnp.bfloat16)
    else:
        branch = split_teacher(embedded, w_qkv, w_out, own_index, group_size)
        visible_projected = None
    all_targets = row_norm(branch).astype(jnp.bfloat16)

    def objective(rows_in):
        return copy_terms(
            rows_in,
            positions,
            all_targets,
            w_qkv,
            w_out,
            mask_embed,
            dec_in,
            conv_w,
            dec_out,
            visible_projected,
        )

    squares, pullback = jax.vjp(objective, visible_in)
    factor = 0.5 / math.sqrt(copies * visible_count)
    (grad_in,) = pullback(jnp.ones_like(squares) * factor)
    copy_loss = jnp.reshape(squares / ((total_rows - visible_count) * D), (1,))
    slot_copy = (own_index + jnp.arange(group_size, dtype=jnp.int32)) % group_size
    slot_rows = []
    for slot in range(group_size):
        chosen = visible_index[0]
        for copy_id in range(1, copies):
            chosen = jnp.where(slot_copy[slot] == copy_id, visible_index[copy_id], chosen)
        slot_rows.append(chosen)
    flat_index = jnp.concatenate(slot_rows, axis=0)
    own_cols = lax.dynamic_slice_in_dim(clip_pixels, own_index * col_width, col_width, 1)
    all_picks = (flat_index[:, None] == clip_ids[None, :]).astype(jnp.bfloat16)
    gathered = jnp.dot(all_picks, own_cols, preferred_element_type=jnp.float32).astype(
        jnp.bfloat16
    )
    embed_grad = jnp.einsum(
        "vc,vd->cd",
        gathered,
        jnp.concatenate(ring_gather(grad_in, group_size), axis=0),
        preferred_element_type=jnp.float32,
    )
    return (embed_grad, copy_loss)


def solution(mesh):
    placed = (P(("dp", "mask"), None), P("dp", None), P(), P(), P(), P(), P(), P(), P())
    return jax.shard_map(
        on_device,
        mesh=mesh,
        in_specs=placed,
        out_specs=(P(("dp", "mask"), None), P(("dp", "mask"))),
        check_vma=False,
    )
```

```python
import math

import jax
import jax.numpy as jnp
from jax import lax
from jax.sharding import PartitionSpec as P

D = 1024
HEADS = 16
DD = 768
GROUPS = 16


EPSILON = 1e-06


def row_norm(values):
    average = jnp.mean(values, axis=-1, keepdims=True)
    centred = values - average
    spread = jnp.mean(centred * centred, axis=-1, keepdims=True)
    return centred * lax.rsqrt(spread + EPSILON)


def head_norm(values):
    return values * lax.rsqrt(jnp.mean(values * values, axis=-1, keepdims=True) + EPSILON)


def mix_heads(queries, key_rows, values):
    score_scale = 1.0 / math.sqrt(queries.shape[-1])
    scores = (
        jnp.einsum("qhd,khd->hqk", queries, key_rows, preferred_element_type=jnp.float32)
        * score_scale
    )
    exponent = jnp.exp(scores)
    weights = (exponent / jnp.sum(exponent, axis=-1, keepdims=True)).astype(jnp.bfloat16)
    mixed = jnp.einsum("hqk,khd->qhd", weights, values, preferred_element_type=jnp.float32)
    return mixed.astype(jnp.bfloat16)


def split_project(projected):
    queries = head_norm(projected[:, 0].astype(jnp.float32)).astype(jnp.bfloat16)
    key_rows = head_norm(projected[:, 1].astype(jnp.float32)).astype(jnp.bfloat16)
    return mix_heads(queries, key_rows, projected[:, 2])


def project_rows(inputs, w_qkv):
    normed = row_norm(inputs.astype(jnp.float32)).astype(jnp.bfloat16)
    return jnp.dot(normed, w_qkv, preferred_element_type=jnp.float32).astype(jnp.bfloat16)


def attention_from(projected, w_out):
    row_count = projected.shape[0]
    context = split_project(projected.reshape(row_count, 3, HEADS, D // HEADS))
    return jnp.dot(context.reshape(row_count, D), w_out, preferred_element_type=jnp.float32)


def attention_branch(inputs, w_qkv, w_out):
    return attention_from(project_rows(inputs, w_qkv), w_out)


@jax.custom_vjp
def reuse_rows(inputs, w_qkv, projected):
    return projected


def reuse_rows_fwd(inputs, w_qkv, projected):
    return projected, (inputs, w_qkv)


def reuse_rows_bwd(saved, cotangent):
    inputs, w_qkv = saved
    _, pullback = jax.vjp(
        lambda rows: row_norm(rows.astype(jnp.float32)).astype(jnp.bfloat16), inputs
    )
    d_normed = jnp.dot(w_qkv, cotangent.T, preferred_element_type=jnp.float32).T
    (d_inputs,) = pullback(d_normed.astype(jnp.bfloat16))
    return d_inputs, jnp.zeros_like(w_qkv), jnp.zeros_like(cotangent)


reuse_rows.defvjp(reuse_rows_fwd, reuse_rows_bwd)


def decoder_output(visible_out, positions, total_rows, mask_embed, dec_in, conv_w, dec_out):
    slot_ids = jnp.arange(total_rows, dtype=jnp.int32)
    picks = (slot_ids[:, None] == positions[None, :]).astype(jnp.bfloat16)
    seen = jnp.max(picks, axis=1, keepdims=True)
    lowered_visible = jnp.dot(visible_out, dec_in, preferred_element_type=jnp.float32).astype(
        jnp.bfloat16
    )
    lowered_mask = jnp.dot(
        mask_embed[None, :], dec_in, preferred_element_type=jnp.float32
    ).astype(jnp.bfloat16)
    placed = jnp.dot(picks, lowered_visible, preferred_element_type=jnp.float32)
    lowered = jnp.where(seen > 0, placed, lowered_mask.astype(jnp.float32)).astype(jnp.bfloat16)
    grouped = lowered.reshape(total_rows, GROUPS, DD // GROUPS)
    padded = jnp.pad(grouped, ((1, 1), (0, 0), (0, 0)))
    convolved = jnp.zeros((total_rows, GROUPS, DD // GROUPS), jnp.float32)
    for offset in range(3):
        convolved = convolved + jnp.einsum(
            "pgi,gio->pgo",
            padded[offset : offset + total_rows],
            conv_w[offset],
            preferred_element_type=jnp.float32,
        )
    activated = jax.nn.gelu(row_norm(convolved.reshape(total_rows, DD)), approximate=False)
    hidden = (lowered.astype(jnp.float32) + activated).astype(jnp.bfloat16)
    return jnp.dot(hidden, dec_out, preferred_element_type=jnp.float32)


def copy_terms(
    visible_in, positions, targets, w_qkv, w_out, mask_embed, dec_in, conv_w, dec_out, projected
):
    total_rows = targets.shape[0]
    if projected is None:
        branch = attention_branch(visible_in, w_qkv, w_out)
    else:
        branch = attention_from(reuse_rows(visible_in, w_qkv, projected), w_out)
    visible_out = (visible_in.astype(jnp.float32) + branch).astype(jnp.bfloat16)
    predicted = decoder_output(
        visible_out, positions, total_rows, mask_embed, dec_in, conv_w, dec_out
    )
    slot_ids = jnp.arange(total_rows, dtype=jnp.int32)
    seen = jnp.max((slot_ids[:, None] == positions[None, :]).astype(jnp.float32), axis=1)
    mismatch = (predicted - targets.astype(jnp.float32)) * (1.0 - seen)[:, None]
    return jnp.sum(mismatch * mismatch)


def ring_gather(values, group_size):
    parts = [values]
    for shift in range(1, group_size):
        pairs = [(source, (source - shift) % group_size) for source in range(group_size)]
        parts.append(lax.ppermute(values, "mask", pairs))
    return parts


def in_mask_order(parts, own_index):
    group_size = len(parts)
    blocks = []
    for block in range(group_size):
        slot = (block - own_index) % group_size
        chosen = parts[0]
        for other in range(1, group_size):
            chosen = jnp.where(slot == other, parts[other], chosen)
        blocks.append(chosen)
    return jnp.concatenate(blocks, axis=0)


def split_teacher(embedded, w_qkv, w_out, own_index, group_size):
    total_rows = embedded.shape[0]
    head_dim = D // HEADS
    heads_here = HEADS // group_size
    head_width = heads_here * head_dim
    normed = row_norm(embedded.astype(jnp.float32)).astype(jnp.bfloat16)
    own_cols = lax.dynamic_slice_in_dim(
        w_qkv.reshape(D, 3, D), own_index * head_width, head_width, 2
    )
    projected = jnp.einsum(
        "sd,dtw->stw", normed, own_cols, preferred_element_type=jnp.float32
    ).astype(jnp.bfloat16)
    context = split_project(projected.reshape(total_rows, 3, heads_here, head_dim))
    out_rows = lax.dynamic_slice_in_dim(w_out, own_index * head_width, head_width, 0)
    partial_value = jnp.dot(
        context.reshape(total_rows, head_width), out_rows, preferred_element_type=jnp.float32
    )
    return lax.psum(partial_value.astype(jnp.bfloat16), "mask").astype(jnp.float32)


def on_device(patches, visible_index, embed_w, w_qkv, w_out, mask_embed, dec_in, conv_w, dec_out):
    tok_rows = patches.shape[0]
    group_size = lax.axis_size("mask")
    own_index = lax.axis_index("mask")
    copies = visible_index.shape[0]
    visible_count = visible_index.shape[1]
    total_rows = tok_rows * group_size
    col_width = patches.shape[1] // group_size
    positions = lax.dynamic_index_in_dim(visible_index, own_index, 0, keepdims=False)
    clip_pixels = in_mask_order(ring_gather(patches, group_size), own_index)
    embedded = jnp.dot(clip_pixels, embed_w, preferred_element_type=jnp.float32).astype(
        jnp.bfloat16
    )
    clip_ids = jnp.arange(total_rows, dtype=jnp.int32)
    own_picks = (positions[:, None] == clip_ids[None, :]).astype(jnp.bfloat16)
    visible_in = jnp.dot(own_picks, embedded, preferred_element_type=jnp.float32).astype(
        jnp.bfloat16
    )
    if HEADS * total_rows * total_rows * 4 <= (1 << 24):
        clip_projected = project_rows(embedded, w_qkv)
        branch = attention_from(clip_projected, w_out)
        visible_projected = jnp.dot(
            own_picks, clip_projected, preferred_element_type=jnp.float32
        ).astype(jnp.bfloat16)
    else:
        branch = split_teacher(embedded, w_qkv, w_out, own_index, group_size)
        visible_projected = None
    all_targets = row_norm(branch).astype(jnp.bfloat16)

    def objective(rows_in):
        return copy_terms(
            rows_in,
            positions,
            all_targets,
            w_qkv,
            w_out,
            mask_embed,
            dec_in,
            conv_w,
            dec_out,
            visible_projected,
        )

    squares, pullback = jax.vjp(objective, visible_in)
    factor = 0.5 / math.sqrt(copies * visible_count)
    (grad_in,) = pullback(jnp.ones_like(squares) * factor)
    copy_loss = jnp.reshape(squares / ((total_rows - visible_count) * D), (1,))
    slot_copy = (own_index + jnp.arange(group_size, dtype=jnp.int32)) % group_size
    flat_index = visible_index[slot_copy].reshape(copies * visible_count)
    own_cols = lax.dynamic_slice_in_dim(clip_pixels, own_index * col_width, col_width, 1)
    all_picks = (flat_index[:, None] == clip_ids[None, :]).astype(jnp.bfloat16)
    gathered = jnp.dot(all_picks, own_cols, preferred_element_type=jnp.float32).astype(
        jnp.bfloat16
    )
    embed_grad = jnp.einsum(
        "vc,vd->cd",
        gathered,
        jnp.concatenate(ring_gather(grad_in, group_size), axis=0),
        preferred_element_type=jnp.float32,
    )
    return (embed_grad, copy_loss)


def solution(mesh):
    placed = (P(("dp", "mask"), None), P("dp", None), P(), P(), P(), P(), P(), P(), P())
    return jax.shard_map(
        on_device,
        mesh=mesh,
        in_specs=placed,
        out_specs=(P(("dp", "mask"), None), P(("dp", "mask"))),
        check_vma=False,
    )
```

```python
import math

import jax
import jax.numpy as jnp
from jax import lax
from jax.sharding import PartitionSpec as P

D = 1024
HEADS = 16
DD = 768
GROUPS = 16


EPSILON = 1e-06


def row_norm(values):
    average = jnp.mean(values, axis=-1, keepdims=True)
    centred = values - average
    spread = jnp.mean(centred * centred, axis=-1, keepdims=True)
    return centred * lax.rsqrt(spread + EPSILON)


def head_norm(values):
    return values * lax.rsqrt(jnp.mean(values * values, axis=-1, keepdims=True) + EPSILON)


def mix_heads(queries, key_rows, values):
    score_scale = 1.0 / math.sqrt(queries.shape[-1])
    scores = (
        jnp.einsum("qhd,khd->hqk", queries, key_rows, preferred_element_type=jnp.float32)
        * score_scale
    )
    exponent = jnp.exp(scores)
    weights = (exponent / jnp.sum(exponent, axis=-1, keepdims=True)).astype(jnp.bfloat16)
    mixed = jnp.einsum("hqk,khd->qhd", weights, values, preferred_element_type=jnp.float32)
    return mixed.astype(jnp.bfloat16)


def split_project(projected):
    queries = head_norm(projected[:, 0].astype(jnp.float32)).astype(jnp.bfloat16)
    key_rows = head_norm(projected[:, 1].astype(jnp.float32)).astype(jnp.bfloat16)
    return mix_heads(queries, key_rows, projected[:, 2])


def project_rows(inputs, w_qkv):
    normed = row_norm(inputs.astype(jnp.float32)).astype(jnp.bfloat16)
    return jnp.dot(normed, w_qkv, preferred_element_type=jnp.float32).astype(jnp.bfloat16)


def attention_from(projected, w_out):
    row_count = projected.shape[0]
    context = split_project(projected.reshape(row_count, 3, HEADS, D // HEADS))
    return jnp.dot(context.reshape(row_count, D), w_out, preferred_element_type=jnp.float32)


def attention_branch(inputs, w_qkv, w_out):
    return attention_from(project_rows(inputs, w_qkv), w_out)


def teacher_branch(embedded, w_qkv, w_out):
    row_count = embedded.shape[0]
    head_dim = D // HEADS
    normed = row_norm(embedded.astype(jnp.float32)).astype(jnp.bfloat16)
    projected_t = jnp.einsum(
        "sd,dk->ks", normed, w_qkv, preferred_element_type=jnp.float32
    ).astype(jnp.bfloat16)
    heads = projected_t.reshape(3, HEADS, head_dim, row_count)
    queries = head_norm_cols(heads[0].astype(jnp.float32)).astype(jnp.bfloat16)
    key_rows = head_norm_cols(heads[1].astype(jnp.float32)).astype(jnp.bfloat16)
    score_scale = 1.0 / math.sqrt(head_dim)
    scores = (
        jnp.einsum("hdq,hdk->hqk", queries, key_rows, preferred_element_type=jnp.float32)
        * score_scale
    )
    exponent = jnp.exp(scores)
    weights = (exponent / jnp.sum(exponent, axis=-1, keepdims=True)).astype(jnp.bfloat16)
    context = jnp.einsum(
        "hqk,hdk->qhd", weights, heads[2], preferred_element_type=jnp.float32
    ).astype(jnp.bfloat16)
    branch = jnp.dot(context.reshape(row_count, D), w_out, preferred_element_type=jnp.float32)
    return projected_t, branch


def head_norm_cols(values):
    return values * lax.rsqrt(jnp.mean(values * values, axis=-2, keepdims=True) + EPSILON)


@jax.custom_vjp
def reuse_rows(inputs, w_qkv, projected):
    return projected


def reuse_rows_fwd(inputs, w_qkv, projected):
    return projected, (inputs, w_qkv)


def reuse_rows_bwd(saved, cotangent):
    inputs, w_qkv = saved
    _, pullback = jax.vjp(lambda rows: project_rows(rows, w_qkv), inputs)
    (d_inputs,) = pullback(cotangent)
    return d_inputs, jnp.zeros_like(w_qkv), jnp.zeros_like(cotangent)


reuse_rows.defvjp(reuse_rows_fwd, reuse_rows_bwd)


def decoder_output(visible_out, positions, total_rows, mask_embed, dec_in, conv_w, dec_out):
    slot_ids = jnp.arange(total_rows, dtype=jnp.int32)
    picks = (slot_ids[:, None] == positions[None, :]).astype(jnp.bfloat16)
    seen = jnp.max(picks, axis=1, keepdims=True)
    lowered_visible = jnp.dot(visible_out, dec_in, preferred_element_type=jnp.float32).astype(
        jnp.bfloat16
    )
    lowered_mask = jnp.dot(
        mask_embed[None, :], dec_in, preferred_element_type=jnp.float32
    ).astype(jnp.bfloat16)
    placed = jnp.dot(picks, lowered_visible, preferred_element_type=jnp.float32)
    lowered = jnp.where(seen > 0, placed, lowered_mask.astype(jnp.float32)).astype(jnp.bfloat16)
    grouped = lowered.reshape(total_rows, GROUPS, DD // GROUPS)
    padded = jnp.pad(grouped, ((1, 1), (0, 0), (0, 0)))
    convolved = jnp.zeros((total_rows, GROUPS, DD // GROUPS), jnp.float32)
    for offset in range(3):
        convolved = convolved + jnp.einsum(
            "pgi,gio->pgo",
            padded[offset : offset + total_rows],
            conv_w[offset],
            preferred_element_type=jnp.float32,
        )
    activated = jax.nn.gelu(row_norm(convolved.reshape(total_rows, DD)), approximate=False)
    hidden = (lowered.astype(jnp.float32) + activated).astype(jnp.bfloat16)
    return jnp.dot(hidden, dec_out, preferred_element_type=jnp.float32)


def copy_terms(
    visible_in, positions, targets, w_qkv, w_out, mask_embed, dec_in, conv_w, dec_out, projected
):
    total_rows = targets.shape[0]
    if projected is None:
        branch = attention_branch(visible_in, w_qkv, w_out)
    else:
        branch = attention_from(reuse_rows(visible_in, w_qkv, projected), w_out)
    visible_out = (visible_in.astype(jnp.float32) + branch).astype(jnp.bfloat16)
    predicted = decoder_output(
        visible_out, positions, total_rows, mask_embed, dec_in, conv_w, dec_out
    )
    slot_ids = jnp.arange(total_rows, dtype=jnp.int32)
    seen = jnp.max((slot_ids[:, None] == positions[None, :]).astype(jnp.float32), axis=1)
    mismatch = (predicted - targets.astype(jnp.float32)) * (1.0 - seen)[:, None]
    return jnp.sum(mismatch * mismatch)


def ring_gather(values, group_size):
    parts = [values]
    for shift in range(1, group_size):
        pairs = [(source, (source - shift) % group_size) for source in range(group_size)]
        parts.append(lax.ppermute(values, "mask", pairs))
    return parts


def in_mask_order(parts, own_index):
    group_size = len(parts)
    blocks = []
    for block in range(group_size):
        slot = (block - own_index) % group_size
        chosen = parts[0]
        for other in range(1, group_size):
            chosen = jnp.where(slot == other, parts[other], chosen)
        blocks.append(chosen)
    return jnp.concatenate(blocks, axis=0)


def split_teacher(embedded, w_qkv, w_out, own_index, group_size):
    total_rows = embedded.shape[0]
    head_dim = D // HEADS
    heads_here = HEADS // group_size
    head_width = heads_here * head_dim
    normed = row_norm(embedded.astype(jnp.float32)).astype(jnp.bfloat16)
    own_cols = lax.dynamic_slice_in_dim(
        w_qkv.reshape(D, 3, D), own_index * head_width, head_width, 2
    )
    projected = jnp.einsum(
        "sd,dtw->stw", normed, own_cols, preferred_element_type=jnp.float32
    ).astype(jnp.bfloat16)
    context = split_project(projected.reshape(total_rows, 3, heads_here, head_dim))
    out_rows = lax.dynamic_slice_in_dim(w_out, own_index * head_width, head_width, 0)
    partial_value = jnp.dot(
        context.reshape(total_rows, head_width), out_rows, preferred_element_type=jnp.float32
    )
    return lax.psum(partial_value.astype(jnp.bfloat16), "mask").astype(jnp.float32)


def on_device(patches, visible_index, embed_w, w_qkv, w_out, mask_embed, dec_in, conv_w, dec_out):
    tok_rows = patches.shape[0]
    group_size = lax.axis_size("mask")
    own_index = lax.axis_index("mask")
    copies = visible_index.shape[0]
    visible_count = visible_index.shape[1]
    total_rows = tok_rows * group_size
    col_width = patches.shape[1] // group_size
    positions = lax.dynamic_index_in_dim(visible_index, own_index, 0, keepdims=False)
    clip_pixels = in_mask_order(ring_gather(patches, group_size), own_index)
    embedded = jnp.dot(clip_pixels, embed_w, preferred_element_type=jnp.float32).astype(
        jnp.bfloat16
    )
    clip_ids = jnp.arange(total_rows, dtype=jnp.int32)
    own_picks = (positions[:, None] == clip_ids[None, :]).astype(jnp.bfloat16)
    visible_in = jnp.dot(own_picks, embedded, preferred_element_type=jnp.float32).astype(
        jnp.bfloat16
    )
    if HEADS * total_rows * total_rows * 4 <= (1 << 24):
        projected_t, branch = teacher_branch(embedded, w_qkv, w_out)
        visible_projected = jnp.einsum(
            "vs,ks->vk", own_picks, projected_t, preferred_element_type=jnp.float32
        ).astype(jnp.bfloat16)
    else:
        branch = split_teacher(embedded, w_qkv, w_out, own_index, group_size)
        visible_projected = None
    all_targets = row_norm(branch).astype(jnp.bfloat16)

    def objective(rows_in):
        return copy_terms(
            rows_in,
            positions,
            all_targets,
            w_qkv,
            w_out,
            mask_embed,
            dec_in,
            conv_w,
            dec_out,
            visible_projected,
        )

    squares, pullback = jax.vjp(objective, visible_in)
    factor = 0.5 / math.sqrt(copies * visible_count)
    (grad_in,) = pullback(jnp.ones_like(squares) * factor)
    copy_loss = jnp.reshape(squares / ((total_rows - visible_count) * D), (1,))
    slot_copy = (own_index + jnp.arange(group_size, dtype=jnp.int32)) % group_size
    flat_index = visible_index[slot_copy].reshape(copies * visible_count)
    own_cols = lax.dynamic_slice_in_dim(clip_pixels, own_index * col_width, col_width, 1)
    all_picks = (flat_index[:, None] == clip_ids[None, :]).astype(jnp.bfloat16)
    gathered = jnp.dot(all_picks, own_cols, preferred_element_type=jnp.float32).astype(
        jnp.bfloat16
    )
    embed_grad = jnp.einsum(
        "vc,vd->cd",
        gathered,
        jnp.concatenate(ring_gather(grad_in, group_size), axis=0),
        preferred_element_type=jnp.float32,
    )
    return (embed_grad, copy_loss)


def solution(mesh):
    placed = (P(("dp", "mask"), None), P("dp", None), P(), P(), P(), P(), P(), P(), P())
    return jax.shard_map(
        on_device,
        mesh=mesh,
        in_specs=placed,
        out_specs=(P(("dp", "mask"), None), P(("dp", "mask"))),
        check_vma=False,
    )
```

```python
import functools
import math

import jax
import jax.numpy as jnp
from jax import lax
from jax.experimental import pallas as pl
from jax.sharding import PartitionSpec as P

D = 1024
HEADS = 16
DD = 768
GROUPS = 16


EPSILON = 1e-06


def row_norm(values):
    average = jnp.mean(values, axis=-1, keepdims=True)
    centred = values - average
    spread = jnp.mean(centred * centred, axis=-1, keepdims=True)
    return centred * lax.rsqrt(spread + EPSILON)


def head_norm(values):
    return values * lax.rsqrt(jnp.mean(values * values, axis=-1, keepdims=True) + EPSILON)


def mix_heads(queries, key_rows, values):
    score_scale = 1.0 / math.sqrt(queries.shape[-1])
    scores = (
        jnp.einsum("qhd,khd->hqk", queries, key_rows, preferred_element_type=jnp.float32)
        * score_scale
    )
    exponent = jnp.exp(scores)
    weights = (exponent / jnp.sum(exponent, axis=-1, keepdims=True)).astype(jnp.bfloat16)
    mixed = jnp.einsum("hqk,khd->qhd", weights, values, preferred_element_type=jnp.float32)
    return mixed.astype(jnp.bfloat16)


def split_project(projected):
    queries = head_norm(projected[:, 0].astype(jnp.float32)).astype(jnp.bfloat16)
    key_rows = head_norm(projected[:, 1].astype(jnp.float32)).astype(jnp.bfloat16)
    return mix_heads(queries, key_rows, projected[:, 2])


def project_rows(inputs, w_qkv):
    normed = row_norm(inputs.astype(jnp.float32)).astype(jnp.bfloat16)
    return jnp.dot(normed, w_qkv, preferred_element_type=jnp.float32).astype(jnp.bfloat16)


def attention_from(projected, w_out):
    row_count = projected.shape[0]
    context = split_project(projected.reshape(row_count, 3, HEADS, D // HEADS))
    return jnp.dot(context.reshape(row_count, D), w_out, preferred_element_type=jnp.float32)


def attention_branch(inputs, w_qkv, w_out):
    return attention_from(project_rows(inputs, w_qkv), w_out)


@jax.custom_vjp
def reuse_rows(inputs, w_qkv, projected):
    return projected


def reuse_rows_fwd(inputs, w_qkv, projected):
    return projected, (inputs, w_qkv)


def reuse_rows_bwd(saved, cotangent):
    inputs, w_qkv = saved
    _, pullback = jax.vjp(lambda rows: project_rows(rows, w_qkv), inputs)
    (d_inputs,) = pullback(cotangent)
    return d_inputs, jnp.zeros_like(w_qkv), jnp.zeros_like(cotangent)


reuse_rows.defvjp(reuse_rows_fwd, reuse_rows_bwd)


def decoder_output(visible_out, positions, total_rows, mask_embed, dec_in, conv_w, dec_out):
    slot_ids = jnp.arange(total_rows, dtype=jnp.int32)
    picks = (slot_ids[:, None] == positions[None, :]).astype(jnp.bfloat16)
    seen = jnp.max(picks, axis=1, keepdims=True)
    lowered_visible = jnp.dot(visible_out, dec_in, preferred_element_type=jnp.float32).astype(
        jnp.bfloat16
    )
    lowered_mask = jnp.dot(
        mask_embed[None, :], dec_in, preferred_element_type=jnp.float32
    ).astype(jnp.bfloat16)
    placed = jnp.dot(picks, lowered_visible, preferred_element_type=jnp.float32)
    lowered = jnp.where(seen > 0, placed, lowered_mask.astype(jnp.float32)).astype(jnp.bfloat16)
    grouped = lowered.reshape(total_rows, GROUPS, DD // GROUPS)
    padded = jnp.pad(grouped, ((1, 1), (0, 0), (0, 0)))
    convolved = jnp.zeros((total_rows, GROUPS, DD // GROUPS), jnp.float32)
    for offset in range(3):
        convolved = convolved + jnp.einsum(
            "pgi,gio->pgo",
            padded[offset : offset + total_rows],
            conv_w[offset],
            preferred_element_type=jnp.float32,
        )
    activated = jax.nn.gelu(row_norm(convolved.reshape(total_rows, DD)), approximate=False)
    return (lowered.astype(jnp.float32) + activated).astype(jnp.bfloat16)


def loss_kernel(hidden_ref, dec_out_ref, targets_ref, keep_ref, squares_ref, d_hidden_ref, *, scale):
    predicted = jnp.dot(hidden_ref[...], dec_out_ref[...], preferred_element_type=jnp.float32)
    mismatch = (predicted - targets_ref[...].astype(jnp.float32)) * keep_ref[...]
    squares_ref[...] = jnp.sum(mismatch * mismatch, keepdims=True)
    d_predicted = (2.0 * scale * mismatch) * keep_ref[...]
    d_hidden = lax.dot_general(
        d_predicted.astype(jnp.bfloat16),
        dec_out_ref[...],
        (((1,), (1,)), ((), ())),
        preferred_element_type=jnp.float32,
    )
    d_hidden_ref[...] = d_hidden.astype(jnp.bfloat16)


def masked_squares(hidden, dec_out, targets, keep, scale):
    rows, width = hidden.shape
    return pl.pallas_call(
        functools.partial(loss_kernel, scale=scale),
        out_shape=(
            jax.ShapeDtypeStruct((1, 1), jnp.float32),
            jax.ShapeDtypeStruct((rows, width), jnp.bfloat16),
        ),
    )(hidden, dec_out, targets, keep)


@functools.partial(jax.custom_vjp, nondiff_argnums=(4,))
def squares_of(hidden, dec_out, targets, keep, scale):
    return masked_squares(hidden, dec_out, targets, keep, scale)[0][0, 0]


def squares_of_fwd(hidden, dec_out, targets, keep, scale):
    squares, d_hidden = masked_squares(hidden, dec_out, targets, keep, scale)
    return squares[0, 0], (d_hidden, dec_out, targets, keep)


def squares_of_bwd(scale, saved, cotangent):
    d_hidden, dec_out, targets, keep = saved
    ratio = (cotangent / scale).astype(jnp.bfloat16)
    return (
        d_hidden * ratio,
        jnp.zeros_like(dec_out),
        jnp.zeros_like(targets),
        jnp.zeros_like(keep),
    )


squares_of.defvjp(squares_of_fwd, squares_of_bwd)


def copy_terms(
    visible_in,
    positions,
    targets,
    w_qkv,
    w_out,
    mask_embed,
    dec_in,
    conv_w,
    dec_out,
    projected,
    scale,
):
    total_rows = targets.shape[0]
    if projected is None:
        branch = attention_branch(visible_in, w_qkv, w_out)
    else:
        branch = attention_from(reuse_rows(visible_in, w_qkv, projected), w_out)
    visible_out = (visible_in.astype(jnp.float32) + branch).astype(jnp.bfloat16)
    hidden = decoder_output(
        visible_out, positions, total_rows, mask_embed, dec_in, conv_w, dec_out
    )
    slot_ids = jnp.arange(total_rows, dtype=jnp.int32)
    seen = jnp.max((slot_ids[:, None] == positions[None, :]).astype(jnp.float32), axis=1)
    return squares_of(hidden, dec_out, targets, (1.0 - seen)[:, None], scale)


def ring_gather(values, group_size):
    parts = [values]
    for shift in range(1, group_size):
        pairs = [(source, (source - shift) % group_size) for source in range(group_size)]
        parts.append(lax.ppermute(values, "mask", pairs))
    return parts


def in_mask_order(parts, own_index):
    group_size = len(parts)
    blocks = []
    for block in range(group_size):
        slot = (block - own_index) % group_size
        chosen = parts[0]
        for other in range(1, group_size):
            chosen = jnp.where(slot == other, parts[other], chosen)
        blocks.append(chosen)
    return jnp.concatenate(blocks, axis=0)


def split_teacher(embedded, w_qkv, w_out, own_index, group_size):
    total_rows = embedded.shape[0]
    head_dim = D // HEADS
    heads_here = HEADS // group_size
    head_width = heads_here * head_dim
    normed = row_norm(embedded.astype(jnp.float32)).astype(jnp.bfloat16)
    own_cols = lax.dynamic_slice_in_dim(
        w_qkv.reshape(D, 3, D), own_index * head_width, head_width, 2
    )
    projected = jnp.einsum(
        "sd,dtw->stw", normed, own_cols, preferred_element_type=jnp.float32
    ).astype(jnp.bfloat16)
    context = split_project(projected.reshape(total_rows, 3, heads_here, head_dim))
    out_rows = lax.dynamic_slice_in_dim(w_out, own_index * head_width, head_width, 0)
    partial_value = jnp.dot(
        context.reshape(total_rows, head_width), out_rows, preferred_element_type=jnp.float32
    )
    return lax.psum(partial_value.astype(jnp.bfloat16), "mask").astype(jnp.float32)


def on_device(patches, visible_index, embed_w, w_qkv, w_out, mask_embed, dec_in, conv_w, dec_out):
    tok_rows = patches.shape[0]
    group_size = lax.axis_size("mask")
    own_index = lax.axis_index("mask")
    copies = visible_index.shape[0]
    visible_count = visible_index.shape[1]
    total_rows = tok_rows * group_size
    col_width = patches.shape[1] // group_size
    positions = lax.dynamic_index_in_dim(visible_index, own_index, 0, keepdims=False)
    clip_pixels = in_mask_order(ring_gather(patches, group_size), own_index)
    embedded = jnp.dot(clip_pixels, embed_w, preferred_element_type=jnp.float32).astype(
        jnp.bfloat16
    )
    clip_ids = jnp.arange(total_rows, dtype=jnp.int32)
    own_picks = (positions[:, None] == clip_ids[None, :]).astype(jnp.bfloat16)
    visible_in = jnp.dot(own_picks, embedded, preferred_element_type=jnp.float32).astype(
        jnp.bfloat16
    )
    if HEADS * total_rows * total_rows * 4 <= (1 << 24):
        clip_projected = project_rows(embedded, w_qkv)
        branch = attention_from(clip_projected, w_out)
        visible_projected = jnp.dot(
            own_picks, clip_projected, preferred_element_type=jnp.float32
        ).astype(jnp.bfloat16)
    else:
        branch = split_teacher(embedded, w_qkv, w_out, own_index, group_size)
        visible_projected = None
    all_targets = row_norm(branch).astype(jnp.bfloat16)

    def objective(rows_in):
        return copy_terms(
            rows_in,
            positions,
            all_targets,
            w_qkv,
            w_out,
            mask_embed,
            dec_in,
            conv_w,
            dec_out,
            visible_projected,
            factor,
        )

    factor = 0.5 / math.sqrt(copies * visible_count)
    squares, pullback = jax.vjp(objective, visible_in)
    (grad_in,) = pullback(jnp.ones_like(squares) * factor)
    copy_loss = jnp.reshape(squares / ((total_rows - visible_count) * D), (1,))
    slot_copy = (own_index + jnp.arange(group_size, dtype=jnp.int32)) % group_size
    flat_index = visible_index[slot_copy].reshape(copies * visible_count)
    own_cols = lax.dynamic_slice_in_dim(clip_pixels, own_index * col_width, col_width, 1)
    all_picks = (flat_index[:, None] == clip_ids[None, :]).astype(jnp.bfloat16)
    gathered = jnp.dot(all_picks, own_cols, preferred_element_type=jnp.float32).astype(
        jnp.bfloat16
    )
    embed_grad = jnp.einsum(
        "vc,vd->cd",
        gathered,
        jnp.concatenate(ring_gather(grad_in, group_size), axis=0),
        preferred_element_type=jnp.float32,
    )
    return (embed_grad, copy_loss)


def solution(mesh):
    placed = (P(("dp", "mask"), None), P("dp", None), P(), P(), P(), P(), P(), P(), P())
    return jax.shard_map(
        on_device,
        mesh=mesh,
        in_specs=placed,
        out_specs=(P(("dp", "mask"), None), P(("dp", "mask"))),
        check_vma=False,
    )
```

```python
import functools
import math

import jax
import jax.numpy as jnp
from jax import lax
from jax.experimental import pallas as pl
from jax.sharding import PartitionSpec as P

D = 1024
HEADS = 16
DD = 768
GROUPS = 16


EPSILON = 1e-06


def row_norm(values):
    average = jnp.mean(values, axis=-1, keepdims=True)
    centred = values - average
    spread = jnp.mean(centred * centred, axis=-1, keepdims=True)
    return centred * lax.rsqrt(spread + EPSILON)


def head_norm(values):
    return values * lax.rsqrt(jnp.mean(values * values, axis=-1, keepdims=True) + EPSILON)


def mix_heads(queries, key_rows, values):
    score_scale = 1.0 / math.sqrt(queries.shape[-1])
    scores = (
        jnp.einsum("qhd,khd->hqk", queries, key_rows, preferred_element_type=jnp.float32)
        * score_scale
    )
    exponent = jnp.exp(scores)
    weights = (exponent / jnp.sum(exponent, axis=-1, keepdims=True)).astype(jnp.bfloat16)
    mixed = jnp.einsum("hqk,khd->qhd", weights, values, preferred_element_type=jnp.float32)
    return mixed.astype(jnp.bfloat16)


def split_project(projected):
    queries = head_norm(projected[:, 0].astype(jnp.float32)).astype(jnp.bfloat16)
    key_rows = head_norm(projected[:, 1].astype(jnp.float32)).astype(jnp.bfloat16)
    return mix_heads(queries, key_rows, projected[:, 2])


def project_rows(inputs, w_qkv):
    normed = row_norm(inputs.astype(jnp.float32)).astype(jnp.bfloat16)
    return jnp.dot(normed, w_qkv, preferred_element_type=jnp.float32).astype(jnp.bfloat16)


def attention_from(projected, w_out):
    row_count = projected.shape[0]
    context = split_project(projected.reshape(row_count, 3, HEADS, D // HEADS))
    return jnp.dot(context.reshape(row_count, D), w_out, preferred_element_type=jnp.float32)


def attention_branch(inputs, w_qkv, w_out):
    return attention_from(project_rows(inputs, w_qkv), w_out)


@jax.custom_vjp
def reuse_rows(inputs, w_qkv, projected):
    return projected


def reuse_rows_fwd(inputs, w_qkv, projected):
    return projected, (inputs, w_qkv)


def reuse_rows_bwd(saved, cotangent):
    inputs, w_qkv = saved
    _, pullback = jax.vjp(lambda rows: project_rows(rows, w_qkv), inputs)
    (d_inputs,) = pullback(cotangent)
    return d_inputs, jnp.zeros_like(w_qkv), jnp.zeros_like(cotangent)


reuse_rows.defvjp(reuse_rows_fwd, reuse_rows_bwd)


def decoder_output(visible_out, positions, total_rows, mask_embed, dec_in, conv_w, dec_out):
    slot_ids = jnp.arange(total_rows, dtype=jnp.int32)
    picks = (slot_ids[:, None] == positions[None, :]).astype(jnp.bfloat16)
    seen = jnp.max(picks, axis=1, keepdims=True)
    lowered_visible = jnp.dot(visible_out, dec_in, preferred_element_type=jnp.float32).astype(
        jnp.bfloat16
    )
    lowered_mask = jnp.dot(
        mask_embed[None, :], dec_in, preferred_element_type=jnp.float32
    ).astype(jnp.bfloat16)
    placed = jnp.dot(picks, lowered_visible, preferred_element_type=jnp.float32)
    lowered = jnp.where(seen > 0, placed, lowered_mask.astype(jnp.float32)).astype(jnp.bfloat16)
    grouped = lowered.reshape(total_rows, GROUPS, DD // GROUPS)
    padded = jnp.pad(grouped, ((1, 1), (0, 0), (0, 0)))
    convolved = jnp.zeros((total_rows, GROUPS, DD // GROUPS), jnp.float32)
    for offset in range(3):
        convolved = convolved + jnp.einsum(
            "pgi,gio->pgo",
            padded[offset : offset + total_rows],
            conv_w[offset],
            preferred_element_type=jnp.float32,
        )
    activated = jax.nn.gelu(row_norm(convolved.reshape(total_rows, DD)), approximate=False)
    return (lowered.astype(jnp.float32) + activated).astype(jnp.bfloat16)


def loss_kernel(hidden_ref, dec_out_ref, targets_ref, keep_ref, squares_ref, d_hidden_ref, *, scale):
    predicted = jnp.dot(hidden_ref[...], dec_out_ref[...], preferred_element_type=jnp.float32)
    mismatch = (predicted - targets_ref[...].astype(jnp.float32)) * keep_ref[...]
    squares_ref[...] = jnp.sum(mismatch * mismatch, keepdims=True)
    d_predicted = (2.0 * scale * mismatch) * keep_ref[...]
    d_hidden = lax.dot_general(
        d_predicted.astype(jnp.bfloat16),
        dec_out_ref[...],
        (((1,), (1,)), ((), ())),
        preferred_element_type=jnp.float32,
    )
    d_hidden_ref[...] = d_hidden.astype(jnp.bfloat16)


def masked_squares(hidden, dec_out, targets, keep, scale):
    rows, width = hidden.shape
    return pl.pallas_call(
        functools.partial(loss_kernel, scale=scale),
        out_shape=(
            jax.ShapeDtypeStruct((1, 1), jnp.float32),
            jax.ShapeDtypeStruct((rows, width), jnp.bfloat16),
        ),
    )(hidden, dec_out, targets, keep)


@functools.partial(jax.custom_vjp, nondiff_argnums=(4,))
def squares_of(hidden, dec_out, targets, keep, scale):
    return masked_squares(hidden, dec_out, targets, keep, scale)[0][0, 0]


def squares_of_fwd(hidden, dec_out, targets, keep, scale):
    squares, d_hidden = masked_squares(hidden, dec_out, targets, keep, scale)
    return squares[0, 0], (d_hidden, dec_out, targets, keep)


def squares_of_bwd(scale, saved, cotangent):
    d_hidden, dec_out, targets, keep = saved
    ratio = (cotangent / scale).astype(jnp.bfloat16)
    return (
        d_hidden * ratio,
        jnp.zeros_like(dec_out),
        jnp.zeros_like(targets),
        jnp.zeros_like(keep),
    )


squares_of.defvjp(squares_of_fwd, squares_of_bwd)


def copy_terms(
    visible_in,
    positions,
    targets,
    w_qkv,
    w_out,
    mask_embed,
    dec_in,
    conv_w,
    dec_out,
    projected,
    scale,
):
    total_rows = targets.shape[0]
    if projected is None:
        branch = attention_branch(visible_in, w_qkv, w_out)
    else:
        branch = attention_from(reuse_rows(visible_in, w_qkv, projected), w_out)
    visible_out = (visible_in.astype(jnp.float32) + branch).astype(jnp.bfloat16)
    hidden = decoder_output(
        visible_out, positions, total_rows, mask_embed, dec_in, conv_w, dec_out
    )
    slot_ids = jnp.arange(total_rows, dtype=jnp.int32)
    seen = jnp.max((slot_ids[:, None] == positions[None, :]).astype(jnp.float32), axis=1)
    return squares_of(hidden, dec_out, targets, (1.0 - seen)[:, None], scale)


def exchange_gather(values, group_size):
    copies_out = jnp.broadcast_to(values[None], (group_size,) + values.shape)
    gathered = lax.all_to_all(copies_out, "mask", split_axis=0, concat_axis=0, tiled=True)
    return gathered.reshape((group_size * values.shape[0],) + values.shape[1:])


def ring_gather(values, group_size):
    parts = [values]
    for shift in range(1, group_size):
        pairs = [(source, (source - shift) % group_size) for source in range(group_size)]
        parts.append(lax.ppermute(values, "mask", pairs))
    return parts


def in_mask_order(parts, own_index):
    group_size = len(parts)
    blocks = []
    for block in range(group_size):
        slot = (block - own_index) % group_size
        chosen = parts[0]
        for other in range(1, group_size):
            chosen = jnp.where(slot == other, parts[other], chosen)
        blocks.append(chosen)
    return jnp.concatenate(blocks, axis=0)


def split_teacher(embedded, w_qkv, w_out, own_index, group_size):
    total_rows = embedded.shape[0]
    head_dim = D // HEADS
    heads_here = HEADS // group_size
    head_width = heads_here * head_dim
    normed = row_norm(embedded.astype(jnp.float32)).astype(jnp.bfloat16)
    own_cols = lax.dynamic_slice_in_dim(
        w_qkv.reshape(D, 3, D), own_index * head_width, head_width, 2
    )
    projected = jnp.einsum(
        "sd,dtw->stw", normed, own_cols, preferred_element_type=jnp.float32
    ).astype(jnp.bfloat16)
    context = split_project(projected.reshape(total_rows, 3, heads_here, head_dim))
    out_rows = lax.dynamic_slice_in_dim(w_out, own_index * head_width, head_width, 0)
    partial_value = jnp.dot(
        context.reshape(total_rows, head_width), out_rows, preferred_element_type=jnp.float32
    )
    return lax.psum(partial_value.astype(jnp.bfloat16), "mask").astype(jnp.float32)


def on_device(patches, visible_index, embed_w, w_qkv, w_out, mask_embed, dec_in, conv_w, dec_out):
    tok_rows = patches.shape[0]
    group_size = lax.axis_size("mask")
    own_index = lax.axis_index("mask")
    copies = visible_index.shape[0]
    visible_count = visible_index.shape[1]
    total_rows = tok_rows * group_size
    col_width = patches.shape[1] // group_size
    positions = lax.dynamic_index_in_dim(visible_index, own_index, 0, keepdims=False)
    clip_pixels = exchange_gather(patches, group_size)
    embedded = jnp.dot(clip_pixels, embed_w, preferred_element_type=jnp.float32).astype(
        jnp.bfloat16
    )
    clip_ids = jnp.arange(total_rows, dtype=jnp.int32)
    own_picks = (positions[:, None] == clip_ids[None, :]).astype(jnp.bfloat16)
    visible_in = jnp.dot(own_picks, embedded, preferred_element_type=jnp.float32).astype(
        jnp.bfloat16
    )
    if HEADS * total_rows * total_rows * 4 <= (1 << 24):
        clip_projected = project_rows(embedded, w_qkv)
        branch = attention_from(clip_projected, w_out)
        visible_projected = jnp.dot(
            own_picks, clip_projected, preferred_element_type=jnp.float32
        ).astype(jnp.bfloat16)
    else:
        branch = split_teacher(embedded, w_qkv, w_out, own_index, group_size)
        visible_projected = None
    all_targets = row_norm(branch).astype(jnp.bfloat16)

    def objective(rows_in):
        return copy_terms(
            rows_in,
            positions,
            all_targets,
            w_qkv,
            w_out,
            mask_embed,
            dec_in,
            conv_w,
            dec_out,
            visible_projected,
            factor,
        )

    factor = 0.5 / math.sqrt(copies * visible_count)
    squares, pullback = jax.vjp(objective, visible_in)
    (grad_in,) = pullback(jnp.ones_like(squares) * factor)
    copy_loss = jnp.reshape(squares / ((total_rows - visible_count) * D), (1,))
    flat_index = visible_index.reshape(copies * visible_count)
    own_cols = lax.dynamic_slice_in_dim(clip_pixels, own_index * col_width, col_width, 1)
    all_picks = (flat_index[:, None] == clip_ids[None, :]).astype(jnp.bfloat16)
    gathered = jnp.dot(all_picks, own_cols, preferred_element_type=jnp.float32).astype(
        jnp.bfloat16
    )
    embed_grad = jnp.einsum(
        "vc,vd->cd",
        gathered,
        exchange_gather(grad_in, group_size),
        preferred_element_type=jnp.float32,
    )
    return (embed_grad, copy_loss)


def solution(mesh):
    placed = (P(("dp", "mask"), None), P("dp", None), P(), P(), P(), P(), P(), P(), P())
    return jax.shard_map(
        on_device,
        mesh=mesh,
        in_specs=placed,
        out_specs=(P(("dp", "mask"), None), P(("dp", "mask"))),
        check_vma=False,
    )
```

```python
import functools
import math

import jax
import jax.numpy as jnp
from jax import lax
from jax.experimental import pallas as pl
from jax.sharding import PartitionSpec as P

D = 1024
HEADS = 16
DD = 768
GROUPS = 16


EPSILON = 1e-06


def row_norm(values):
    average = jnp.mean(values, axis=-1, keepdims=True)
    centred = values - average
    spread = jnp.mean(centred * centred, axis=-1, keepdims=True)
    return centred * lax.rsqrt(spread + EPSILON)


def head_norm(values):
    return values * lax.rsqrt(jnp.mean(values * values, axis=-1, keepdims=True) + EPSILON)


def mix_heads(queries, key_rows, values):
    score_scale = 1.0 / math.sqrt(queries.shape[-1])
    scores = (
        jnp.einsum("qhd,khd->hqk", queries, key_rows, preferred_element_type=jnp.float32)
        * score_scale
    )
    exponent = jnp.exp(scores)
    weights = (exponent / jnp.sum(exponent, axis=-1, keepdims=True)).astype(jnp.bfloat16)
    mixed = jnp.einsum("hqk,khd->qhd", weights, values, preferred_element_type=jnp.float32)
    return mixed.astype(jnp.bfloat16)


def split_project(projected):
    queries = head_norm(projected[:, 0].astype(jnp.float32)).astype(jnp.bfloat16)
    key_rows = head_norm(projected[:, 1].astype(jnp.float32)).astype(jnp.bfloat16)
    return mix_heads(queries, key_rows, projected[:, 2])


def project_rows(inputs, w_qkv):
    normed = row_norm(inputs.astype(jnp.float32)).astype(jnp.bfloat16)
    return jnp.dot(normed, w_qkv, preferred_element_type=jnp.float32).astype(jnp.bfloat16)


def attention_from(projected, w_out):
    row_count = projected.shape[0]
    context = split_project(projected.reshape(row_count, 3, HEADS, D // HEADS))
    return jnp.dot(context.reshape(row_count, D), w_out, preferred_element_type=jnp.float32)


def attention_branch(inputs, w_qkv, w_out):
    return attention_from(project_rows(inputs, w_qkv), w_out)


@jax.custom_vjp
def reuse_rows(inputs, w_qkv, projected):
    return projected


def reuse_rows_fwd(inputs, w_qkv, projected):
    return projected, (inputs, w_qkv)


def reuse_rows_bwd(saved, cotangent):
    inputs, w_qkv = saved
    _, pullback = jax.vjp(
        lambda rows: row_norm(rows.astype(jnp.float32)).astype(jnp.bfloat16), inputs
    )
    d_normed = jnp.dot(cotangent, w_qkv.T, preferred_element_type=jnp.float32)
    d_normed = lax.optimization_barrier(d_normed.astype(jnp.bfloat16))
    (d_inputs,) = pullback(d_normed)
    return d_inputs, jnp.zeros_like(w_qkv), jnp.zeros_like(cotangent)


reuse_rows.defvjp(reuse_rows_fwd, reuse_rows_bwd)


def decoder_output(visible_out, positions, total_rows, mask_embed, dec_in, conv_w, dec_out):
    slot_ids = jnp.arange(total_rows, dtype=jnp.int32)
    picks = (slot_ids[:, None] == positions[None, :]).astype(jnp.bfloat16)
    seen = jnp.max(picks, axis=1, keepdims=True)
    lowered_visible = jnp.dot(visible_out, dec_in, preferred_element_type=jnp.float32).astype(
        jnp.bfloat16
    )
    lowered_mask = jnp.dot(
        mask_embed[None, :], dec_in, preferred_element_type=jnp.float32
    ).astype(jnp.bfloat16)
    placed = jnp.dot(picks, lowered_visible, preferred_element_type=jnp.float32)
    lowered = jnp.where(seen > 0, placed, lowered_mask.astype(jnp.float32)).astype(jnp.bfloat16)
    grouped = lowered.reshape(total_rows, GROUPS, DD // GROUPS)
    padded = jnp.pad(grouped, ((1, 1), (0, 0), (0, 0)))
    convolved = jnp.zeros((total_rows, GROUPS, DD // GROUPS), jnp.float32)
    for offset in range(3):
        convolved = convolved + jnp.einsum(
            "pgi,gio->pgo",
            padded[offset : offset + total_rows],
            conv_w[offset],
            preferred_element_type=jnp.float32,
        )
    activated = jax.nn.gelu(row_norm(convolved.reshape(total_rows, DD)), approximate=False)
    return (lowered.astype(jnp.float32) + activated).astype(jnp.bfloat16)


def loss_kernel(hidden_ref, dec_out_ref, targets_ref, keep_ref, squares_ref, d_hidden_ref, *, scale):
    predicted = jnp.dot(hidden_ref[...], dec_out_ref[...], preferred_element_type=jnp.float32)
    mismatch = (predicted - targets_ref[...].astype(jnp.float32)) * keep_ref[...]
    squares_ref[...] = jnp.sum(mismatch * mismatch, keepdims=True)
    d_predicted = (2.0 * scale * mismatch) * keep_ref[...]
    d_hidden = lax.dot_general(
        d_predicted.astype(jnp.bfloat16),
        dec_out_ref[...],
        (((1,), (1,)), ((), ())),
        preferred_element_type=jnp.float32,
    )
    d_hidden_ref[...] = d_hidden.astype(jnp.bfloat16)


def masked_squares(hidden, dec_out, targets, keep, scale):
    rows, width = hidden.shape
    return pl.pallas_call(
        functools.partial(loss_kernel, scale=scale),
        out_shape=(
            jax.ShapeDtypeStruct((1, 1), jnp.float32),
            jax.ShapeDtypeStruct((rows, width), jnp.bfloat16),
        ),
    )(hidden, dec_out, targets, keep)


@functools.partial(jax.custom_vjp, nondiff_argnums=(4,))
def squares_of(hidden, dec_out, targets, keep, scale):
    return masked_squares(hidden, dec_out, targets, keep, scale)[0][0, 0]


def squares_of_fwd(hidden, dec_out, targets, keep, scale):
    squares, d_hidden = masked_squares(hidden, dec_out, targets, keep, scale)
    return squares[0, 0], (d_hidden, dec_out, targets, keep)


def squares_of_bwd(scale, saved, cotangent):
    d_hidden, dec_out, targets, keep = saved
    ratio = (cotangent / scale).astype(jnp.bfloat16)
    return (
        d_hidden * ratio,
        jnp.zeros_like(dec_out),
        jnp.zeros_like(targets),
        jnp.zeros_like(keep),
    )


squares_of.defvjp(squares_of_fwd, squares_of_bwd)


def copy_terms(
    visible_in,
    positions,
    targets,
    w_qkv,
    w_out,
    mask_embed,
    dec_in,
    conv_w,
    dec_out,
    projected,
    scale,
):
    total_rows = targets.shape[0]
    if projected is None:
        branch = attention_branch(visible_in, w_qkv, w_out)
    else:
        branch = attention_from(reuse_rows(visible_in, w_qkv, projected), w_out)
    visible_out = (visible_in.astype(jnp.float32) + branch).astype(jnp.bfloat16)
    hidden = decoder_output(
        visible_out, positions, total_rows, mask_embed, dec_in, conv_w, dec_out
    )
    slot_ids = jnp.arange(total_rows, dtype=jnp.int32)
    seen = jnp.max((slot_ids[:, None] == positions[None, :]).astype(jnp.float32), axis=1)
    return squares_of(hidden, dec_out, targets, (1.0 - seen)[:, None], scale)


def ring_gather(values, group_size):
    parts = [values]
    for shift in range(1, group_size):
        pairs = [(source, (source - shift) % group_size) for source in range(group_size)]
        parts.append(lax.ppermute(values, "mask", pairs))
    return parts


def in_mask_order(parts, own_index):
    group_size = len(parts)
    blocks = []
    for block in range(group_size):
        slot = (block - own_index) % group_size
        chosen = parts[0]
        for other in range(1, group_size):
            chosen = jnp.where(slot == other, parts[other], chosen)
        blocks.append(chosen)
    return jnp.concatenate(blocks, axis=0)


def split_teacher(embedded, w_qkv, w_out, own_index, group_size):
    total_rows = embedded.shape[0]
    head_dim = D // HEADS
    heads_here = HEADS // group_size
    head_width = heads_here * head_dim
    normed = row_norm(embedded.astype(jnp.float32)).astype(jnp.bfloat16)
    own_cols = lax.dynamic_slice_in_dim(
        w_qkv.reshape(D, 3, D), own_index * head_width, head_width, 2
    )
    projected = jnp.einsum(
        "sd,dtw->stw", normed, own_cols, preferred_element_type=jnp.float32
    ).astype(jnp.bfloat16)
    context = split_project(projected.reshape(total_rows, 3, heads_here, head_dim))
    out_rows = lax.dynamic_slice_in_dim(w_out, own_index * head_width, head_width, 0)
    partial_value = jnp.dot(
        context.reshape(total_rows, head_width), out_rows, preferred_element_type=jnp.float32
    )
    return lax.psum(partial_value.astype(jnp.bfloat16), "mask").astype(jnp.float32)


def on_device(patches, visible_index, embed_w, w_qkv, w_out, mask_embed, dec_in, conv_w, dec_out):
    tok_rows = patches.shape[0]
    group_size = lax.axis_size("mask")
    own_index = lax.axis_index("mask")
    copies = visible_index.shape[0]
    visible_count = visible_index.shape[1]
    total_rows = tok_rows * group_size
    col_width = patches.shape[1] // group_size
    positions = lax.dynamic_index_in_dim(visible_index, own_index, 0, keepdims=False)
    clip_pixels = in_mask_order(ring_gather(patches, group_size), own_index)
    embedded = jnp.dot(clip_pixels, embed_w, preferred_element_type=jnp.float32).astype(
        jnp.bfloat16
    )
    clip_ids = jnp.arange(total_rows, dtype=jnp.int32)
    own_picks = (positions[:, None] == clip_ids[None, :]).astype(jnp.bfloat16)
    visible_in = jnp.dot(own_picks, embedded, preferred_element_type=jnp.float32).astype(
        jnp.bfloat16
    )
    if HEADS * total_rows * total_rows * 4 <= (1 << 24):
        clip_projected = project_rows(embedded, w_qkv)
        branch = attention_from(clip_projected, w_out)
        visible_projected = jnp.dot(
            own_picks, clip_projected, preferred_element_type=jnp.float32
        ).astype(jnp.bfloat16)
    else:
        branch = split_teacher(embedded, w_qkv, w_out, own_index, group_size)
        visible_projected = None
    all_targets = row_norm(branch).astype(jnp.bfloat16)

    def objective(rows_in):
        return copy_terms(
            rows_in,
            positions,
            all_targets,
            w_qkv,
            w_out,
            mask_embed,
            dec_in,
            conv_w,
            dec_out,
            visible_projected,
            factor,
        )

    factor = 0.5 / math.sqrt(copies * visible_count)
    squares, pullback = jax.vjp(objective, visible_in)
    (grad_in,) = pullback(jnp.ones_like(squares) * factor)
    copy_loss = jnp.reshape(squares / ((total_rows - visible_count) * D), (1,))
    slot_copy = (own_index + jnp.arange(group_size, dtype=jnp.int32)) % group_size
    flat_index = visible_index[slot_copy].reshape(copies * visible_count)
    own_cols = lax.dynamic_slice_in_dim(clip_pixels, own_index * col_width, col_width, 1)
    all_picks = (flat_index[:, None] == clip_ids[None, :]).astype(jnp.bfloat16)
    gathered = jnp.dot(all_picks, own_cols, preferred_element_type=jnp.float32).astype(
        jnp.bfloat16
    )
    embed_grad = jnp.einsum(
        "vc,vd->cd",
        gathered,
        jnp.concatenate(ring_gather(grad_in, group_size), axis=0),
        preferred_element_type=jnp.float32,
    )
    return (embed_grad, copy_loss)


def solution(mesh):
    placed = (P(("dp", "mask"), None), P("dp", None), P(), P(), P(), P(), P(), P(), P())
    return jax.shard_map(
        on_device,
        mesh=mesh,
        in_specs=placed,
        out_specs=(P(("dp", "mask"), None), P(("dp", "mask"))),
        check_vma=False,
    )
```

```python
import functools
import math

import jax
import jax.numpy as jnp
from jax import lax
from jax.experimental import pallas as pl
from jax.sharding import PartitionSpec as P

D = 1024
HEADS = 16
DD = 768
GROUPS = 16


EPSILON = 1e-06


def row_norm(values):
    average = jnp.mean(values, axis=-1, keepdims=True)
    centred = values - average
    spread = jnp.mean(centred * centred, axis=-1, keepdims=True)
    return centred * lax.rsqrt(spread + EPSILON)


def head_norm(values):
    return values * lax.rsqrt(jnp.mean(values * values, axis=-1, keepdims=True) + EPSILON)


def mix_heads(queries, key_rows, values):
    score_scale = 1.0 / math.sqrt(queries.shape[-1])
    scores = (
        jnp.einsum("qhd,khd->hqk", queries, key_rows, preferred_element_type=jnp.float32)
        * score_scale
    )
    exponent = jnp.exp(scores)
    weights = (exponent / jnp.sum(exponent, axis=-1, keepdims=True)).astype(jnp.bfloat16)
    mixed = jnp.einsum("hqk,khd->qhd", weights, values, preferred_element_type=jnp.float32)
    return mixed.astype(jnp.bfloat16)


def split_project(projected):
    queries = head_norm(projected[:, 0].astype(jnp.float32)).astype(jnp.bfloat16)
    key_rows = head_norm(projected[:, 1].astype(jnp.float32)).astype(jnp.bfloat16)
    return mix_heads(queries, key_rows, projected[:, 2])


def project_rows(inputs, w_qkv):
    normed = row_norm(inputs.astype(jnp.float32)).astype(jnp.bfloat16)
    return jnp.dot(normed, w_qkv, preferred_element_type=jnp.float32).astype(jnp.bfloat16)


def attention_from(projected, w_out):
    row_count = projected.shape[0]
    context = split_project(projected.reshape(row_count, 3, HEADS, D // HEADS))
    return jnp.dot(context.reshape(row_count, D), w_out, preferred_element_type=jnp.float32)


def attention_branch(inputs, w_qkv, w_out):
    return attention_from(project_rows(inputs, w_qkv), w_out)


def transposed_product_kernel(rows_ref, weight_ref, out_ref):
    step = pl.program_id(0)
    part = lax.dot_general(
        rows_ref[...],
        weight_ref[...],
        (((1,), (1,)), ((), ())),
        preferred_element_type=jnp.float32,
    )

    @pl.when(step == 0)
    def _():
        out_ref[...] = part

    @pl.when(step > 0)
    def _():
        out_ref[...] += part


def transposed_product(rows, weight):
    count, inner = rows.shape
    outer = weight.shape[0]
    block = 512 if inner % 512 == 0 else inner
    return pl.pallas_call(
        transposed_product_kernel,
        grid=(inner // block,),
        in_specs=[
            pl.BlockSpec((count, block), lambda k: (0, k)),
            pl.BlockSpec((outer, block), lambda k: (0, k)),
        ],
        out_specs=pl.BlockSpec((count, outer), lambda k: (0, 0)),
        out_shape=jax.ShapeDtypeStruct((count, outer), jnp.float32),
    )(rows, weight)


@jax.custom_vjp
def reuse_rows(inputs, w_qkv, projected):
    return projected


def reuse_rows_fwd(inputs, w_qkv, projected):
    return projected, (inputs, w_qkv)


def reuse_rows_bwd(saved, cotangent):
    inputs, w_qkv = saved
    _, pullback = jax.vjp(
        lambda rows: row_norm(rows.astype(jnp.float32)).astype(jnp.bfloat16), inputs
    )
    d_normed = transposed_product(cotangent, w_qkv)
    (d_inputs,) = pullback(d_normed.astype(jnp.bfloat16))
    return d_inputs, jnp.zeros_like(w_qkv), jnp.zeros_like(cotangent)


reuse_rows.defvjp(reuse_rows_fwd, reuse_rows_bwd)


def decoder_output(visible_out, positions, total_rows, mask_embed, dec_in, conv_w, dec_out):
    slot_ids = jnp.arange(total_rows, dtype=jnp.int32)
    picks = (slot_ids[:, None] == positions[None, :]).astype(jnp.bfloat16)
    seen = jnp.max(picks, axis=1, keepdims=True)
    lowered_visible = jnp.dot(visible_out, dec_in, preferred_element_type=jnp.float32).astype(
        jnp.bfloat16
    )
    lowered_mask = jnp.dot(
        mask_embed[None, :], dec_in, preferred_element_type=jnp.float32
    ).astype(jnp.bfloat16)
    placed = jnp.dot(picks, lowered_visible, preferred_element_type=jnp.float32)
    lowered = jnp.where(seen > 0, placed, lowered_mask.astype(jnp.float32)).astype(jnp.bfloat16)
    grouped = lowered.reshape(total_rows, GROUPS, DD // GROUPS)
    padded = jnp.pad(grouped, ((1, 1), (0, 0), (0, 0)))
    convolved = jnp.zeros((total_rows, GROUPS, DD // GROUPS), jnp.float32)
    for offset in range(3):
        convolved = convolved + jnp.einsum(
            "pgi,gio->pgo",
            padded[offset : offset + total_rows],
            conv_w[offset],
            preferred_element_type=jnp.float32,
        )
    activated = jax.nn.gelu(row_norm(convolved.reshape(total_rows, DD)), approximate=False)
    return (lowered.astype(jnp.float32) + activated).astype(jnp.bfloat16)


def loss_kernel(hidden_ref, dec_out_ref, targets_ref, keep_ref, squares_ref, d_hidden_ref, *, scale):
    predicted = jnp.dot(hidden_ref[...], dec_out_ref[...], preferred_element_type=jnp.float32)
    mismatch = (predicted - targets_ref[...].astype(jnp.float32)) * keep_ref[...]
    squares_ref[...] = jnp.sum(mismatch * mismatch, keepdims=True)
    d_predicted = (2.0 * scale * mismatch) * keep_ref[...]
    d_hidden = lax.dot_general(
        d_predicted.astype(jnp.bfloat16),
        dec_out_ref[...],
        (((1,), (1,)), ((), ())),
        preferred_element_type=jnp.float32,
    )
    d_hidden_ref[...] = d_hidden.astype(jnp.bfloat16)


def masked_squares(hidden, dec_out, targets, keep, scale):
    rows, width = hidden.shape
    return pl.pallas_call(
        functools.partial(loss_kernel, scale=scale),
        out_shape=(
            jax.ShapeDtypeStruct((1, 1), jnp.float32),
            jax.ShapeDtypeStruct((rows, width), jnp.bfloat16),
        ),
    )(hidden, dec_out, targets, keep)


@functools.partial(jax.custom_vjp, nondiff_argnums=(4,))
def squares_of(hidden, dec_out, targets, keep, scale):
    return masked_squares(hidden, dec_out, targets, keep, scale)[0][0, 0]


def squares_of_fwd(hidden, dec_out, targets, keep, scale):
    squares, d_hidden = masked_squares(hidden, dec_out, targets, keep, scale)
    return squares[0, 0], (d_hidden, dec_out, targets, keep)


def squares_of_bwd(scale, saved, cotangent):
    d_hidden, dec_out, targets, keep = saved
    ratio = (cotangent / scale).astype(jnp.bfloat16)
    return (
        d_hidden * ratio,
        jnp.zeros_like(dec_out),
        jnp.zeros_like(targets),
        jnp.zeros_like(keep),
    )


squares_of.defvjp(squares_of_fwd, squares_of_bwd)


def copy_terms(
    visible_in,
    positions,
    targets,
    w_qkv,
    w_out,
    mask_embed,
    dec_in,
    conv_w,
    dec_out,
    projected,
    scale,
):
    total_rows = targets.shape[0]
    if projected is None:
        branch = attention_branch(visible_in, w_qkv, w_out)
    else:
        branch = attention_from(reuse_rows(visible_in, w_qkv, projected), w_out)
    visible_out = (visible_in.astype(jnp.float32) + branch).astype(jnp.bfloat16)
    hidden = decoder_output(
        visible_out, positions, total_rows, mask_embed, dec_in, conv_w, dec_out
    )
    slot_ids = jnp.arange(total_rows, dtype=jnp.int32)
    seen = jnp.max((slot_ids[:, None] == positions[None, :]).astype(jnp.float32), axis=1)
    return squares_of(hidden, dec_out, targets, (1.0 - seen)[:, None], scale)


def ring_gather(values, group_size):
    parts = [values]
    for shift in range(1, group_size):
        pairs = [(source, (source - shift) % group_size) for source in range(group_size)]
        parts.append(lax.ppermute(values, "mask", pairs))
    return parts


def in_mask_order(parts, own_index):
    group_size = len(parts)
    blocks = []
    for block in range(group_size):
        slot = (block - own_index) % group_size
        chosen = parts[0]
        for other in range(1, group_size):
            chosen = jnp.where(slot == other, parts[other], chosen)
        blocks.append(chosen)
    return jnp.concatenate(blocks, axis=0)


def split_teacher(embedded, w_qkv, w_out, own_index, group_size):
    total_rows = embedded.shape[0]
    head_dim = D // HEADS
    heads_here = HEADS // group_size
    head_width = heads_here * head_dim
    normed = row_norm(embedded.astype(jnp.float32)).astype(jnp.bfloat16)
    own_cols = lax.dynamic_slice_in_dim(
        w_qkv.reshape(D, 3, D), own_index * head_width, head_width, 2
    )
    projected = jnp.einsum(
        "sd,dtw->stw", normed, own_cols, preferred_element_type=jnp.float32
    ).astype(jnp.bfloat16)
    context = split_project(projected.reshape(total_rows, 3, heads_here, head_dim))
    out_rows = lax.dynamic_slice_in_dim(w_out, own_index * head_width, head_width, 0)
    partial_value = jnp.dot(
        context.reshape(total_rows, head_width), out_rows, preferred_element_type=jnp.float32
    )
    return lax.psum(partial_value.astype(jnp.bfloat16), "mask").astype(jnp.float32)


def on_device(patches, visible_index, embed_w, w_qkv, w_out, mask_embed, dec_in, conv_w, dec_out):
    tok_rows = patches.shape[0]
    group_size = lax.axis_size("mask")
    own_index = lax.axis_index("mask")
    copies = visible_index.shape[0]
    visible_count = visible_index.shape[1]
    total_rows = tok_rows * group_size
    col_width = patches.shape[1] // group_size
    positions = lax.dynamic_index_in_dim(visible_index, own_index, 0, keepdims=False)
    clip_pixels = in_mask_order(ring_gather(patches, group_size), own_index)
    embedded = jnp.dot(clip_pixels, embed_w, preferred_element_type=jnp.float32).astype(
        jnp.bfloat16
    )
    clip_ids = jnp.arange(total_rows, dtype=jnp.int32)
    own_picks = (positions[:, None] == clip_ids[None, :]).astype(jnp.bfloat16)
    visible_in = jnp.dot(own_picks, embedded, preferred_element_type=jnp.float32).astype(
        jnp.bfloat16
    )
    if HEADS * total_rows * total_rows * 4 <= (1 << 24):
        clip_projected = project_rows(embedded, w_qkv)
        branch = attention_from(clip_projected, w_out)
        visible_projected = jnp.dot(
            own_picks, clip_projected, preferred_element_type=jnp.float32
        ).astype(jnp.bfloat16)
    else:
        branch = split_teacher(embedded, w_qkv, w_out, own_index, group_size)
        visible_projected = None
    all_targets = row_norm(branch).astype(jnp.bfloat16)

    def objective(rows_in):
        return copy_terms(
            rows_in,
            positions,
            all_targets,
            w_qkv,
            w_out,
            mask_embed,
            dec_in,
            conv_w,
            dec_out,
            visible_projected,
            factor,
        )

    factor = 0.5 / math.sqrt(copies * visible_count)
    squares, pullback = jax.vjp(objective, visible_in)
    (grad_in,) = pullback(jnp.ones_like(squares) * factor)
    copy_loss = jnp.reshape(squares / ((total_rows - visible_count) * D), (1,))
    slot_copy = (own_index + jnp.arange(group_size, dtype=jnp.int32)) % group_size
    flat_index = visible_index[slot_copy].reshape(copies * visible_count)
    own_cols = lax.dynamic_slice_in_dim(clip_pixels, own_index * col_width, col_width, 1)
    all_picks = (flat_index[:, None] == clip_ids[None, :]).astype(jnp.bfloat16)
    gathered = jnp.dot(all_picks, own_cols, preferred_element_type=jnp.float32).astype(
        jnp.bfloat16
    )
    embed_grad = jnp.einsum(
        "vc,vd->cd",
        gathered,
        jnp.concatenate(ring_gather(grad_in, group_size), axis=0),
        preferred_element_type=jnp.float32,
    )
    return (embed_grad, copy_loss)


def solution(mesh):
    placed = (P(("dp", "mask"), None), P("dp", None), P(), P(), P(), P(), P(), P(), P())
    return jax.shard_map(
        on_device,
        mesh=mesh,
        in_specs=placed,
        out_specs=(P(("dp", "mask"), None), P(("dp", "mask"))),
        check_vma=False,
    )
```

```python
import functools
import math

import jax
import jax.numpy as jnp
from jax import lax
from jax.experimental import pallas as pl
from jax.sharding import PartitionSpec as P

D = 1024
HEADS = 16
DD = 768
GROUPS = 16


EPSILON = 1e-06


def row_norm(values):
    average = jnp.mean(values, axis=-1, keepdims=True)
    centred = values - average
    spread = jnp.mean(centred * centred, axis=-1, keepdims=True)
    return centred * lax.rsqrt(spread + EPSILON)


def head_norm(values):
    return values * lax.rsqrt(jnp.mean(values * values, axis=-1, keepdims=True) + EPSILON)


def mix_heads(queries, key_rows, values):
    score_scale = 1.0 / math.sqrt(queries.shape[-1])
    scores = (
        jnp.einsum("qhd,khd->hqk", queries, key_rows, preferred_element_type=jnp.float32)
        * score_scale
    )
    exponent = jnp.exp(scores)
    weights = (exponent / jnp.sum(exponent, axis=-1, keepdims=True)).astype(jnp.bfloat16)
    mixed = jnp.einsum("hqk,khd->qhd", weights, values, preferred_element_type=jnp.float32)
    return mixed.astype(jnp.bfloat16)


def split_project(projected):
    queries = head_norm(projected[:, 0].astype(jnp.float32)).astype(jnp.bfloat16)
    key_rows = head_norm(projected[:, 1].astype(jnp.float32)).astype(jnp.bfloat16)
    return mix_heads(queries, key_rows, projected[:, 2])


def project_rows(inputs, w_qkv):
    normed = row_norm(inputs.astype(jnp.float32)).astype(jnp.bfloat16)
    return jnp.dot(normed, w_qkv, preferred_element_type=jnp.float32).astype(jnp.bfloat16)


def attention_from(projected, w_out):
    row_count = projected.shape[0]
    context = split_project(projected.reshape(row_count, 3, HEADS, D // HEADS))
    return jnp.dot(context.reshape(row_count, D), w_out, preferred_element_type=jnp.float32)


def attention_branch(inputs, w_qkv, w_out):
    return attention_from(project_rows(inputs, w_qkv), w_out)


@jax.custom_vjp
def reuse_rows(inputs, w_qkv, projected):
    return projected


def reuse_rows_fwd(inputs, w_qkv, projected):
    return projected, (inputs, w_qkv)


def reuse_rows_bwd(saved, cotangent):
    inputs, w_qkv = saved
    _, pullback = jax.vjp(
        lambda rows: row_norm(rows.astype(jnp.float32)).astype(jnp.bfloat16), inputs
    )
    d_normed = jnp.dot(cotangent, w_qkv.T, preferred_element_type=jnp.float32)
    d_normed = lax.optimization_barrier(d_normed.astype(jnp.bfloat16))
    (d_inputs,) = pullback(d_normed)
    return d_inputs, jnp.zeros_like(w_qkv), jnp.zeros_like(cotangent)


reuse_rows.defvjp(reuse_rows_fwd, reuse_rows_bwd)


def decoder_output(visible_out, positions, total_rows, mask_embed, dec_in, conv_w, dec_out):
    slot_ids = jnp.arange(total_rows, dtype=jnp.int32)
    picks = (slot_ids[:, None] == positions[None, :]).astype(jnp.bfloat16)
    seen = jnp.max(picks, axis=1, keepdims=True)
    lowered_visible = jnp.dot(visible_out, dec_in, preferred_element_type=jnp.float32).astype(
        jnp.bfloat16
    )
    lowered_mask = jnp.dot(
        mask_embed[None, :], dec_in, preferred_element_type=jnp.float32
    ).astype(jnp.bfloat16)
    placed = jnp.dot(picks, lowered_visible, preferred_element_type=jnp.float32)
    lowered = jnp.where(seen > 0, placed, lowered_mask.astype(jnp.float32)).astype(jnp.bfloat16)
    grouped = lowered.reshape(total_rows, GROUPS, DD // GROUPS)
    padded = jnp.pad(grouped, ((1, 1), (0, 0), (0, 0)))
    convolved = jnp.zeros((total_rows, GROUPS, DD // GROUPS), jnp.float32)
    for offset in range(3):
        convolved = convolved + jnp.einsum(
            "pgi,gio->pgo",
            padded[offset : offset + total_rows],
            conv_w[offset],
            preferred_element_type=jnp.float32,
        )
    activated = jax.nn.gelu(row_norm(convolved.reshape(total_rows, DD)), approximate=False)
    return (lowered.astype(jnp.float32) + activated).astype(jnp.bfloat16)


def loss_kernel(hidden_ref, dec_out_ref, targets_ref, keep_ref, squares_ref, d_hidden_ref, *, scale):
    predicted = jnp.dot(hidden_ref[...], dec_out_ref[...], preferred_element_type=jnp.float32)
    mismatch = (predicted - targets_ref[...].astype(jnp.float32)) * keep_ref[...]
    squares_ref[...] = jnp.sum(mismatch * mismatch, keepdims=True)
    d_predicted = (2.0 * scale * mismatch) * keep_ref[...]
    d_hidden = lax.dot_general(
        d_predicted.astype(jnp.bfloat16),
        dec_out_ref[...],
        (((1,), (1,)), ((), ())),
        preferred_element_type=jnp.float32,
    )
    d_hidden_ref[...] = d_hidden.astype(jnp.bfloat16)


def masked_squares(hidden, dec_out, targets, keep, scale):
    rows, width = hidden.shape
    return pl.pallas_call(
        functools.partial(loss_kernel, scale=scale),
        out_shape=(
            jax.ShapeDtypeStruct((1, 1), jnp.float32),
            jax.ShapeDtypeStruct((rows, width), jnp.bfloat16),
        ),
    )(hidden, dec_out, targets, keep)


@functools.partial(jax.custom_vjp, nondiff_argnums=(4,))
def squares_of(hidden, dec_out, targets, keep, scale):
    return masked_squares(hidden, dec_out, targets, keep, scale)[0][0, 0]


def squares_of_fwd(hidden, dec_out, targets, keep, scale):
    squares, d_hidden = masked_squares(hidden, dec_out, targets, keep, scale)
    return squares[0, 0], (d_hidden, dec_out, targets, keep)


def squares_of_bwd(scale, saved, cotangent):
    d_hidden, dec_out, targets, keep = saved
    ratio = (cotangent / scale).astype(jnp.bfloat16)
    return (
        d_hidden * ratio,
        jnp.zeros_like(dec_out),
        jnp.zeros_like(targets),
        jnp.zeros_like(keep),
    )


squares_of.defvjp(squares_of_fwd, squares_of_bwd)


def copy_terms(
    visible_in,
    positions,
    targets,
    w_qkv,
    w_out,
    mask_embed,
    dec_in,
    conv_w,
    dec_out,
    projected,
    scale,
):
    total_rows = targets.shape[0]
    if projected is None:
        branch = attention_branch(visible_in, w_qkv, w_out)
    else:
        branch = attention_from(reuse_rows(visible_in, w_qkv, projected), w_out)
    visible_out = (visible_in.astype(jnp.float32) + branch).astype(jnp.bfloat16)
    hidden = decoder_output(
        visible_out, positions, total_rows, mask_embed, dec_in, conv_w, dec_out
    )
    slot_ids = jnp.arange(total_rows, dtype=jnp.int32)
    seen = jnp.max((slot_ids[:, None] == positions[None, :]).astype(jnp.float32), axis=1)
    return squares_of(hidden, dec_out, targets, (1.0 - seen)[:, None], scale)


def ring_gather(values, group_size):
    parts = [values]
    for shift in range(1, group_size):
        pairs = [(source, (source - shift) % group_size) for source in range(group_size)]
        parts.append(lax.ppermute(values, "mask", pairs))
    return parts


def in_mask_order(parts, own_index):
    group_size = len(parts)
    blocks = []
    for block in range(group_size):
        slot = (block - own_index) % group_size
        chosen = parts[0]
        for other in range(1, group_size):
            chosen = jnp.where(slot == other, parts[other], chosen)
        blocks.append(chosen)
    return jnp.concatenate(blocks, axis=0)


def split_teacher(embedded, w_qkv, w_out, own_index, group_size):
    total_rows = embedded.shape[0]
    head_dim = D // HEADS
    heads_here = HEADS // group_size
    head_width = heads_here * head_dim
    normed = row_norm(embedded.astype(jnp.float32)).astype(jnp.bfloat16)
    own_cols = lax.dynamic_slice_in_dim(
        w_qkv.reshape(D, 3, D), own_index * head_width, head_width, 2
    )
    projected = jnp.einsum(
        "sd,dtw->stw", normed, own_cols, preferred_element_type=jnp.float32
    ).astype(jnp.bfloat16)
    context = split_project(projected.reshape(total_rows, 3, heads_here, head_dim))
    out_rows = lax.dynamic_slice_in_dim(w_out, own_index * head_width, head_width, 0)
    partial_value = jnp.dot(
        context.reshape(total_rows, head_width), out_rows, preferred_element_type=jnp.float32
    )
    return lax.psum(partial_value.astype(jnp.bfloat16), "mask").astype(jnp.float32)


def on_device(patches, visible_index, embed_w, w_qkv, w_out, mask_embed, dec_in, conv_w, dec_out):
    tok_rows = patches.shape[0]
    group_size = lax.axis_size("mask")
    own_index = lax.axis_index("mask")
    copies = visible_index.shape[0]
    visible_count = visible_index.shape[1]
    total_rows = tok_rows * group_size
    col_width = patches.shape[1] // group_size
    positions = lax.dynamic_index_in_dim(visible_index, own_index, 0, keepdims=False)
    clip_pixels = in_mask_order(ring_gather(patches, group_size), own_index)
    embedded = jnp.dot(clip_pixels, embed_w, preferred_element_type=jnp.float32).astype(
        jnp.bfloat16
    )
    clip_ids = jnp.arange(total_rows, dtype=jnp.int32)
    own_picks = (positions[:, None] == clip_ids[None, :]).astype(jnp.bfloat16)
    visible_in = jnp.dot(own_picks, embedded, preferred_element_type=jnp.float32).astype(
        jnp.bfloat16
    )
    if HEADS * total_rows * total_rows * 4 <= (1 << 24):
        clip_projected = project_rows(embedded, w_qkv)
        branch = attention_from(clip_projected, w_out)
        visible_projected = jnp.dot(
            own_picks, clip_projected, preferred_element_type=jnp.float32
        ).astype(jnp.bfloat16)
    else:
        branch = split_teacher(embedded, w_qkv, w_out, own_index, group_size)
        visible_projected = None
    all_targets = row_norm(branch).astype(jnp.bfloat16)

    def objective(rows_in):
        return copy_terms(
            rows_in,
            positions,
            all_targets,
            w_qkv,
            w_out,
            mask_embed,
            dec_in,
            conv_w,
            dec_out,
            visible_projected,
            factor,
        )

    factor = 0.5 / math.sqrt(copies * visible_count)
    squares, pullback = jax.vjp(objective, visible_in)
    (grad_in,) = pullback(jnp.ones_like(squares) * factor)
    copy_loss = jnp.reshape(squares / ((total_rows - visible_count) * D), (1,))
    slot_copy = (own_index + jnp.arange(group_size, dtype=jnp.int32)) % group_size
    flat_index = visible_index[slot_copy].reshape(copies * visible_count)
    own_cols = lax.dynamic_slice_in_dim(clip_pixels, own_index * col_width, col_width, 1)
    all_picks = (flat_index[:, None] == clip_ids[None, :]).astype(jnp.bfloat16)
    gathered = jnp.dot(all_picks, own_cols, preferred_element_type=jnp.float32).astype(
        jnp.bfloat16
    )
    embed_grad = None
    for slot, rows in enumerate(ring_gather(grad_in, group_size)):
        term = jnp.einsum(
            "vc,vd->cd",
            gathered[slot * visible_count : (slot + 1) * visible_count],
            rows,
            preferred_element_type=jnp.float32,
        )
        embed_grad = term if embed_grad is None else embed_grad + term
    return (embed_grad, copy_loss)


def solution(mesh):
    placed = (P(("dp", "mask"), None), P("dp", None), P(), P(), P(), P(), P(), P(), P())
    return jax.shard_map(
        on_device,
        mesh=mesh,
        in_specs=placed,
        out_specs=(P(("dp", "mask"), None), P(("dp", "mask"))),
        check_vma=False,
    )
```

```python
import functools
import math

import jax
import numpy as np
import jax.numpy as jnp
from jax import lax
from jax.experimental import pallas as pl
from jax.sharding import PartitionSpec as P

D = 1024
HEADS = 16
DD = 768
GROUPS = 16


EPSILON = 1e-06


def row_norm(values):
    average = jnp.mean(values, axis=-1, keepdims=True)
    centred = values - average
    spread = jnp.mean(centred * centred, axis=-1, keepdims=True)
    return centred * lax.rsqrt(spread + EPSILON)


def head_norm(values):
    return values * lax.rsqrt(jnp.mean(values * values, axis=-1, keepdims=True) + EPSILON)


def mix_heads(queries, key_rows, values):
    score_scale = 1.0 / math.sqrt(queries.shape[-1])
    scores = (
        jnp.einsum("qhd,khd->hqk", queries, key_rows, preferred_element_type=jnp.float32)
        * score_scale
    )
    exponent = jnp.exp(scores)
    weights = (exponent / jnp.sum(exponent, axis=-1, keepdims=True)).astype(jnp.bfloat16)
    mixed = jnp.einsum("hqk,khd->qhd", weights, values, preferred_element_type=jnp.float32)
    return mixed.astype(jnp.bfloat16)


def split_project(projected):
    queries = head_norm(projected[:, 0].astype(jnp.float32)).astype(jnp.bfloat16)
    key_rows = head_norm(projected[:, 1].astype(jnp.float32)).astype(jnp.bfloat16)
    return mix_heads(queries, key_rows, projected[:, 2])


def project_rows(inputs, w_qkv):
    normed = row_norm(inputs.astype(jnp.float32)).astype(jnp.bfloat16)
    return jnp.dot(normed, w_qkv, preferred_element_type=jnp.float32).astype(jnp.bfloat16)


def attention_from(projected, w_out):
    row_count = projected.shape[0]
    context = split_project(projected.reshape(row_count, 3, HEADS, D // HEADS))
    return jnp.dot(context.reshape(row_count, D), w_out, preferred_element_type=jnp.float32)


def attention_branch(inputs, w_qkv, w_out):
    return attention_from(project_rows(inputs, w_qkv), w_out)


@jax.custom_vjp
def reuse_rows(inputs, w_qkv, projected):
    return projected


def reuse_rows_fwd(inputs, w_qkv, projected):
    return projected, (inputs, w_qkv)


def reuse_rows_bwd(saved, cotangent):
    inputs, w_qkv = saved
    _, pullback = jax.vjp(
        lambda rows: row_norm(rows.astype(jnp.float32)).astype(jnp.bfloat16), inputs
    )
    d_normed = jnp.dot(cotangent, w_qkv.T, preferred_element_type=jnp.float32)
    d_normed = lax.optimization_barrier(d_normed.astype(jnp.bfloat16))
    (d_inputs,) = pullback(d_normed)
    return d_inputs, jnp.zeros_like(w_qkv), jnp.zeros_like(cotangent)


reuse_rows.defvjp(reuse_rows_fwd, reuse_rows_bwd)


def decoder_output(visible_out, positions, total_rows, mask_embed, dec_in, conv_w, dec_out):
    slot_ids = jnp.arange(total_rows, dtype=jnp.int32)
    picks = (slot_ids[:, None] == positions[None, :]).astype(jnp.bfloat16)
    seen = jnp.max(picks, axis=1, keepdims=True)
    lowered_visible = jnp.dot(visible_out, dec_in, preferred_element_type=jnp.float32).astype(
        jnp.bfloat16
    )
    lowered_mask = jnp.dot(
        mask_embed[None, :], dec_in, preferred_element_type=jnp.float32
    ).astype(jnp.bfloat16)
    placed = jnp.dot(picks, lowered_visible, preferred_element_type=jnp.float32)
    lowered = jnp.where(seen > 0, placed, lowered_mask.astype(jnp.float32)).astype(jnp.bfloat16)
    grouped = lowered.reshape(total_rows, GROUPS, DD // GROUPS)
    padded = jnp.pad(grouped, ((1, 1), (0, 0), (0, 0)))
    convolved = jnp.zeros((total_rows, GROUPS, DD // GROUPS), jnp.float32)
    for offset in range(3):
        convolved = convolved + jnp.einsum(
            "pgi,gio->pgo",
            padded[offset : offset + total_rows],
            conv_w[offset],
            preferred_element_type=jnp.float32,
        )
    activated = jax.nn.gelu(row_norm(convolved.reshape(total_rows, DD)), approximate=False)
    return (lowered.astype(jnp.float32) + activated).astype(jnp.bfloat16)


def loss_kernel(hidden_ref, dec_out_ref, targets_ref, keep_ref, squares_ref, d_hidden_ref, *, scale):
    rows = hidden_ref.shape[0]
    slot_ids = lax.broadcasted_iota(jnp.int32, (rows, keep_ref.shape[1]), 0)
    seen = jnp.max((slot_ids == keep_ref[...]).astype(jnp.float32), axis=1, keepdims=True)
    keep = 1.0 - seen
    predicted = jnp.dot(hidden_ref[...], dec_out_ref[...], preferred_element_type=jnp.float32)
    mismatch = (predicted - targets_ref[...].astype(jnp.float32)) * keep
    squares_ref[...] = jnp.sum(mismatch * mismatch, keepdims=True)
    d_predicted = (2.0 * scale * mismatch) * keep
    d_hidden = lax.dot_general(
        d_predicted.astype(jnp.bfloat16),
        dec_out_ref[...],
        (((1,), (1,)), ((), ())),
        preferred_element_type=jnp.float32,
    )
    d_hidden_ref[...] = d_hidden.astype(jnp.bfloat16)


def masked_squares(hidden, dec_out, targets, keep, scale):
    rows, width = hidden.shape
    return pl.pallas_call(
        functools.partial(loss_kernel, scale=scale),
        out_shape=(
            jax.ShapeDtypeStruct((1, 1), jnp.float32),
            jax.ShapeDtypeStruct((rows, width), jnp.bfloat16),
        ),
    )(hidden, dec_out, targets, keep)


@functools.partial(jax.custom_vjp, nondiff_argnums=(4,))
def squares_of(hidden, dec_out, targets, keep, scale):
    return masked_squares(hidden, dec_out, targets, keep, scale)[0][0, 0]


def squares_of_fwd(hidden, dec_out, targets, keep, scale):
    squares, d_hidden = masked_squares(hidden, dec_out, targets, keep, scale)
    return squares[0, 0], (d_hidden, dec_out, targets, keep)


def squares_of_bwd(scale, saved, cotangent):
    d_hidden, dec_out, targets, keep = saved
    ratio = (cotangent / scale).astype(jnp.bfloat16)
    return (
        d_hidden * ratio,
        jnp.zeros_like(dec_out),
        jnp.zeros_like(targets),
        np.zeros(keep.shape, jax.dtypes.float0),
    )


squares_of.defvjp(squares_of_fwd, squares_of_bwd)


def copy_terms(
    visible_in,
    positions,
    targets,
    w_qkv,
    w_out,
    mask_embed,
    dec_in,
    conv_w,
    dec_out,
    projected,
    scale,
):
    total_rows = targets.shape[0]
    if projected is None:
        branch = attention_branch(visible_in, w_qkv, w_out)
    else:
        branch = attention_from(reuse_rows(visible_in, w_qkv, projected), w_out)
    visible_out = (visible_in.astype(jnp.float32) + branch).astype(jnp.bfloat16)
    hidden = decoder_output(
        visible_out, positions, total_rows, mask_embed, dec_in, conv_w, dec_out
    )
    return squares_of(hidden, dec_out, targets, positions[None, :], scale)


def ring_gather(values, group_size):
    parts = [values]
    for shift in range(1, group_size):
        pairs = [(source, (source - shift) % group_size) for source in range(group_size)]
        parts.append(lax.ppermute(values, "mask", pairs))
    return parts


def in_mask_order(parts, own_index):
    group_size = len(parts)
    blocks = []
    for block in range(group_size):
        slot = (block - own_index) % group_size
        chosen = parts[0]
        for other in range(1, group_size):
            chosen = jnp.where(slot == other, parts[other], chosen)
        blocks.append(chosen)
    return jnp.concatenate(blocks, axis=0)


def split_teacher(embedded, w_qkv, w_out, own_index, group_size):
    total_rows = embedded.shape[0]
    head_dim = D // HEADS
    heads_here = HEADS // group_size
    head_width = heads_here * head_dim
    normed = row_norm(embedded.astype(jnp.float32)).astype(jnp.bfloat16)
    own_cols = lax.dynamic_slice_in_dim(
        w_qkv.reshape(D, 3, D), own_index * head_width, head_width, 2
    )
    projected = jnp.einsum(
        "sd,dtw->stw", normed, own_cols, preferred_element_type=jnp.float32
    ).astype(jnp.bfloat16)
    context = split_project(projected.reshape(total_rows, 3, heads_here, head_dim))
    out_rows = lax.dynamic_slice_in_dim(w_out, own_index * head_width, head_width, 0)
    partial_value = jnp.dot(
        context.reshape(total_rows, head_width), out_rows, preferred_element_type=jnp.float32
    )
    return lax.psum(partial_value.astype(jnp.bfloat16), "mask").astype(jnp.float32)


def on_device(patches, visible_index, embed_w, w_qkv, w_out, mask_embed, dec_in, conv_w, dec_out):
    tok_rows = patches.shape[0]
    group_size = lax.axis_size("mask")
    own_index = lax.axis_index("mask")
    copies = visible_index.shape[0]
    visible_count = visible_index.shape[1]
    total_rows = tok_rows * group_size
    col_width = patches.shape[1] // group_size
    positions = lax.dynamic_index_in_dim(visible_index, own_index, 0, keepdims=False)
    clip_pixels = in_mask_order(ring_gather(patches, group_size), own_index)
    embedded = jnp.dot(clip_pixels, embed_w, preferred_element_type=jnp.float32).astype(
        jnp.bfloat16
    )
    clip_ids = jnp.arange(total_rows, dtype=jnp.int32)
    own_picks = (positions[:, None] == clip_ids[None, :]).astype(jnp.bfloat16)
    visible_in = jnp.dot(own_picks, embedded, preferred_element_type=jnp.float32).astype(
        jnp.bfloat16
    )
    if HEADS * total_rows * total_rows * 4 <= (1 << 24):
        clip_projected = project_rows(embedded, w_qkv)
        branch = attention_from(clip_projected, w_out)
        visible_projected = jnp.dot(
            own_picks, clip_projected, preferred_element_type=jnp.float32
        ).astype(jnp.bfloat16)
    else:
        branch = split_teacher(embedded, w_qkv, w_out, own_index, group_size)
        visible_projected = None
    all_targets = row_norm(branch).astype(jnp.bfloat16)

    def objective(rows_in):
        return copy_terms(
            rows_in,
            positions,
            all_targets,
            w_qkv,
            w_out,
            mask_embed,
            dec_in,
            conv_w,
            dec_out,
            visible_projected,
            factor,
        )

    factor = 0.5 / math.sqrt(copies * visible_count)
    squares, pullback = jax.vjp(objective, visible_in)
    (grad_in,) = pullback(jnp.ones_like(squares) * factor)
    copy_loss = jnp.reshape(squares / ((total_rows - visible_count) * D), (1,))
    slot_copy = (own_index + jnp.arange(group_size, dtype=jnp.int32)) % group_size
    flat_index = visible_index[slot_copy].reshape(copies * visible_count)
    own_cols = lax.dynamic_slice_in_dim(clip_pixels, own_index * col_width, col_width, 1)
    all_picks = (flat_index[:, None] == clip_ids[None, :]).astype(jnp.bfloat16)
    gathered = jnp.dot(all_picks, own_cols, preferred_element_type=jnp.float32).astype(
        jnp.bfloat16
    )
    embed_grad = jnp.einsum(
        "vc,vd->cd",
        gathered,
        jnp.concatenate(ring_gather(grad_in, group_size), axis=0),
        preferred_element_type=jnp.float32,
    )
    return (embed_grad, copy_loss)


def solution(mesh):
    placed = (P(("dp", "mask"), None), P("dp", None), P(), P(), P(), P(), P(), P(), P())
    return jax.shard_map(
        on_device,
        mesh=mesh,
        in_specs=placed,
        out_specs=(P(("dp", "mask"), None), P(("dp", "mask"))),
        check_vma=False,
    )
```

```python
import functools
import math

import jax
import jax.numpy as jnp
from jax import lax
from jax.experimental import pallas as pl
from jax.sharding import PartitionSpec as P

D = 1024
HEADS = 16
DD = 768
GROUPS = 16


EPSILON = 1e-06


def row_norm(values):
    average = jnp.mean(values, axis=-1, keepdims=True)
    centred = values - average
    spread = jnp.mean(centred * centred, axis=-1, keepdims=True)
    return centred * lax.rsqrt(spread + EPSILON)


def head_norm(values):
    return values * lax.rsqrt(jnp.mean(values * values, axis=-1, keepdims=True) + EPSILON)


def mix_heads(queries, key_rows, values):
    score_scale = 1.0 / math.sqrt(queries.shape[-1])
    scores = (
        jnp.einsum("qhd,khd->hqk", queries, key_rows, preferred_element_type=jnp.float32)
        * score_scale
    )
    exponent = jnp.exp(scores)
    weights = (exponent / jnp.sum(exponent, axis=-1, keepdims=True)).astype(jnp.bfloat16)
    mixed = jnp.einsum("hqk,khd->qhd", weights, values, preferred_element_type=jnp.float32)
    return mixed.astype(jnp.bfloat16)


def split_project(projected):
    queries = head_norm(projected[:, 0].astype(jnp.float32)).astype(jnp.bfloat16)
    key_rows = head_norm(projected[:, 1].astype(jnp.float32)).astype(jnp.bfloat16)
    return mix_heads(queries, key_rows, projected[:, 2])


def project_rows(inputs, w_qkv):
    normed = row_norm(inputs.astype(jnp.float32)).astype(jnp.bfloat16)
    return jnp.dot(normed, w_qkv, preferred_element_type=jnp.float32).astype(jnp.bfloat16)


def attention_from(projected, w_out):
    row_count = projected.shape[0]
    context = split_project(projected.reshape(row_count, 3, HEADS, D // HEADS))
    return jnp.dot(context.reshape(row_count, D), w_out, preferred_element_type=jnp.float32)


def attention_branch(inputs, w_qkv, w_out):
    return attention_from(project_rows(inputs, w_qkv), w_out)


@jax.custom_vjp
def reuse_rows(inputs, w_qkv, projected):
    return projected


def reuse_rows_fwd(inputs, w_qkv, projected):
    return projected, (inputs, w_qkv)


def reuse_rows_bwd(saved, cotangent):
    inputs, w_qkv = saved
    _, pullback = jax.vjp(
        lambda rows: row_norm(rows.astype(jnp.float32)).astype(jnp.bfloat16), inputs
    )
    d_normed = jnp.dot(cotangent, w_qkv.T, preferred_element_type=jnp.float32)
    d_normed = lax.optimization_barrier(d_normed.astype(jnp.bfloat16))
    (d_inputs,) = pullback(d_normed)
    return d_inputs, jnp.zeros_like(w_qkv), jnp.zeros_like(cotangent)


reuse_rows.defvjp(reuse_rows_fwd, reuse_rows_bwd)


def decoder_output(visible_out, positions, total_rows, mask_embed, dec_in, conv_w, dec_out):
    slot_ids = jnp.arange(total_rows, dtype=jnp.int32)
    picks = (slot_ids[:, None] == positions[None, :]).astype(jnp.bfloat16)
    unseen = 1.0 - jnp.max(picks, axis=1, keepdims=True)
    picks = jnp.concatenate([picks, unseen], axis=1)
    distinct_rows = jnp.concatenate([visible_out, mask_embed[None, :]], axis=0)
    lowered_rows = jnp.dot(distinct_rows, dec_in, preferred_element_type=jnp.float32).astype(
        jnp.bfloat16
    )
    lowered = jnp.dot(picks, lowered_rows, preferred_element_type=jnp.float32).astype(
        jnp.bfloat16
    )
    grouped = lowered.reshape(total_rows, GROUPS, DD // GROUPS)
    padded = jnp.pad(grouped, ((1, 1), (0, 0), (0, 0)))
    convolved = jnp.zeros((total_rows, GROUPS, DD // GROUPS), jnp.float32)
    for offset in range(3):
        convolved = convolved + jnp.einsum(
            "pgi,gio->pgo",
            padded[offset : offset + total_rows],
            conv_w[offset],
            preferred_element_type=jnp.float32,
        )
    activated = jax.nn.gelu(row_norm(convolved.reshape(total_rows, DD)), approximate=False)
    return (lowered.astype(jnp.float32) + activated).astype(jnp.bfloat16)


def loss_kernel(hidden_ref, dec_out_ref, targets_ref, keep_ref, squares_ref, d_hidden_ref, *, scale):
    predicted = jnp.dot(hidden_ref[...], dec_out_ref[...], preferred_element_type=jnp.float32)
    mismatch = (predicted - targets_ref[...].astype(jnp.float32)) * keep_ref[...]
    squares_ref[...] = jnp.sum(mismatch * mismatch, keepdims=True)
    d_predicted = (2.0 * scale * mismatch) * keep_ref[...]
    d_hidden = lax.dot_general(
        d_predicted.astype(jnp.bfloat16),
        dec_out_ref[...],
        (((1,), (1,)), ((), ())),
        preferred_element_type=jnp.float32,
    )
    d_hidden_ref[...] = d_hidden.astype(jnp.bfloat16)


def masked_squares(hidden, dec_out, targets, keep, scale):
    rows, width = hidden.shape
    return pl.pallas_call(
        functools.partial(loss_kernel, scale=scale),
        out_shape=(
            jax.ShapeDtypeStruct((1, 1), jnp.float32),
            jax.ShapeDtypeStruct((rows, width), jnp.bfloat16),
        ),
    )(hidden, dec_out, targets, keep)


@functools.partial(jax.custom_vjp, nondiff_argnums=(4,))
def squares_of(hidden, dec_out, targets, keep, scale):
    return masked_squares(hidden, dec_out, targets, keep, scale)[0][0, 0]


def squares_of_fwd(hidden, dec_out, targets, keep, scale):
    squares, d_hidden = masked_squares(hidden, dec_out, targets, keep, scale)
    return squares[0, 0], (d_hidden, dec_out, targets, keep)


def squares_of_bwd(scale, saved, cotangent):
    d_hidden, dec_out, targets, keep = saved
    ratio = (cotangent / scale).astype(jnp.bfloat16)
    return (
        d_hidden * ratio,
        jnp.zeros_like(dec_out),
        jnp.zeros_like(targets),
        jnp.zeros_like(keep),
    )


squares_of.defvjp(squares_of_fwd, squares_of_bwd)


def copy_terms(
    visible_in,
    positions,
    targets,
    w_qkv,
    w_out,
    mask_embed,
    dec_in,
    conv_w,
    dec_out,
    projected,
    scale,
):
    total_rows = targets.shape[0]
    if projected is None:
        branch = attention_branch(visible_in, w_qkv, w_out)
    else:
        branch = attention_from(reuse_rows(visible_in, w_qkv, projected), w_out)
    visible_out = (visible_in.astype(jnp.float32) + branch).astype(jnp.bfloat16)
    hidden = decoder_output(
        visible_out, positions, total_rows, mask_embed, dec_in, conv_w, dec_out
    )
    slot_ids = jnp.arange(total_rows, dtype=jnp.int32)
    seen = jnp.max((slot_ids[:, None] == positions[None, :]).astype(jnp.float32), axis=1)
    return squares_of(hidden, dec_out, targets, (1.0 - seen)[:, None], scale)


def ring_gather(values, group_size):
    parts = [values]
    for shift in range(1, group_size):
        pairs = [(source, (source - shift) % group_size) for source in range(group_size)]
        parts.append(lax.ppermute(values, "mask", pairs))
    return parts


def in_mask_order(parts, own_index):
    group_size = len(parts)
    blocks = []
    for block in range(group_size):
        slot = (block - own_index) % group_size
        chosen = parts[0]
        for other in range(1, group_size):
            chosen = jnp.where(slot == other, parts[other], chosen)
        blocks.append(chosen)
    return jnp.concatenate(blocks, axis=0)


def split_teacher(embedded, w_qkv, w_out, own_index, group_size):
    total_rows = embedded.shape[0]
    head_dim = D // HEADS
    heads_here = HEADS // group_size
    head_width = heads_here * head_dim
    normed = row_norm(embedded.astype(jnp.float32)).astype(jnp.bfloat16)
    own_cols = lax.dynamic_slice_in_dim(
        w_qkv.reshape(D, 3, D), own_index * head_width, head_width, 2
    )
    projected = jnp.einsum(
        "sd,dtw->stw", normed, own_cols, preferred_element_type=jnp.float32
    ).astype(jnp.bfloat16)
    context = split_project(projected.reshape(total_rows, 3, heads_here, head_dim))
    out_rows = lax.dynamic_slice_in_dim(w_out, own_index * head_width, head_width, 0)
    partial_value = jnp.dot(
        context.reshape(total_rows, head_width), out_rows, preferred_element_type=jnp.float32
    )
    return lax.psum(partial_value.astype(jnp.bfloat16), "mask").astype(jnp.float32)


def on_device(patches, visible_index, embed_w, w_qkv, w_out, mask_embed, dec_in, conv_w, dec_out):
    tok_rows = patches.shape[0]
    group_size = lax.axis_size("mask")
    own_index = lax.axis_index("mask")
    copies = visible_index.shape[0]
    visible_count = visible_index.shape[1]
    total_rows = tok_rows * group_size
    col_width = patches.shape[1] // group_size
    positions = lax.dynamic_index_in_dim(visible_index, own_index, 0, keepdims=False)
    clip_pixels = in_mask_order(ring_gather(patches, group_size), own_index)
    embedded = jnp.dot(clip_pixels, embed_w, preferred_element_type=jnp.float32).astype(
        jnp.bfloat16
    )
    clip_ids = jnp.arange(total_rows, dtype=jnp.int32)
    own_picks = (positions[:, None] == clip_ids[None, :]).astype(jnp.bfloat16)
    visible_in = jnp.dot(own_picks, embedded, preferred_element_type=jnp.float32).astype(
        jnp.bfloat16
    )
    if HEADS * total_rows * total_rows * 4 <= (1 << 24):
        clip_projected = project_rows(embedded, w_qkv)
        branch = attention_from(clip_projected, w_out)
        visible_projected = jnp.dot(
            own_picks, clip_projected, preferred_element_type=jnp.float32
        ).astype(jnp.bfloat16)
    else:
        branch = split_teacher(embedded, w_qkv, w_out, own_index, group_size)
        visible_projected = None
    all_targets = row_norm(branch).astype(jnp.bfloat16)

    def objective(rows_in):
        return copy_terms(
            rows_in,
            positions,
            all_targets,
            w_qkv,
            w_out,
            mask_embed,
            dec_in,
            conv_w,
            dec_out,
            visible_projected,
            factor,
        )

    factor = 0.5 / math.sqrt(copies * visible_count)
    squares, pullback = jax.vjp(objective, visible_in)
    (grad_in,) = pullback(jnp.ones_like(squares) * factor)
    copy_loss = jnp.reshape(squares / ((total_rows - visible_count) * D), (1,))
    slot_copy = (own_index + jnp.arange(group_size, dtype=jnp.int32)) % group_size
    flat_index = visible_index[slot_copy].reshape(copies * visible_count)
    own_cols = lax.dynamic_slice_in_dim(clip_pixels, own_index * col_width, col_width, 1)
    all_picks = (flat_index[:, None] == clip_ids[None, :]).astype(jnp.bfloat16)
    gathered = jnp.dot(all_picks, own_cols, preferred_element_type=jnp.float32).astype(
        jnp.bfloat16
    )
    embed_grad = jnp.einsum(
        "vc,vd->cd",
        gathered,
        jnp.concatenate(ring_gather(grad_in, group_size), axis=0),
        preferred_element_type=jnp.float32,
    )
    return (embed_grad, copy_loss)


def solution(mesh):
    placed = (P(("dp", "mask"), None), P("dp", None), P(), P(), P(), P(), P(), P(), P())
    return jax.shard_map(
        on_device,
        mesh=mesh,
        in_specs=placed,
        out_specs=(P(("dp", "mask"), None), P(("dp", "mask"))),
        check_vma=False,
    )
```

```python
import functools
import math

import jax
import jax.numpy as jnp
from jax import lax
from jax.experimental import pallas as pl
from jax.sharding import PartitionSpec as P

D = 1024
HEADS = 16
DD = 768
GROUPS = 16


EPSILON = 1e-06


def row_norm(values):
    average = jnp.mean(values, axis=-1, keepdims=True)
    centred = values - average
    spread = jnp.mean(centred * centred, axis=-1, keepdims=True)
    return centred * lax.rsqrt(spread + EPSILON)


def head_norm(values):
    return values * lax.rsqrt(jnp.mean(values * values, axis=-1, keepdims=True) + EPSILON)


def mix_heads(queries, key_rows, values):
    score_scale = 1.0 / math.sqrt(queries.shape[-1])
    scores = (
        jnp.einsum("qhd,khd->hqk", queries, key_rows, preferred_element_type=jnp.float32)
        * score_scale
    )
    exponent = jnp.exp(scores)
    weights = (exponent / jnp.sum(exponent, axis=-1, keepdims=True)).astype(jnp.bfloat16)
    mixed = jnp.einsum("hqk,khd->qhd", weights, values, preferred_element_type=jnp.float32)
    return mixed.astype(jnp.bfloat16)


def split_project(projected):
    queries = head_norm(projected[:, 0].astype(jnp.float32)).astype(jnp.bfloat16)
    key_rows = head_norm(projected[:, 1].astype(jnp.float32)).astype(jnp.bfloat16)
    return mix_heads(queries, key_rows, projected[:, 2])


def project_rows(inputs, w_qkv):
    normed = row_norm(inputs.astype(jnp.float32)).astype(jnp.bfloat16)
    return jnp.dot(normed, w_qkv, preferred_element_type=jnp.float32).astype(jnp.bfloat16)


def attention_from(projected, w_out):
    row_count = projected.shape[0]
    context = split_project(projected.reshape(row_count, 3, HEADS, D // HEADS))
    return jnp.dot(context.reshape(row_count, D), w_out, preferred_element_type=jnp.float32)


def attention_branch(inputs, w_qkv, w_out):
    return attention_from(project_rows(inputs, w_qkv), w_out)


@jax.custom_vjp
def reuse_rows(inputs, w_qkv, projected):
    return projected


def reuse_rows_fwd(inputs, w_qkv, projected):
    return projected, (inputs, w_qkv)


def reuse_rows_bwd(saved, cotangent):
    inputs, w_qkv = saved
    _, pullback = jax.vjp(
        lambda rows: row_norm(rows.astype(jnp.float32)).astype(jnp.bfloat16), inputs
    )
    d_normed = jnp.dot(cotangent, w_qkv.T, preferred_element_type=jnp.float32)
    d_normed = lax.optimization_barrier(d_normed.astype(jnp.bfloat16))
    (d_inputs,) = pullback(d_normed)
    return d_inputs, jnp.zeros_like(w_qkv), jnp.zeros_like(cotangent)


reuse_rows.defvjp(reuse_rows_fwd, reuse_rows_bwd)


def decoder_output(visible_out, positions, total_rows, mask_embed, dec_in, conv_w, dec_out):
    slot_ids = jnp.arange(total_rows, dtype=jnp.int32)
    picks = (slot_ids[:, None] == positions[None, :]).astype(jnp.bfloat16)
    seen = jnp.max(picks, axis=1, keepdims=True)
    lowered_visible = jnp.dot(visible_out, dec_in, preferred_element_type=jnp.float32).astype(
        jnp.bfloat16
    )
    lowered_mask = jnp.dot(
        mask_embed[None, :], dec_in, preferred_element_type=jnp.float32
    ).astype(jnp.bfloat16)
    placed = jnp.dot(picks, lowered_visible, preferred_element_type=jnp.float32)
    lowered = jnp.where(seen > 0, placed, lowered_mask.astype(jnp.float32)).astype(jnp.bfloat16)
    grouped = lowered.reshape(total_rows, GROUPS, DD // GROUPS)
    padded = jnp.pad(grouped, ((1, 1), (0, 0), (0, 0)))
    convolved = jnp.zeros((total_rows, GROUPS, DD // GROUPS), jnp.float32)
    for offset in range(3):
        convolved = convolved + jnp.einsum(
            "pgi,gio->pgo",
            padded[offset : offset + total_rows],
            conv_w[offset],
            preferred_element_type=jnp.float32,
        )
    activated = jax.nn.gelu(row_norm(convolved.reshape(total_rows, DD)), approximate=False)
    return (lowered.astype(jnp.float32) + activated).astype(jnp.bfloat16)


def loss_kernel(hidden_ref, dec_out_ref, targets_ref, keep_ref, squares_ref, d_hidden_ref, *, scale):
    predicted = jnp.dot(hidden_ref[...], dec_out_ref[...], preferred_element_type=jnp.float32)
    mismatch = (predicted - targets_ref[...].astype(jnp.float32)) * keep_ref[...]
    squares_ref[...] = jnp.sum(mismatch * mismatch, keepdims=True)
    d_predicted = (2.0 * scale * mismatch) * keep_ref[...]
    d_hidden = lax.dot_general(
        d_predicted.astype(jnp.bfloat16),
        dec_out_ref[...],
        (((1,), (1,)), ((), ())),
        preferred_element_type=jnp.float32,
    )
    d_hidden_ref[...] = d_hidden.astype(jnp.bfloat16)


def masked_squares(hidden, dec_out, targets, keep, scale):
    rows, width = hidden.shape
    return pl.pallas_call(
        functools.partial(loss_kernel, scale=scale),
        out_shape=(
            jax.ShapeDtypeStruct((1, 1), jnp.float32),
            jax.ShapeDtypeStruct((rows, width), jnp.bfloat16),
        ),
    )(hidden, dec_out, targets, keep)


@functools.partial(jax.custom_vjp, nondiff_argnums=(4,))
def squares_of(hidden, dec_out, targets, keep, scale):
    return masked_squares(hidden, dec_out, targets, keep, scale)[0][0, 0]


def squares_of_fwd(hidden, dec_out, targets, keep, scale):
    squares, d_hidden = masked_squares(hidden, dec_out, targets, keep, scale)
    return squares[0, 0], (d_hidden, dec_out, targets, keep)


def squares_of_bwd(scale, saved, cotangent):
    d_hidden, dec_out, targets, keep = saved
    ratio = (cotangent / scale).astype(jnp.bfloat16)
    return (
        d_hidden * ratio,
        jnp.zeros_like(dec_out),
        jnp.zeros_like(targets),
        jnp.zeros_like(keep),
    )


squares_of.defvjp(squares_of_fwd, squares_of_bwd)


def copy_terms(
    visible_in,
    positions,
    targets,
    w_qkv,
    w_out,
    mask_embed,
    dec_in,
    conv_w,
    dec_out,
    projected,
    scale,
):
    total_rows = targets.shape[0]
    if projected is None:
        branch = attention_branch(visible_in, w_qkv, w_out)
    else:
        branch = attention_from(reuse_rows(visible_in, w_qkv, projected), w_out)
    visible_out = (visible_in.astype(jnp.float32) + branch).astype(jnp.bfloat16)
    hidden = decoder_output(
        visible_out, positions, total_rows, mask_embed, dec_in, conv_w, dec_out
    )
    slot_ids = jnp.arange(total_rows, dtype=jnp.int32)
    seen = jnp.max((slot_ids[:, None] == positions[None, :]).astype(jnp.float32), axis=1)
    return squares_of(hidden, dec_out, targets, (1.0 - seen)[:, None], scale)


def ring_gather(values, group_size):
    parts = [values]
    for shift in range(1, group_size):
        pairs = [(source, (source - shift) % group_size) for source in range(group_size)]
        parts.append(lax.ppermute(values, "mask", pairs))
    return parts


def in_mask_order(parts, own_index):
    group_size = len(parts)
    blocks = []
    for block in range(group_size):
        slot = (block - own_index) % group_size
        chosen = parts[0]
        for other in range(1, group_size):
            chosen = jnp.where(slot == other, parts[other], chosen)
        blocks.append(chosen)
    return jnp.concatenate(blocks, axis=0)


def split_teacher(embedded, w_qkv, w_out, own_index, group_size):
    total_rows = embedded.shape[0]
    head_dim = D // HEADS
    heads_here = HEADS // group_size
    head_width = heads_here * head_dim
    normed = row_norm(embedded.astype(jnp.float32)).astype(jnp.bfloat16)
    own_cols = lax.dynamic_slice_in_dim(
        w_qkv.reshape(D, 3, D), own_index * head_width, head_width, 2
    )
    projected = jnp.einsum(
        "sd,dtw->stw", normed, own_cols, preferred_element_type=jnp.float32
    ).astype(jnp.bfloat16)
    context = split_project(projected.reshape(total_rows, 3, heads_here, head_dim))
    out_rows = lax.dynamic_slice_in_dim(w_out, own_index * head_width, head_width, 0)
    partial_value = jnp.dot(
        context.reshape(total_rows, head_width), out_rows, preferred_element_type=jnp.float32
    )
    return lax.psum(partial_value.astype(jnp.bfloat16), "mask").astype(jnp.float32)


def on_device(patches, visible_index, embed_w, w_qkv, w_out, mask_embed, dec_in, conv_w, dec_out):
    tok_rows = patches.shape[0]
    group_size = lax.axis_size("mask")
    own_index = lax.axis_index("mask")
    copies = visible_index.shape[0]
    visible_count = visible_index.shape[1]
    total_rows = tok_rows * group_size
    col_width = patches.shape[1] // group_size
    positions = lax.dynamic_index_in_dim(visible_index, own_index, 0, keepdims=False)
    clip_pixels = in_mask_order(ring_gather(patches, group_size), own_index)
    embedded = jnp.dot(clip_pixels, embed_w, preferred_element_type=jnp.float32).astype(
        jnp.bfloat16
    )
    clip_ids = jnp.arange(total_rows, dtype=jnp.int32)
    own_picks = (positions[:, None] == clip_ids[None, :]).astype(jnp.bfloat16)
    visible_in = jnp.dot(own_picks, embedded, preferred_element_type=jnp.float32).astype(
        jnp.bfloat16
    )
    if HEADS * total_rows * total_rows * 4 <= (1 << 24):
        clip_projected = project_rows(embedded, w_qkv)
        branch = attention_from(clip_projected, w_out)
        visible_projected = jnp.dot(
            own_picks, clip_projected, preferred_element_type=jnp.float32
        ).astype(jnp.bfloat16)
    else:
        branch = split_teacher(embedded, w_qkv, w_out, own_index, group_size)
        visible_projected = None
    all_targets = row_norm(branch).astype(jnp.bfloat16)

    def objective(rows_in):
        return copy_terms(
            rows_in,
            positions,
            all_targets,
            w_qkv,
            w_out,
            mask_embed,
            dec_in,
            conv_w,
            dec_out,
            visible_projected,
            factor,
        )

    factor = 0.5 / math.sqrt(copies * visible_count)
    squares, pullback = jax.vjp(objective, visible_in)
    (grad_in,) = pullback(jnp.ones_like(squares) * factor)
    copy_loss = jnp.reshape(squares / ((total_rows - visible_count) * D), (1,))
    doubled_index = jnp.concatenate([visible_index, visible_index], axis=0)
    flat_index = lax.dynamic_slice_in_dim(doubled_index, own_index, copies, 0).reshape(
        copies * visible_count
    )
    own_cols = lax.dynamic_slice_in_dim(clip_pixels, own_index * col_width, col_width, 1)
    all_picks = (flat_index[:, None] == clip_ids[None, :]).astype(jnp.bfloat16)
    gathered = jnp.dot(all_picks, own_cols, preferred_element_type=jnp.float32).astype(
        jnp.bfloat16
    )
    embed_grad = jnp.einsum(
        "vc,vd->cd",
        gathered,
        jnp.concatenate(ring_gather(grad_in, group_size), axis=0),
        preferred_element_type=jnp.float32,
    )
    return (embed_grad, copy_loss)


def solution(mesh):
    placed = (P(("dp", "mask"), None), P("dp", None), P(), P(), P(), P(), P(), P(), P())
    return jax.shard_map(
        on_device,
        mesh=mesh,
        in_specs=placed,
        out_specs=(P(("dp", "mask"), None), P(("dp", "mask"))),
        check_vma=False,
    )
```

```python
import functools
import math

import jax
import jax.numpy as jnp
from jax import lax
from jax.experimental import pallas as pl
from jax.sharding import PartitionSpec as P

D = 1024
HEADS = 16
DD = 768
GROUPS = 16


EPSILON = 1e-06


def row_norm(values):
    average = jnp.mean(values, axis=-1, keepdims=True)
    centred = values - average
    spread = jnp.mean(centred * centred, axis=-1, keepdims=True)
    return centred * lax.rsqrt(spread + EPSILON)


def head_norm(values):
    return values * lax.rsqrt(jnp.mean(values * values, axis=-1, keepdims=True) + EPSILON)


def mix_heads(queries, key_rows, values):
    score_scale = 1.0 / math.sqrt(queries.shape[-1])
    scores = (
        jnp.einsum("qhd,khd->hqk", queries, key_rows, preferred_element_type=jnp.float32)
        * score_scale
    )
    exponent = jnp.exp(scores)
    weights = (exponent / jnp.sum(exponent, axis=-1, keepdims=True)).astype(jnp.bfloat16)
    mixed = jnp.einsum("hqk,khd->qhd", weights, values, preferred_element_type=jnp.float32)
    return mixed.astype(jnp.bfloat16)


def split_project(projected):
    queries = head_norm(projected[:, 0].astype(jnp.float32)).astype(jnp.bfloat16)
    key_rows = head_norm(projected[:, 1].astype(jnp.float32)).astype(jnp.bfloat16)
    return mix_heads(queries, key_rows, projected[:, 2])


def project_rows(inputs, w_qkv):
    normed = row_norm(inputs.astype(jnp.float32)).astype(jnp.bfloat16)
    return jnp.dot(normed, w_qkv, preferred_element_type=jnp.float32).astype(jnp.bfloat16)


def attention_from(projected, w_out):
    row_count = projected.shape[0]
    context = split_project(projected.reshape(row_count, 3, HEADS, D // HEADS))
    return jnp.dot(context.reshape(row_count, D), w_out, preferred_element_type=jnp.float32)


def attention_branch(inputs, w_qkv, w_out):
    return attention_from(project_rows(inputs, w_qkv), w_out)


@jax.custom_vjp
def reuse_rows(inputs, w_qkv, projected):
    return projected


def reuse_rows_fwd(inputs, w_qkv, projected):
    return projected, (inputs, w_qkv)


def reuse_rows_bwd(saved, cotangent):
    inputs, w_qkv = saved
    _, pullback = jax.vjp(
        lambda rows: row_norm(rows.astype(jnp.float32)).astype(jnp.bfloat16), inputs
    )
    d_normed = jnp.dot(cotangent, w_qkv.T, preferred_element_type=jnp.float32)
    d_normed = lax.optimization_barrier(d_normed.astype(jnp.bfloat16))
    (d_inputs,) = pullback(d_normed)
    return d_inputs, jnp.zeros_like(w_qkv), jnp.zeros_like(cotangent)


reuse_rows.defvjp(reuse_rows_fwd, reuse_rows_bwd)


def decoder_output(visible_out, positions, total_rows, mask_embed, dec_in, conv_w, dec_out):
    slot_ids = jnp.arange(total_rows, dtype=jnp.int32)
    picks = (slot_ids[:, None] == positions[None, :]).astype(jnp.bfloat16)
    seen = jnp.max(picks, axis=1, keepdims=True)
    lowered_visible = jnp.dot(visible_out, dec_in, preferred_element_type=jnp.float32).astype(
        jnp.bfloat16
    )
    lowered_mask = jnp.dot(
        mask_embed[None, :], dec_in, preferred_element_type=jnp.float32
    ).astype(jnp.bfloat16)
    placed = jnp.dot(picks, lowered_visible, preferred_element_type=jnp.float32)
    lowered = jnp.where(seen > 0, placed, lowered_mask.astype(jnp.float32)).astype(jnp.bfloat16)
    grouped = lowered.reshape(total_rows, GROUPS, DD // GROUPS)
    padded = jnp.pad(grouped, ((1, 1), (0, 0), (0, 0)))
    convolved = jnp.zeros((total_rows, GROUPS, DD // GROUPS), jnp.float32)
    for offset in range(3):
        convolved = convolved + jnp.einsum(
            "pgi,gio->pgo",
            padded[offset : offset + total_rows],
            conv_w[offset],
            preferred_element_type=jnp.float32,
        )
    activated = jax.nn.gelu(row_norm(convolved.reshape(total_rows, DD)), approximate=False)
    return (lowered.astype(jnp.float32) + activated).astype(jnp.bfloat16)


def loss_kernel(hidden_ref, dec_out_ref, targets_ref, keep_ref, squares_ref, d_hidden_ref, *, scale):
    predicted = jnp.dot(hidden_ref[...], dec_out_ref[...], preferred_element_type=jnp.float32)
    mismatch = (predicted - targets_ref[...].astype(jnp.float32)) * keep_ref[...]
    squares_ref[...] = jnp.sum(mismatch * mismatch, keepdims=True)
    d_predicted = (2.0 * scale * mismatch) * keep_ref[...]
    d_hidden = lax.dot_general(
        d_predicted.astype(jnp.bfloat16),
        dec_out_ref[...],
        (((1,), (1,)), ((), ())),
        preferred_element_type=jnp.float32,
    )
    d_hidden_ref[...] = d_hidden.astype(jnp.bfloat16)


def masked_squares(hidden, dec_out, targets, keep, scale):
    rows, width = hidden.shape
    return pl.pallas_call(
        functools.partial(loss_kernel, scale=scale),
        out_shape=(
            jax.ShapeDtypeStruct((1, 1), jnp.float32),
            jax.ShapeDtypeStruct((rows, width), jnp.bfloat16),
        ),
    )(hidden, dec_out, targets, keep)


@functools.partial(jax.custom_vjp, nondiff_argnums=(4,))
def squares_of(hidden, dec_out, targets, keep, scale):
    return masked_squares(hidden, dec_out, targets, keep, scale)[0][0, 0]


def squares_of_fwd(hidden, dec_out, targets, keep, scale):
    squares, d_hidden = masked_squares(hidden, dec_out, targets, keep, scale)
    return squares[0, 0], (d_hidden, dec_out, targets, keep)


def squares_of_bwd(scale, saved, cotangent):
    d_hidden, dec_out, targets, keep = saved
    ratio = (cotangent / scale).astype(jnp.bfloat16)
    return (
        d_hidden * ratio,
        jnp.zeros_like(dec_out),
        jnp.zeros_like(targets),
        jnp.zeros_like(keep),
    )


squares_of.defvjp(squares_of_fwd, squares_of_bwd)


def copy_terms(
    visible_in,
    positions,
    targets,
    w_qkv,
    w_out,
    mask_embed,
    dec_in,
    conv_w,
    dec_out,
    projected,
    scale,
):
    total_rows = targets.shape[0]
    if projected is None:
        branch = attention_branch(visible_in, w_qkv, w_out)
    else:
        branch = attention_from(reuse_rows(visible_in, w_qkv, projected), w_out)
    visible_out = (visible_in.astype(jnp.float32) + branch).astype(jnp.bfloat16)
    hidden = decoder_output(
        visible_out, positions, total_rows, mask_embed, dec_in, conv_w, dec_out
    )
    slot_ids = jnp.arange(total_rows, dtype=jnp.int32)
    seen = jnp.max((slot_ids[:, None] == positions[None, :]).astype(jnp.float32), axis=1)
    return squares_of(hidden, dec_out, targets, (1.0 - seen)[:, None], scale)


def ring_gather(values, group_size):
    parts = [values]
    for shift in range(1, group_size):
        pairs = [(source, (source - shift) % group_size) for source in range(group_size)]
        parts.append(lax.ppermute(values, "mask", pairs))
    return parts


def in_mask_order(parts, own_index):
    group_size = len(parts)
    blocks = []
    for block in range(group_size):
        slot = (block - own_index) % group_size
        chosen = parts[0]
        for other in range(1, group_size):
            chosen = jnp.where(slot == other, parts[other], chosen)
        blocks.append(chosen)
    return jnp.concatenate(blocks, axis=0)


def split_teacher(embedded, w_qkv, w_out, own_index, group_size):
    total_rows = embedded.shape[0]
    head_dim = D // HEADS
    heads_here = HEADS // group_size
    head_width = heads_here * head_dim
    normed = row_norm(embedded.astype(jnp.float32)).astype(jnp.bfloat16)
    own_cols = lax.dynamic_slice_in_dim(
        w_qkv.reshape(D, 3, D), own_index * head_width, head_width, 2
    )
    projected = jnp.einsum(
        "sd,dtw->stw", normed, own_cols, preferred_element_type=jnp.float32
    ).astype(jnp.bfloat16)
    context = split_project(projected.reshape(total_rows, 3, heads_here, head_dim))
    out_rows = lax.dynamic_slice_in_dim(w_out, own_index * head_width, head_width, 0)
    partial_value = jnp.dot(
        context.reshape(total_rows, head_width), out_rows, preferred_element_type=jnp.float32
    )
    return lax.psum(partial_value.astype(jnp.bfloat16), "mask").astype(jnp.float32)


def on_device(patches, visible_index, embed_w, w_qkv, w_out, mask_embed, dec_in, conv_w, dec_out):
    tok_rows = patches.shape[0]
    group_size = lax.axis_size("mask")
    own_index = lax.axis_index("mask")
    copies = visible_index.shape[0]
    visible_count = visible_index.shape[1]
    total_rows = tok_rows * group_size
    col_width = patches.shape[1] // group_size
    positions = lax.dynamic_index_in_dim(visible_index, own_index, 0, keepdims=False)
    clip_pixels = in_mask_order(ring_gather(patches, group_size), own_index)
    embedded = jnp.dot(clip_pixels, embed_w, preferred_element_type=jnp.float32).astype(
        jnp.bfloat16
    )
    clip_ids = jnp.arange(total_rows, dtype=jnp.int32)
    own_picks = (positions[:, None] == clip_ids[None, :]).astype(jnp.bfloat16)
    visible_in = jnp.dot(own_picks, embedded, preferred_element_type=jnp.float32).astype(
        jnp.bfloat16
    )
    if HEADS * total_rows * total_rows * 4 <= (1 << 24):
        clip_projected = project_rows(embedded, w_qkv)
        branch = attention_from(clip_projected, w_out)
        visible_projected = jnp.dot(
            own_picks, clip_projected, preferred_element_type=jnp.float32
        ).astype(jnp.bfloat16)
    else:
        branch = split_teacher(embedded, w_qkv, w_out, own_index, group_size)
        visible_projected = None
    all_targets = row_norm(branch).astype(jnp.bfloat16)

    def objective(rows_in):
        return copy_terms(
            rows_in,
            positions,
            all_targets,
            w_qkv,
            w_out,
            mask_embed,
            dec_in,
            conv_w,
            dec_out,
            visible_projected,
            factor,
        )

    factor = 0.5 / math.sqrt(copies * visible_count)
    squares, pullback = jax.vjp(objective, visible_in)
    (grad_in,) = pullback(jnp.ones_like(squares) * factor)
    copy_loss = jnp.reshape(squares / ((total_rows - visible_count) * D), (1,))
    doubled_index = jnp.concatenate([visible_index, visible_index], axis=0)
    flat_index = lax.dynamic_slice_in_dim(doubled_index, own_index, copies, 0).reshape(
        copies * visible_count
    )
    own_cols = lax.dynamic_slice_in_dim(clip_pixels, own_index * col_width, col_width, 1)
    all_picks = (flat_index[:, None] == clip_ids[None, :]).astype(jnp.bfloat16)
    gathered_t = jnp.einsum(
        "sc,vs->cv", own_cols, all_picks, preferred_element_type=jnp.float32
    ).astype(jnp.bfloat16)
    embed_grad = jnp.dot(
        gathered_t,
        jnp.concatenate(ring_gather(grad_in, group_size), axis=0),
        preferred_element_type=jnp.float32,
    )
    return (embed_grad, copy_loss)


def solution(mesh):
    placed = (P(("dp", "mask"), None), P("dp", None), P(), P(), P(), P(), P(), P(), P())
    return jax.shard_map(
        on_device,
        mesh=mesh,
        in_specs=placed,
        out_specs=(P(("dp", "mask"), None), P(("dp", "mask"))),
        check_vma=False,
    )
```

```python
import functools
import math

import jax
import jax.numpy as jnp
from jax import lax
from jax.experimental import pallas as pl
from jax.sharding import PartitionSpec as P

D = 1024
HEADS = 16
DD = 768
GROUPS = 16


EPSILON = 1e-06


def row_norm(values):
    average = jnp.mean(values, axis=-1, keepdims=True)
    centred = values - average
    spread = jnp.mean(centred * centred, axis=-1, keepdims=True)
    return centred * lax.rsqrt(spread + EPSILON)


def head_norm(values):
    return values * lax.rsqrt(jnp.mean(values * values, axis=-1, keepdims=True) + EPSILON)


def mix_heads(queries, key_rows, values):
    score_scale = 1.0 / math.sqrt(queries.shape[-1])
    scores = (
        jnp.einsum("qhd,khd->hqk", queries, key_rows, preferred_element_type=jnp.float32)
        * score_scale
    )
    exponent = jnp.exp(scores)
    weights = (exponent / jnp.sum(exponent, axis=-1, keepdims=True)).astype(jnp.bfloat16)
    mixed = jnp.einsum("hqk,khd->qhd", weights, values, preferred_element_type=jnp.float32)
    return mixed.astype(jnp.bfloat16)


def split_project(projected):
    queries = head_norm(projected[:, 0].astype(jnp.float32)).astype(jnp.bfloat16)
    key_rows = head_norm(projected[:, 1].astype(jnp.float32)).astype(jnp.bfloat16)
    return mix_heads(queries, key_rows, projected[:, 2])


def project_rows(inputs, w_qkv):
    normed = row_norm(inputs.astype(jnp.float32)).astype(jnp.bfloat16)
    return jnp.dot(normed, w_qkv, preferred_element_type=jnp.float32).astype(jnp.bfloat16)


def attention_from(projected, w_out):
    row_count = projected.shape[0]
    context = split_project(projected.reshape(row_count, 3, HEADS, D // HEADS))
    return jnp.dot(context.reshape(row_count, D), w_out, preferred_element_type=jnp.float32)


def attention_branch(inputs, w_qkv, w_out):
    return attention_from(project_rows(inputs, w_qkv), w_out)


@jax.custom_vjp
def reuse_rows(inputs, w_qkv, projected):
    return projected


def reuse_rows_fwd(inputs, w_qkv, projected):
    return projected, (inputs, w_qkv)


def reuse_rows_bwd(saved, cotangent):
    inputs, w_qkv = saved
    _, pullback = jax.vjp(
        lambda rows: row_norm(rows.astype(jnp.float32)).astype(jnp.bfloat16), inputs
    )
    d_normed = jnp.dot(cotangent, w_qkv.T, preferred_element_type=jnp.float32)
    d_normed = lax.optimization_barrier(d_normed.astype(jnp.bfloat16))
    (d_inputs,) = pullback(d_normed)
    return d_inputs, jnp.zeros_like(w_qkv), jnp.zeros_like(cotangent)


reuse_rows.defvjp(reuse_rows_fwd, reuse_rows_bwd)


def decoder_output(visible_out, positions, total_rows, mask_embed, dec_in, conv_w, dec_out):
    slot_ids = jnp.arange(total_rows, dtype=jnp.int32)
    picks = (slot_ids[:, None] == positions[None, :]).astype(jnp.bfloat16)
    seen = jnp.max(picks, axis=1, keepdims=True)
    lowered_visible = jnp.dot(visible_out, dec_in, preferred_element_type=jnp.float32).astype(
        jnp.bfloat16
    )
    lowered_mask = jnp.dot(
        mask_embed[None, :], dec_in, preferred_element_type=jnp.float32
    ).astype(jnp.bfloat16)
    placed = jnp.dot(picks, lowered_visible, preferred_element_type=jnp.float32)
    lowered = jnp.where(seen > 0, placed, lowered_mask.astype(jnp.float32)).astype(jnp.bfloat16)
    grouped = lowered.reshape(total_rows, GROUPS, DD // GROUPS)
    padded = jnp.pad(grouped, ((1, 1), (0, 0), (0, 0)))
    convolved = jnp.zeros((total_rows, GROUPS, DD // GROUPS), jnp.float32)
    for offset in range(3):
        convolved = convolved + jnp.einsum(
            "pgi,gio->pgo",
            padded[offset : offset + total_rows],
            conv_w[offset],
            preferred_element_type=jnp.float32,
        )
    activated = jax.nn.gelu(row_norm(convolved.reshape(total_rows, DD)), approximate=False)
    return (lowered.astype(jnp.float32) + activated).astype(jnp.bfloat16)


def loss_kernel(hidden_ref, dec_out_ref, targets_ref, keep_ref, squares_ref, d_hidden_ref, *, scale):
    predicted = jnp.dot(hidden_ref[...], dec_out_ref[...], preferred_element_type=jnp.float32)
    mismatch = (predicted - targets_ref[...].astype(jnp.float32)) * keep_ref[...]
    squares_ref[...] = jnp.sum(mismatch * mismatch, keepdims=True)
    d_predicted = (2.0 * scale * mismatch) * keep_ref[...]
    d_hidden = lax.dot_general(
        d_predicted.astype(jnp.bfloat16),
        dec_out_ref[...],
        (((1,), (1,)), ((), ())),
        preferred_element_type=jnp.float32,
    )
    d_hidden_ref[...] = d_hidden.astype(jnp.bfloat16)


def masked_squares(hidden, dec_out, targets, keep, scale):
    rows, width = hidden.shape
    return pl.pallas_call(
        functools.partial(loss_kernel, scale=scale),
        out_shape=(
            jax.ShapeDtypeStruct((1, 1), jnp.float32),
            jax.ShapeDtypeStruct((rows, width), jnp.bfloat16),
        ),
    )(hidden, dec_out, targets, keep)


@functools.partial(jax.custom_vjp, nondiff_argnums=(4,))
def squares_of(hidden, dec_out, targets, keep, scale):
    return masked_squares(hidden, dec_out, targets, keep, scale)[0][0, 0]


def squares_of_fwd(hidden, dec_out, targets, keep, scale):
    squares, d_hidden = masked_squares(hidden, dec_out, targets, keep, scale)
    return squares[0, 0], (d_hidden, dec_out, targets, keep)


def squares_of_bwd(scale, saved, cotangent):
    d_hidden, dec_out, targets, keep = saved
    ratio = (cotangent / scale).astype(jnp.bfloat16)
    return (
        d_hidden * ratio,
        jnp.zeros_like(dec_out),
        jnp.zeros_like(targets),
        jnp.zeros_like(keep),
    )


squares_of.defvjp(squares_of_fwd, squares_of_bwd)


def copy_terms(
    visible_in,
    positions,
    targets,
    w_qkv,
    w_out,
    mask_embed,
    dec_in,
    conv_w,
    dec_out,
    projected,
    scale,
):
    total_rows = targets.shape[0]
    if projected is None:
        branch = attention_branch(visible_in, w_qkv, w_out)
    else:
        branch = attention_from(reuse_rows(visible_in, w_qkv, projected), w_out)
    visible_out = (visible_in.astype(jnp.float32) + branch).astype(jnp.bfloat16)
    hidden = decoder_output(
        visible_out, positions, total_rows, mask_embed, dec_in, conv_w, dec_out
    )
    slot_ids = jnp.arange(total_rows, dtype=jnp.int32)
    seen = jnp.max((slot_ids[:, None] == positions[None, :]).astype(jnp.float32), axis=1)
    return squares_of(hidden, dec_out, targets, (1.0 - seen)[:, None], scale)


def ring_gather(values, group_size):
    parts = [values]
    for shift in range(1, group_size):
        pairs = [(source, (source - shift) % group_size) for source in range(group_size)]
        parts.append(lax.ppermute(values, "mask", pairs))
    return parts


def in_mask_order(parts, own_index):
    group_size = len(parts)
    blocks = []
    for block in range(group_size):
        slot = (block - own_index) % group_size
        chosen = parts[0]
        for other in range(1, group_size):
            chosen = jnp.where(slot == other, parts[other], chosen)
        blocks.append(chosen)
    return jnp.concatenate(blocks, axis=0)


def split_teacher(embedded, w_qkv, w_out, own_index, group_size):
    total_rows = embedded.shape[0]
    head_dim = D // HEADS
    heads_here = HEADS // group_size
    head_width = heads_here * head_dim
    normed = row_norm(embedded.astype(jnp.float32)).astype(jnp.bfloat16)
    own_cols = lax.dynamic_slice_in_dim(
        w_qkv.reshape(D, 3, D), own_index * head_width, head_width, 2
    )
    projected = jnp.einsum(
        "sd,dtw->stw", normed, own_cols, preferred_element_type=jnp.float32
    ).astype(jnp.bfloat16)
    context = split_project(projected.reshape(total_rows, 3, heads_here, head_dim))
    out_rows = lax.dynamic_slice_in_dim(w_out, own_index * head_width, head_width, 0)
    partial_value = jnp.dot(
        context.reshape(total_rows, head_width), out_rows, preferred_element_type=jnp.float32
    )
    return lax.psum(partial_value.astype(jnp.bfloat16), "mask").astype(jnp.float32)


def on_device(patches, visible_index, embed_w, w_qkv, w_out, mask_embed, dec_in, conv_w, dec_out):
    tok_rows = patches.shape[0]
    group_size = lax.axis_size("mask")
    own_index = lax.axis_index("mask")
    copies = visible_index.shape[0]
    visible_count = visible_index.shape[1]
    total_rows = tok_rows * group_size
    col_width = patches.shape[1] // group_size
    doubled_index = jnp.concatenate([visible_index, visible_index], axis=0)
    slot_index = lax.dynamic_slice_in_dim(doubled_index, own_index, copies, 0)
    positions = slot_index[0]
    clip_pixels = in_mask_order(ring_gather(patches, group_size), own_index)
    embedded = jnp.dot(clip_pixels, embed_w, preferred_element_type=jnp.float32).astype(
        jnp.bfloat16
    )
    clip_ids = jnp.arange(total_rows, dtype=jnp.int32)
    own_picks = (positions[:, None] == clip_ids[None, :]).astype(jnp.bfloat16)
    visible_in = jnp.dot(own_picks, embedded, preferred_element_type=jnp.float32).astype(
        jnp.bfloat16
    )
    if HEADS * total_rows * total_rows * 4 <= (1 << 24):
        clip_projected = project_rows(embedded, w_qkv)
        branch = attention_from(clip_projected, w_out)
        visible_projected = jnp.dot(
            own_picks, clip_projected, preferred_element_type=jnp.float32
        ).astype(jnp.bfloat16)
    else:
        branch = split_teacher(embedded, w_qkv, w_out, own_index, group_size)
        visible_projected = None
    all_targets = row_norm(branch).astype(jnp.bfloat16)

    def objective(rows_in):
        return copy_terms(
            rows_in,
            positions,
            all_targets,
            w_qkv,
            w_out,
            mask_embed,
            dec_in,
            conv_w,
            dec_out,
            visible_projected,
            factor,
        )

    factor = 0.5 / math.sqrt(copies * visible_count)
    squares, pullback = jax.vjp(objective, visible_in)
    (grad_in,) = pullback(jnp.ones_like(squares) * factor)
    copy_loss = jnp.reshape(squares / ((total_rows - visible_count) * D), (1,))
    flat_index = slot_index.reshape(copies * visible_count)
    own_cols = lax.dynamic_slice_in_dim(clip_pixels, own_index * col_width, col_width, 1)
    all_picks = (flat_index[:, None] == clip_ids[None, :]).astype(jnp.bfloat16)
    gathered = jnp.dot(all_picks, own_cols, preferred_element_type=jnp.float32).astype(
        jnp.bfloat16
    )
    embed_grad = jnp.einsum(
        "vc,vd->cd",
        gathered,
        jnp.concatenate(ring_gather(grad_in, group_size), axis=0),
        preferred_element_type=jnp.float32,
    )
    return (embed_grad, copy_loss)


def solution(mesh):
    placed = (P(("dp", "mask"), None), P("dp", None), P(), P(), P(), P(), P(), P(), P())
    return jax.shard_map(
        on_device,
        mesh=mesh,
        in_specs=placed,
        out_specs=(P(("dp", "mask"), None), P(("dp", "mask"))),
        check_vma=False,
    )
```

```python
import functools
import math

import jax
import jax.numpy as jnp
from jax import lax
from jax.experimental import pallas as pl
from jax.sharding import PartitionSpec as P

D = 1024
HEADS = 16
DD = 768
GROUPS = 16


EPSILON = 1e-06


def row_norm(values):
    average = jnp.mean(values, axis=-1, keepdims=True)
    centred = values - average
    spread = jnp.mean(centred * centred, axis=-1, keepdims=True)
    return centred * lax.rsqrt(spread + EPSILON)


def head_norm(values):
    return values * lax.rsqrt(jnp.mean(values * values, axis=-1, keepdims=True) + EPSILON)


def mix_heads(queries, key_rows, values):
    score_scale = 1.0 / math.sqrt(queries.shape[-1])
    scores = (
        jnp.einsum("qhd,khd->hqk", queries, key_rows, preferred_element_type=jnp.float32)
        * score_scale
    )
    exponent = jnp.exp(scores)
    weights = (exponent / jnp.sum(exponent, axis=-1, keepdims=True)).astype(jnp.bfloat16)
    mixed = jnp.einsum("hqk,khd->qhd", weights, values, preferred_element_type=jnp.float32)
    return mixed.astype(jnp.bfloat16)


def split_project(projected):
    queries = head_norm(projected[:, 0].astype(jnp.float32)).astype(jnp.bfloat16)
    key_rows = head_norm(projected[:, 1].astype(jnp.float32)).astype(jnp.bfloat16)
    return mix_heads(queries, key_rows, projected[:, 2])


def project_rows(inputs, w_qkv):
    normed = row_norm(inputs.astype(jnp.float32)).astype(jnp.bfloat16)
    return jnp.dot(normed, w_qkv, preferred_element_type=jnp.float32).astype(jnp.bfloat16)


def attention_from(projected, w_out):
    row_count = projected.shape[0]
    context = split_project(projected.reshape(row_count, 3, HEADS, D // HEADS))
    return jnp.dot(context.reshape(row_count, D), w_out, preferred_element_type=jnp.float32)


def attention_branch(inputs, w_qkv, w_out):
    return attention_from(project_rows(inputs, w_qkv), w_out)


@jax.custom_vjp
def reuse_rows(inputs, w_qkv, projected):
    return projected


def reuse_rows_fwd(inputs, w_qkv, projected):
    return projected, (inputs, w_qkv)


def reuse_rows_bwd(saved, cotangent):
    inputs, w_qkv = saved
    _, pullback = jax.vjp(
        lambda rows: row_norm(rows.astype(jnp.float32)).astype(jnp.bfloat16), inputs
    )
    d_normed = jnp.dot(cotangent, w_qkv.T, preferred_element_type=jnp.float32)
    d_normed = lax.optimization_barrier(d_normed.astype(jnp.bfloat16))
    (d_inputs,) = pullback(d_normed)
    return d_inputs, jnp.zeros_like(w_qkv), jnp.zeros_like(cotangent)


reuse_rows.defvjp(reuse_rows_fwd, reuse_rows_bwd)


def decoder_output(visible_out, positions, total_rows, mask_embed, dec_in, conv_w, dec_out):
    slot_ids = jnp.arange(total_rows, dtype=jnp.int32)
    picks = (slot_ids[:, None] == positions[None, :]).astype(jnp.bfloat16)
    seen = jnp.max(picks, axis=1, keepdims=True)
    lowered_visible = jnp.dot(visible_out, dec_in, preferred_element_type=jnp.float32).astype(
        jnp.bfloat16
    )
    lowered_mask = jnp.dot(
        mask_embed[None, :], dec_in, preferred_element_type=jnp.float32
    ).astype(jnp.bfloat16)
    placed = jnp.dot(picks, lowered_visible, preferred_element_type=jnp.float32)
    lowered = jnp.where(seen > 0, placed, lowered_mask.astype(jnp.float32)).astype(jnp.bfloat16)
    grouped = lowered.reshape(total_rows, GROUPS, DD // GROUPS)
    padded = jnp.pad(grouped, ((1, 1), (0, 0), (0, 0)))
    convolved = jnp.zeros((total_rows, GROUPS, DD // GROUPS), jnp.float32)
    for offset in range(3):
        convolved = convolved + jnp.einsum(
            "pgi,gio->pgo",
            padded[offset : offset + total_rows],
            conv_w[offset],
            preferred_element_type=jnp.float32,
        )
    activated = jax.nn.gelu(row_norm(convolved.reshape(total_rows, DD)), approximate=False)
    return (lowered.astype(jnp.float32) + activated).astype(jnp.bfloat16), seen


def loss_kernel(hidden_ref, dec_out_ref, targets_ref, keep_ref, squares_ref, d_hidden_ref, *, scale):
    predicted = jnp.dot(hidden_ref[...], dec_out_ref[...], preferred_element_type=jnp.float32)
    mismatch = (predicted - targets_ref[...].astype(jnp.float32)) * keep_ref[...]
    squares_ref[...] = jnp.sum(mismatch * mismatch, keepdims=True)
    d_predicted = (2.0 * scale * mismatch) * keep_ref[...]
    d_hidden = lax.dot_general(
        d_predicted.astype(jnp.bfloat16),
        dec_out_ref[...],
        (((1,), (1,)), ((), ())),
        preferred_element_type=jnp.float32,
    )
    d_hidden_ref[...] = d_hidden.astype(jnp.bfloat16)


def masked_squares(hidden, dec_out, targets, keep, scale):
    rows, width = hidden.shape
    return pl.pallas_call(
        functools.partial(loss_kernel, scale=scale),
        out_shape=(
            jax.ShapeDtypeStruct((1, 1), jnp.float32),
            jax.ShapeDtypeStruct((rows, width), jnp.bfloat16),
        ),
    )(hidden, dec_out, targets, keep)


@functools.partial(jax.custom_vjp, nondiff_argnums=(4,))
def squares_of(hidden, dec_out, targets, keep, scale):
    return masked_squares(hidden, dec_out, targets, keep, scale)[0][0, 0]


def squares_of_fwd(hidden, dec_out, targets, keep, scale):
    squares, d_hidden = masked_squares(hidden, dec_out, targets, keep, scale)
    return squares[0, 0], (d_hidden, dec_out, targets, keep)


def squares_of_bwd(scale, saved, cotangent):
    d_hidden, dec_out, targets, keep = saved
    ratio = (cotangent / scale).astype(jnp.bfloat16)
    return (
        d_hidden * ratio,
        jnp.zeros_like(dec_out),
        jnp.zeros_like(targets),
        jnp.zeros_like(keep),
    )


squares_of.defvjp(squares_of_fwd, squares_of_bwd)


def copy_terms(
    visible_in,
    positions,
    targets,
    w_qkv,
    w_out,
    mask_embed,
    dec_in,
    conv_w,
    dec_out,
    projected,
    scale,
):
    total_rows = targets.shape[0]
    if projected is None:
        branch = attention_branch(visible_in, w_qkv, w_out)
    else:
        branch = attention_from(reuse_rows(visible_in, w_qkv, projected), w_out)
    visible_out = (visible_in.astype(jnp.float32) + branch).astype(jnp.bfloat16)
    hidden, seen = decoder_output(
        visible_out, positions, total_rows, mask_embed, dec_in, conv_w, dec_out
    )
    slot_ids = jnp.arange(total_rows, dtype=jnp.int32)
    return squares_of(hidden, dec_out, targets, 1.0 - seen.astype(jnp.float32), scale)


def ring_gather(values, group_size):
    parts = [values]
    for shift in range(1, group_size):
        pairs = [(source, (source - shift) % group_size) for source in range(group_size)]
        parts.append(lax.ppermute(values, "mask", pairs))
    return parts


def in_mask_order(parts, own_index):
    group_size = len(parts)
    blocks = []
    for block in range(group_size):
        slot = (block - own_index) % group_size
        chosen = parts[0]
        for other in range(1, group_size):
            chosen = jnp.where(slot == other, parts[other], chosen)
        blocks.append(chosen)
    return jnp.concatenate(blocks, axis=0)


def split_teacher(embedded, w_qkv, w_out, own_index, group_size):
    total_rows = embedded.shape[0]
    head_dim = D // HEADS
    heads_here = HEADS // group_size
    head_width = heads_here * head_dim
    normed = row_norm(embedded.astype(jnp.float32)).astype(jnp.bfloat16)
    own_cols = lax.dynamic_slice_in_dim(
        w_qkv.reshape(D, 3, D), own_index * head_width, head_width, 2
    )
    projected = jnp.einsum(
        "sd,dtw->stw", normed, own_cols, preferred_element_type=jnp.float32
    ).astype(jnp.bfloat16)
    context = split_project(projected.reshape(total_rows, 3, heads_here, head_dim))
    out_rows = lax.dynamic_slice_in_dim(w_out, own_index * head_width, head_width, 0)
    partial_value = jnp.dot(
        context.reshape(total_rows, head_width), out_rows, preferred_element_type=jnp.float32
    )
    return lax.psum(partial_value.astype(jnp.bfloat16), "mask").astype(jnp.float32)


def on_device(patches, visible_index, embed_w, w_qkv, w_out, mask_embed, dec_in, conv_w, dec_out):
    tok_rows = patches.shape[0]
    group_size = lax.axis_size("mask")
    own_index = lax.axis_index("mask")
    copies = visible_index.shape[0]
    visible_count = visible_index.shape[1]
    total_rows = tok_rows * group_size
    col_width = patches.shape[1] // group_size
    doubled_index = jnp.concatenate([visible_index, visible_index], axis=0)
    slot_index = lax.dynamic_slice_in_dim(doubled_index, own_index, copies, 0)
    positions = slot_index[0]
    clip_pixels = in_mask_order(ring_gather(patches, group_size), own_index)
    embedded = jnp.dot(clip_pixels, embed_w, preferred_element_type=jnp.float32).astype(
        jnp.bfloat16
    )
    clip_ids = jnp.arange(total_rows, dtype=jnp.int32)
    own_picks = (positions[:, None] == clip_ids[None, :]).astype(jnp.bfloat16)
    visible_in = jnp.dot(own_picks, embedded, preferred_element_type=jnp.float32).astype(
        jnp.bfloat16
    )
    if HEADS * total_rows * total_rows * 4 <= (1 << 24):
        clip_projected = project_rows(embedded, w_qkv)
        branch = attention_from(clip_projected, w_out)
        visible_projected = jnp.dot(
            own_picks, clip_projected, preferred_element_type=jnp.float32
        ).astype(jnp.bfloat16)
    else:
        branch = split_teacher(embedded, w_qkv, w_out, own_index, group_size)
        visible_projected = None
    all_targets = row_norm(branch).astype(jnp.bfloat16)

    def objective(rows_in):
        return copy_terms(
            rows_in,
            positions,
            all_targets,
            w_qkv,
            w_out,
            mask_embed,
            dec_in,
            conv_w,
            dec_out,
            visible_projected,
            factor,
        )

    factor = 0.5 / math.sqrt(copies * visible_count)
    squares, pullback = jax.vjp(objective, visible_in)
    (grad_in,) = pullback(jnp.ones_like(squares) * factor)
    copy_loss = jnp.reshape(squares / ((total_rows - visible_count) * D), (1,))
    flat_index = slot_index.reshape(copies * visible_count)
    own_cols = lax.dynamic_slice_in_dim(clip_pixels, own_index * col_width, col_width, 1)
    all_picks = (flat_index[:, None] == clip_ids[None, :]).astype(jnp.bfloat16)
    gathered = jnp.dot(all_picks, own_cols, preferred_element_type=jnp.float32).astype(
        jnp.bfloat16
    )
    embed_grad = jnp.einsum(
        "vc,vd->cd",
        gathered,
        jnp.concatenate(ring_gather(grad_in, group_size), axis=0),
        preferred_element_type=jnp.float32,
    )
    return (embed_grad, copy_loss)


def solution(mesh):
    placed = (P(("dp", "mask"), None), P("dp", None), P(), P(), P(), P(), P(), P(), P())
    return jax.shard_map(
        on_device,
        mesh=mesh,
        in_specs=placed,
        out_specs=(P(("dp", "mask"), None), P(("dp", "mask"))),
        check_vma=False,
    )
```

```python
import functools
import math

import jax
import jax.numpy as jnp
from jax import lax
from jax.experimental import pallas as pl
from jax.sharding import PartitionSpec as P

D = 1024
HEADS = 16
DD = 768
GROUPS = 16


EPSILON = 1e-06


def row_norm(values):
    average = jnp.mean(values, axis=-1, keepdims=True)
    centred = values - average
    spread = jnp.mean(centred * centred, axis=-1, keepdims=True)
    return centred * lax.rsqrt(spread + EPSILON)


def head_norm(values):
    return values * lax.rsqrt(jnp.mean(values * values, axis=-1, keepdims=True) + EPSILON)


def mix_heads(queries, key_rows, values):
    score_scale = 1.0 / math.sqrt(queries.shape[-1])
    scores = (
        jnp.einsum("qhd,khd->hqk", queries, key_rows, preferred_element_type=jnp.float32)
        * score_scale
    )
    exponent = jnp.exp(scores)
    weights = (exponent / jnp.sum(exponent, axis=-1, keepdims=True)).astype(jnp.bfloat16)
    mixed = jnp.einsum("hqk,khd->qhd", weights, values, preferred_element_type=jnp.float32)
    return mixed.astype(jnp.bfloat16)


def split_project(projected):
    queries = head_norm(projected[:, 0].astype(jnp.float32)).astype(jnp.bfloat16)
    key_rows = head_norm(projected[:, 1].astype(jnp.float32)).astype(jnp.bfloat16)
    return mix_heads(queries, key_rows, projected[:, 2])


def project_rows(inputs, w_qkv):
    normed = row_norm(inputs.astype(jnp.float32)).astype(jnp.bfloat16)
    return jnp.dot(normed, w_qkv, preferred_element_type=jnp.float32).astype(jnp.bfloat16)


def attention_from(projected, w_out):
    row_count = projected.shape[0]
    context = split_project(projected.reshape(row_count, 3, HEADS, D // HEADS))
    return jnp.dot(context.reshape(row_count, D), w_out, preferred_element_type=jnp.float32)


def attention_branch(inputs, w_qkv, w_out):
    return attention_from(project_rows(inputs, w_qkv), w_out)


@jax.custom_vjp
def reuse_rows(inputs, w_qkv, projected):
    return projected


def reuse_rows_fwd(inputs, w_qkv, projected):
    return projected, (inputs, w_qkv)


def reuse_rows_bwd(saved, cotangent):
    inputs, w_qkv = saved
    _, pullback = jax.vjp(
        lambda rows: row_norm(rows.astype(jnp.float32)).astype(jnp.bfloat16), inputs
    )
    d_normed = jnp.dot(cotangent, w_qkv.T, preferred_element_type=jnp.float32)
    d_normed = lax.optimization_barrier(d_normed.astype(jnp.bfloat16))
    (d_inputs,) = pullback(d_normed)
    return d_inputs, jnp.zeros_like(w_qkv), jnp.zeros_like(cotangent)


reuse_rows.defvjp(reuse_rows_fwd, reuse_rows_bwd)


def decoder_output(visible_out, positions, total_rows, mask_embed, dec_in, conv_w, dec_out):
    slot_ids = jnp.arange(total_rows, dtype=jnp.int32)
    picks = (slot_ids[:, None] == positions[None, :]).astype(jnp.bfloat16)
    seen = jnp.max(picks, axis=1, keepdims=True)
    lowered_visible = jnp.dot(visible_out, dec_in, preferred_element_type=jnp.float32).astype(
        jnp.bfloat16
    )
    lowered_mask = jnp.dot(
        mask_embed[None, :], dec_in, preferred_element_type=jnp.float32
    ).astype(jnp.bfloat16)
    placed = jnp.dot(picks, lowered_visible, preferred_element_type=jnp.float32)
    lowered = jnp.where(seen > 0, placed, lowered_mask.astype(jnp.float32)).astype(jnp.bfloat16)
    grouped = lowered.reshape(total_rows, GROUPS, DD // GROUPS)
    padded = jnp.pad(grouped, ((1, 1), (0, 0), (0, 0)))
    convolved = jnp.zeros((total_rows, GROUPS, DD // GROUPS), jnp.float32)
    for offset in range(3):
        convolved = convolved + jnp.einsum(
            "pgi,gio->pgo",
            padded[offset : offset + total_rows],
            conv_w[offset],
            preferred_element_type=jnp.float32,
        )
    activated = jax.nn.gelu(row_norm(convolved.reshape(total_rows, DD)), approximate=False)
    return (lowered.astype(jnp.float32) + activated).astype(jnp.bfloat16), seen


def loss_kernel(hidden_ref, dec_out_ref, targets_ref, keep_ref, squares_ref, d_hidden_ref, *, scale):
    predicted = jnp.dot(hidden_ref[...], dec_out_ref[...], preferred_element_type=jnp.float32)
    mismatch = (predicted - targets_ref[...].astype(jnp.float32)) * keep_ref[...]
    squares_ref[...] = jnp.sum(mismatch * mismatch, keepdims=True)
    d_predicted = (2.0 * scale * mismatch) * keep_ref[...]
    d_hidden = lax.dot_general(
        d_predicted.astype(jnp.bfloat16),
        dec_out_ref[...],
        (((1,), (1,)), ((), ())),
        preferred_element_type=jnp.float32,
    )
    d_hidden_ref[...] = d_hidden.astype(jnp.bfloat16)


def masked_squares(hidden, dec_out, targets, keep, scale):
    rows, width = hidden.shape
    return pl.pallas_call(
        functools.partial(loss_kernel, scale=scale),
        out_shape=(
            jax.ShapeDtypeStruct((1, 1), jnp.float32),
            jax.ShapeDtypeStruct((rows, width), jnp.bfloat16),
        ),
    )(hidden, dec_out, targets, keep)


@functools.partial(jax.custom_vjp, nondiff_argnums=(4,))
def squares_of(hidden, dec_out, targets, keep, scale):
    return masked_squares(hidden, dec_out, targets, keep, scale)[0][0, 0]


def squares_of_fwd(hidden, dec_out, targets, keep, scale):
    squares, d_hidden = masked_squares(hidden, dec_out, targets, keep, scale)
    return squares[0, 0], (d_hidden, dec_out, targets, keep)


def squares_of_bwd(scale, saved, cotangent):
    d_hidden, dec_out, targets, keep = saved
    ratio = (cotangent / scale).astype(jnp.bfloat16)
    return (
        d_hidden * ratio,
        jnp.zeros_like(dec_out),
        jnp.zeros_like(targets),
        jnp.zeros_like(keep),
    )


squares_of.defvjp(squares_of_fwd, squares_of_bwd)


def copy_terms(
    visible_in,
    positions,
    targets,
    w_qkv,
    w_out,
    mask_embed,
    dec_in,
    conv_w,
    dec_out,
    projected,
    scale,
):
    total_rows = targets.shape[0]
    if projected is None:
        branch = attention_branch(visible_in, w_qkv, w_out)
    else:
        branch = attention_from(reuse_rows(visible_in, w_qkv, projected), w_out)
    visible_out = (visible_in.astype(jnp.float32) + branch).astype(jnp.bfloat16)
    hidden, seen = decoder_output(
        visible_out, positions, total_rows, mask_embed, dec_in, conv_w, dec_out
    )
    slot_ids = jnp.arange(total_rows, dtype=jnp.int32)
    return squares_of(hidden, dec_out, targets, 1.0 - seen.astype(jnp.float32), scale)


def ring_gather(values, group_size):
    parts = [values]
    for shift in range(1, group_size):
        pairs = [(source, (source - shift) % group_size) for source in range(group_size)]
        parts.append(lax.ppermute(values, "mask", pairs))
    return parts


def in_mask_order(parts, own_index):
    group_size = len(parts)
    blocks = []
    for block in range(group_size):
        slot = (block - own_index) % group_size
        chosen = parts[0]
        for other in range(1, group_size):
            chosen = jnp.where(slot == other, parts[other], chosen)
        blocks.append(chosen)
    return jnp.concatenate(blocks, axis=0)


def split_teacher(embedded, w_qkv, w_out, own_index, group_size):
    total_rows = embedded.shape[0]
    head_dim = D // HEADS
    heads_here = HEADS // group_size
    head_width = heads_here * head_dim
    normed = row_norm(embedded.astype(jnp.float32)).astype(jnp.bfloat16)
    own_cols = lax.dynamic_slice_in_dim(
        w_qkv.reshape(D, 3, D), own_index * head_width, head_width, 2
    )
    projected = jnp.einsum(
        "sd,dtw->stw", normed, own_cols, preferred_element_type=jnp.float32
    ).astype(jnp.bfloat16)
    context = split_project(projected.reshape(total_rows, 3, heads_here, head_dim))
    out_rows = lax.dynamic_slice_in_dim(w_out, own_index * head_width, head_width, 0)
    partial_value = jnp.dot(
        context.reshape(total_rows, head_width), out_rows, preferred_element_type=jnp.float32
    )
    return lax.psum(partial_value.astype(jnp.bfloat16), "mask").astype(jnp.float32)


def on_device(patches, visible_index, embed_w, w_qkv, w_out, mask_embed, dec_in, conv_w, dec_out):
    tok_rows = patches.shape[0]
    group_size = lax.axis_size("mask")
    own_index = lax.axis_index("mask")
    copies = visible_index.shape[0]
    visible_count = visible_index.shape[1]
    total_rows = tok_rows * group_size
    col_width = patches.shape[1] // group_size
    doubled_index = jnp.concatenate([visible_index, visible_index], axis=0)
    slot_index = lax.dynamic_slice_in_dim(doubled_index, own_index, copies, 0)
    positions = slot_index[0]
    clip_pixels = in_mask_order(ring_gather(patches, group_size), own_index)
    embedded = jnp.dot(clip_pixels, embed_w, preferred_element_type=jnp.float32).astype(
        jnp.bfloat16
    )
    clip_ids = jnp.arange(total_rows, dtype=jnp.int32)
    own_picks = (positions[:, None] == clip_ids[None, :]).astype(jnp.bfloat16)
    visible_in = jnp.dot(own_picks, embedded, preferred_element_type=jnp.float32).astype(
        jnp.bfloat16
    )
    if HEADS * total_rows * total_rows * 4 <= (1 << 24):
        clip_projected = project_rows(embedded, w_qkv)
        branch = attention_from(clip_projected, w_out)
        visible_projected = jnp.dot(
            own_picks, clip_projected, preferred_element_type=jnp.float32
        ).astype(jnp.bfloat16)
    else:
        branch = split_teacher(embedded, w_qkv, w_out, own_index, group_size)
        visible_projected = None
    all_targets = row_norm(branch).astype(jnp.bfloat16)

    def objective(rows_in):
        return copy_terms(
            rows_in,
            positions,
            all_targets,
            w_qkv,
            w_out,
            mask_embed,
            dec_in,
            conv_w,
            dec_out,
            visible_projected,
            factor,
        )

    factor = 0.5 / math.sqrt(copies * visible_count)
    squares, pullback = jax.vjp(objective, visible_in)
    (grad_in,) = pullback(jnp.ones_like(squares) * factor)
    copy_loss = jnp.reshape(squares / ((total_rows - visible_count) * D), (1,))
    flat_index = slot_index.reshape(copies * visible_count)
    own_cols = lax.dynamic_slice_in_dim(clip_pixels, own_index * col_width, col_width, 1)
    all_picks = (flat_index[:, None] == clip_ids[None, :]).astype(jnp.bfloat16)
    gathered_t = jnp.einsum(
        "sc,vs->cv", own_cols, all_picks, preferred_element_type=jnp.float32
    ).astype(jnp.bfloat16)
    embed_grad = jnp.dot(
        gathered_t,
        jnp.concatenate(ring_gather(grad_in, group_size), axis=0),
        preferred_element_type=jnp.float32,
    )
    return (embed_grad, copy_loss)


def solution(mesh):
    placed = (P(("dp", "mask"), None), P("dp", None), P(), P(), P(), P(), P(), P(), P())
    return jax.shard_map(
        on_device,
        mesh=mesh,
        in_specs=placed,
        out_specs=(P(("dp", "mask"), None), P(("dp", "mask"))),
        check_vma=False,
    )
```
